32 devices in a mesh: groups: 2 (over y), row: 8 (over z, x), col: 2 (over core).
Axes of the slice: x: 2, y: 2, z: 4, core: 2. Of those that a mesh axis runs over, the one named last changes fastest.
Arguments:
- tokens: bfloat16 [4, 1024, 3584], P('groups', 'row', 'col'), parts along dimension 0, may hold values from -40 to 40
- gain: float32 [3584], replicated, may hold values from 0.5 to 2
- w_query: bfloat16 [3584, 1792], P('row', 'col'), may hold values from -0.125 to 0.125
- b_query: float32 [1792], P('col'), may hold values from -24 to 24
- key_weight: bfloat16 [3584, 256], P('row', 'col'), may hold values from -0.125 to 0.125
- b_key: float32 [256], P('col'), may hold values from -24 to 24
- value_weight: bfloat16 [3584, 256], P('row', 'col'), may hold values from -0.09375 to 0.09375
- value_bias: float32 [256], P('col'), may hold values from -3 to 3
- random_block_index: int32 [4, 16, 14, 2], P('groups'), parts along dimension 0, may hold values from 0 to 15, as said below
- global_block_index: int32 [4, 2, 2], P('groups'), parts along dimension 0, may hold values from 0 to 15
Outputs:
- context: bfloat16 [4, 1024, 1792], P('groups', 'row', 'col'), parts along dimension 0
The draws below stay inside these ranges and needn't reach their ends.
There are 2 independent parts, one for each index of `groups`. The reference program is written for one: setup_inputs(seed, part) draws one part's arguments, and reference() takes and returns one part's arrays. A program takes and returns all parts, laid end to end along the dimension named above; an argument that names none is the same for every part. Nothing has to cross between parts.
Inputs may be any that keep to these rules, and one draw needn't show every extreme that they name: `random_block_index`: A request group is the 56 entries of both passages whose query block lies in one aligned run of 2 blocks and whose head lies in one aligned run of 7 heads. In every request group at most 7 entries name blocks of any one aligned run of 2 blocks, and some run is named exactly 7 times.
All inputs are finite; a program needn't handle non-finite values.
Results may differ from the reference program's by a relative error of at most 0.003.
The reference program's roundings to bfloat16 on the way count: a program that leaves them out, or rounds other values in their place, can miss the bound.
Values may be sent and summed in bfloat16 or wider, within the bound.
No kernel may reach another device: no remote copies, remote signals or barrier semaphores. Data moves between devices by JAX's collectives and lax.ppermute only.
A program may use at most 128 MiB of HBM per device.

```python
import math
import jax
import jax.numpy as jnp
from jax import lax

MODEL_WIDTH = 3584
HEAD_SIZE = 128
QUERY_HEADS = 14
KEY_HEADS = 2
BLOCK_TOKENS = 64
RANDOM_BLOCKS = 2
GLOBAL_BLOCKS = 2
GROUP_PASSAGES = 2
PASSAGE_TOKENS = 1024
PASSAGE_BLOCKS = 16
QBD = 2
OWNERS = 8
HCOL = 7
NREQ = 56
CAP = 7


def draw_tokens(key, part):
    keys = jax.random.split(key, 3)
    row_scale = jnp.exp(jax.random.uniform(keys[1], (GROUP_PASSAGES, PASSAGE_TOKENS, 1), jnp.float32, 0.0, 2.302585))
    column_scale = jnp.exp(jax.random.uniform(keys[2], (1, 1, MODEL_WIDTH), jnp.float32, 0.0, 2.302585))
    base = jnp.clip(jax.random.normal(keys[0], (GROUP_PASSAGES, PASSAGE_TOKENS, MODEL_WIDTH), jnp.float32), -4.0, 4.0)
    return (base * row_scale * column_scale * 0.1).astype(jnp.bfloat16)


def draw_bias(key, query_head_count):
    keys = jax.random.split(key, 2)
    values = jnp.clip(jax.random.normal(keys[1], (query_head_count, HEAD_SIZE), jnp.float32), -4.0, 4.0)
    return values.reshape(query_head_count * HEAD_SIZE)


def draw_b_query(key, part):
    return draw_bias(key, QUERY_HEADS)


def draw_b_key(key, part):
    return draw_bias(key, KEY_HEADS)


def draw_random_block_index(key, part):
    column_count = QUERY_HEADS // HCOL
    count = OWNERS * column_count
    keys = jax.random.split(key, 2)
    slot_keys = jax.random.split(keys[0], count)
    chosen = jax.vmap(lambda one: jax.random.permutation(one, OWNERS * CAP)[:NREQ])(slot_keys)
    local = jax.random.randint(keys[1], (count, NREQ), 0, QBD, dtype=jnp.int32)
    blocks = chosen.astype(jnp.int32) // CAP * QBD + local
    blocks = blocks.reshape(OWNERS, column_count, GROUP_PASSAGES, QBD, HCOL, RANDOM_BLOCKS)
    blocks = blocks.transpose(2, 0, 3, 1, 4, 5)
    return blocks.reshape(GROUP_PASSAGES, PASSAGE_BLOCKS, QUERY_HEADS, RANDOM_BLOCKS)


def set_ends(values, own_key, smallest, high):
    spot = [jax.random.randint(jax.random.fold_in(own_key, axis), (), 0, length) for axis, length in enumerate(values.shape)]
    longest = values.shape.index(max(values.shape))
    next_to = spot[:longest] + [(spot[longest] + 1) % values.shape[longest]] + spot[longest + 1:]
    return values.at[tuple(spot)].set(smallest).at[tuple(next_to)].set(high)


def levels(key, dims, pieces, least, high):
    level = 1.0
    for dim, shards_of in pieces:
        draws = jax.random.uniform(jax.random.fold_in(jax.random.fold_in(key, 6), dim), (shards_of,), jnp.float32, least / len(pieces), high / len(pieces))
        level = level * jnp.repeat(jnp.exp(draws), dims[dim] // shards_of).reshape((-1,) + (1,) * (len(dims) - 1 - dim))
    return level


def scatter_about(own_key, dims, scale, limit, cuts=(), held_as=jnp.bfloat16):
    level = levels(own_key, dims, cuts, -0.22, 0.18) if cuts else 1.0
    values = jax.random.normal(own_key, dims, jnp.float32) * scale * level
    return jnp.minimum(jnp.maximum(values, -limit), limit).astype(held_as)


def setup_inputs(seed: int = 0, part: int = 0) -> dict:
    splits = jax.random.split(jax.random.key(seed), 11)
    part_keys = jax.random.split(jax.random.fold_in(splits[10], part), 11)
    return {
        "tokens": draw_tokens(jax.random.fold_in(jax.random.fold_in(splits[10], part), 71), part),
        "gain": jnp.clip(jnp.exp(jax.random.uniform(splits[1], (MODEL_WIDTH,), jnp.float32, math.log(0.5), math.log(2.0))), 0.5, 2.0),
        "w_query": scatter_about(splits[2], (MODEL_WIDTH, QUERY_HEADS * HEAD_SIZE), (MODEL_WIDTH // 2) ** -0.5, 0.125, ((0, 8), (1, 2))),
        "b_query": draw_b_query(jax.random.fold_in(splits[10], 71), part),
        "key_weight": scatter_about(splits[4], (MODEL_WIDTH, KEY_HEADS * HEAD_SIZE), (MODEL_WIDTH // 2) ** -0.5, 0.125, ((0, 8), (1, 2))),
        "b_key": draw_b_key(jax.random.fold_in(splits[10], 71), part),
        "value_weight": scatter_about(splits[6], (MODEL_WIDTH, KEY_HEADS * HEAD_SIZE), MODEL_WIDTH ** -0.5, 0.09375, ((0, 8), (1, 2))),
        "value_bias": scatter_about(splits[7], (KEY_HEADS * HEAD_SIZE,), 0.5, 3.0, ((0, 2),), jnp.float32),
        "random_block_index": draw_random_block_index(jax.random.fold_in(jax.random.fold_in(splits[10], part), 71), part),
        "global_block_index": set_ends(jax.random.randint(part_keys[9], (GROUP_PASSAGES, KEY_HEADS, GLOBAL_BLOCKS), 0, PASSAGE_BLOCKS), jax.random.fold_in(part_keys[9], 1), 0, PASSAGE_BLOCKS - 1).astype(jnp.int32),
    }


rope_base = 1000000.0
norm_eps = 1e-06

def apply_rotation(values, token_positions):
    half = values.shape[-1] // 2
    freqs = 1.0 / rope_base ** (jnp.arange(half, dtype=jnp.float32) * 2.0 / values.shape[-1])
    angles = token_positions[:, None] * freqs[None, :]
    cosine = jnp.concatenate([jnp.cos(angles), jnp.cos(angles)], axis=-1)[None, :, None, :]
    sine = jnp.concatenate([jnp.sin(angles), jnp.sin(angles)], axis=-1)[None, :, None, :]
    turned = jnp.concatenate([-values[..., half:], values[..., :half]], axis=-1)
    return values * cosine + turned * sine

def reference(tokens, gain, w_query, b_query, key_weight, b_key, value_weight, value_bias, random_block_index, global_block_index):
    passage_groups = QUERY_HEADS // KEY_HEADS
    scale = 1.0 / math.sqrt(HEAD_SIZE)
    token_positions = jnp.arange(PASSAGE_TOKENS, dtype=jnp.int32).astype(jnp.float32)
    query_head_count = jnp.arange(KEY_HEADS, dtype=jnp.int32)
    offsets = jnp.arange(3, dtype=jnp.int32) - 1
    outputs = []
    for passage_index in range(GROUP_PASSAGES):
        values = tokens[passage_index].astype(jnp.float32)
        power = lax.optimization_barrier(jnp.mean(values * values, axis=-1, keepdims=True))
        normed = (values * lax.rsqrt(power + norm_eps) * gain).astype(jnp.bfloat16)
        query_sum = jnp.dot(normed, w_query, preferred_element_type=jnp.float32) + b_query
        summed_keys = jnp.dot(normed, key_weight, preferred_element_type=jnp.float32) + b_key
        value_sum = jnp.dot(normed, value_weight, preferred_element_type=jnp.float32) + value_bias
        query_rows = apply_rotation(query_sum.reshape(1, PASSAGE_TOKENS, QUERY_HEADS, HEAD_SIZE), token_positions)[0].astype(jnp.bfloat16)
        key = apply_rotation(summed_keys.reshape(1, PASSAGE_TOKENS, KEY_HEADS, HEAD_SIZE), token_positions)[0].astype(jnp.bfloat16)
        value_rows = value_sum.astype(jnp.bfloat16)
        query_rows = lax.optimization_barrier(query_rows).astype(jnp.float32)
        key = lax.optimization_barrier(key).astype(jnp.float32)
        value_rows = lax.optimization_barrier(value_rows).astype(jnp.float32)
        query_block_rows = query_rows.reshape(PASSAGE_BLOCKS, BLOCK_TOKENS, KEY_HEADS, passage_groups, HEAD_SIZE)
        key_head_rows = key.reshape(PASSAGE_BLOCKS, BLOCK_TOKENS, KEY_HEADS, HEAD_SIZE).transpose(2, 0, 1, 3)
        value_head_rows = value_rows.reshape(PASSAGE_BLOCKS, BLOCK_TOKENS, KEY_HEADS, HEAD_SIZE).transpose(2, 0, 1, 3)
        global_key_rows = key_head_rows[query_head_count[:, None], global_block_index[passage_index]].reshape(KEY_HEADS, GLOBAL_BLOCKS * BLOCK_TOKENS, HEAD_SIZE)
        global_value_rows = value_head_rows[query_head_count[:, None], global_block_index[passage_index]].reshape(KEY_HEADS, GLOBAL_BLOCKS * BLOCK_TOKENS, HEAD_SIZE)
        rotation_table = random_block_index[passage_index].reshape(PASSAGE_BLOCKS, KEY_HEADS, passage_groups, RANDOM_BLOCKS)

        def one_block(index):
            nearby_blocks = index + offsets
            valid = (nearby_blocks >= 0) & (nearby_blocks < PASSAGE_BLOCKS)
            nearby_blocks = jnp.clip(nearby_blocks, 0, PASSAGE_BLOCKS - 1)
            sliding_key_rows = key_head_rows[:, nearby_blocks].reshape(KEY_HEADS, 3 * BLOCK_TOKENS, HEAD_SIZE)
            sliding_value_rows = value_head_rows[:, nearby_blocks].reshape(KEY_HEADS, 3 * BLOCK_TOKENS, HEAD_SIZE)
            picked_blocks = rotation_table[index]
            random_key_rows = key_head_rows[query_head_count[:, None, None], picked_blocks].reshape(KEY_HEADS, passage_groups, RANDOM_BLOCKS * BLOCK_TOKENS, HEAD_SIZE)
            random_value_rows = value_head_rows[query_head_count[:, None, None], picked_blocks].reshape(KEY_HEADS, passage_groups, RANDOM_BLOCKS * BLOCK_TOKENS, HEAD_SIZE)
            block_query = query_block_rows[index]
            first = jnp.einsum('bkgh,kwh->kgbw', block_query, sliding_key_rows)
            second = jnp.einsum('bkgh,kwh->kgbw', block_query, global_key_rows)
            third = jnp.einsum('bkgh,kgwh->kgbw', block_query, random_key_rows)
            scores = jnp.concatenate([first, second, third], axis=-1) * scale
            mask = jnp.concatenate([jnp.repeat(valid, BLOCK_TOKENS), jnp.ones(((GLOBAL_BLOCKS + RANDOM_BLOCKS) * BLOCK_TOKENS,), dtype=jnp.bool_)])
            scores = jnp.where(mask, scores, -jnp.inf)
            top = lax.optimization_barrier(jnp.max(scores, axis=-1, keepdims=True))
            weights = jnp.exp(scores - top)
            probs = weights / lax.optimization_barrier(jnp.sum(weights, axis=-1, keepdims=True))
            probs = lax.optimization_barrier(probs.astype(jnp.bfloat16)).astype(jnp.float32)
            near_probs = probs[..., :3 * BLOCK_TOKENS]
            global_probs = probs[..., 3 * BLOCK_TOKENS:(3 + GLOBAL_BLOCKS) * BLOCK_TOKENS]
            random_probs = probs[..., (3 + GLOBAL_BLOCKS) * BLOCK_TOKENS:]
            mixed = jnp.einsum('kgbw,kwh->bkgh', near_probs, sliding_value_rows)
            mixed = mixed + jnp.einsum('kgbw,kwh->bkgh', global_probs, global_value_rows)
            mixed = mixed + jnp.einsum('kgbw,kgwh->bkgh', random_probs, random_value_rows)
            return mixed.reshape(BLOCK_TOKENS, QUERY_HEADS * HEAD_SIZE).astype(jnp.bfloat16)
        result = lax.map(one_block, jnp.arange(PASSAGE_BLOCKS, dtype=jnp.int32))
        outputs.append(result.reshape(PASSAGE_TOKENS, QUERY_HEADS * HEAD_SIZE))
    return jnp.stack(outputs, axis=0)
```

```python
import math

import jax
import jax.numpy as jnp
from jax import lax
from jax.sharding import PartitionSpec as P

HEAD_SIZE = 128
BLOCK_TOKENS = 64
RANDOM_BLOCKS = 2
GLOBAL_BLOCKS = 2


rope_base = 1000000.0
norm_eps = 1e-06

SWAP = [(0, 1), (1, 0)]


def apply_rotation(values, token_positions):
    half = values.shape[-1] // 2
    freqs = 1.0 / rope_base ** (jnp.arange(half, dtype=jnp.float32) * 2.0 / values.shape[-1])
    angles = token_positions[:, None] * freqs[None, :]
    cosine = jnp.concatenate([jnp.cos(angles), jnp.cos(angles)], axis=-1)[None, :, None, :]
    sine = jnp.concatenate([jnp.sin(angles), jnp.sin(angles)], axis=-1)[None, :, None, :]
    turned = jnp.concatenate([-values[..., half:], values[..., :half]], axis=-1)
    return values * cosine + turned * sine


def shards(
    tokens,
    gain,
    w_query,
    b_query,
    key_weight,
    b_key,
    value_weight,
    value_bias,
    random_block_index,
    global_block_index,
):
    row_count = lax.axis_size("row")
    here = lax.axis_index("row")
    column = lax.axis_index("col")
    group = lax.axis_index("groups")
    passages, length, _ = tokens.shape
    heads_here = w_query.shape[1] // HEAD_SIZE
    pairs_here = key_weight.shape[1] // HEAD_SIZE
    passage_groups = heads_here // pairs_here
    per_device = length // BLOCK_TOKENS
    passage_blocks = row_count * per_device
    scale = 1.0 / math.sqrt(HEAD_SIZE)

    rotary_cols = (heads_here + pairs_here) * HEAD_SIZE
    split = rotary_cols // 2
    value_cols = pairs_here * HEAD_SIZE
    value_split = value_cols // 2
    rotary_w = jnp.concatenate([w_query, key_weight], axis=1)
    rotary_b = jnp.concatenate([b_query, b_key], axis=0)
    first = group == 0
    panel = jnp.where(
        first,
        jnp.concatenate([rotary_w[:, :split], value_weight[:, :value_split]], axis=1),
        jnp.concatenate([rotary_w[:, split:], value_weight[:, value_split:]], axis=1),
    )
    panel_bias = jnp.where(
        first,
        jnp.concatenate([rotary_b[:split], value_bias[:value_split]]),
        jnp.concatenate([rotary_b[split:], value_bias[value_split:]]),
    )
    full_panel = lax.all_gather(panel, "row", axis=0, tiled=True)

    other_half = lax.ppermute(tokens, "col", SWAP)
    whole = jnp.where(
        column == 0,
        jnp.concatenate([tokens, other_half], axis=2),
        jnp.concatenate([other_half, tokens], axis=2),
    )
    partner = lax.ppermute(whole, "groups", SWAP)
    both = jnp.concatenate([whole, partner], axis=0)
    widened = both.astype(jnp.float32)
    power = jnp.mean(widened * widened, axis=-1, keepdims=True)
    normed = (
        (widened * lax.rsqrt(power + norm_eps) * gain)
        .astype(jnp.bfloat16)
        .reshape(2 * passages * length, -1)
    )
    token_positions = (here * length + jnp.arange(length, dtype=jnp.int32)).astype(jnp.float32)

    summed = jnp.dot(normed, full_panel, preferred_element_type=jnp.float32) + panel_bias
    summed = summed.reshape(2 * passages, length, split + value_split)
    turned = apply_rotation(
        summed[..., :split].reshape(2 * passages, length, split // HEAD_SIZE, HEAD_SIZE),
        token_positions,
    ).astype(jnp.bfloat16)
    result = jnp.concatenate(
        [turned.reshape(2 * passages, length, split), summed[..., split:].astype(jnp.bfloat16)],
        axis=-1,
    )
    mine = result[:passages]
    returned = lax.ppermute(result[passages:], "groups", SWAP)
    low = jnp.where(first, mine, returned)
    high = jnp.where(first, returned, mine)
    rotary_rows = jnp.concatenate([low[..., :split], high[..., :split]], axis=-1)
    query_rows = rotary_rows[..., : heads_here * HEAD_SIZE]
    key = rotary_rows[..., heads_here * HEAD_SIZE :]
    value_rows = jnp.concatenate([low[..., split:], high[..., split:]], axis=-1)

    pairs = jnp.concatenate([key, value_rows], axis=-1)
    gathered = lax.all_gather(pairs, "row", axis=0, tiled=False)
    gathered = gathered.transpose(1, 0, 2, 3).reshape(
        passages, passage_blocks, BLOCK_TOKENS, pairs_here, 2 * HEAD_SIZE
    )
    kv_blocks = gathered[:, :, :, 0]

    local_blocks = here * per_device + jnp.arange(per_device, dtype=jnp.int32)
    nearby_blocks = local_blocks[:, None] + jnp.arange(3, dtype=jnp.int32)[None, :] - 1
    inside = (nearby_blocks >= 0) & (nearby_blocks < passage_blocks)
    nearby_clamped = jnp.clip(nearby_blocks, 0, passage_blocks - 1)
    passage_ids = jnp.arange(passages, dtype=jnp.int32)
    window = kv_blocks[passage_ids[:, None, None], nearby_clamped[None]]
    window = window.reshape(passages, per_device, 3 * BLOCK_TOKENS, 2 * HEAD_SIZE)

    global_here = lax.dynamic_slice_in_dim(global_block_index, column * pairs_here, pairs_here, 1)
    global_pairs = kv_blocks[passage_ids[:, None], global_here[:, 0, :]]
    global_pairs = global_pairs.reshape(passages, GLOBAL_BLOCKS * BLOCK_TOKENS, 2 * HEAD_SIZE)

    selected = lax.dynamic_slice_in_dim(random_block_index, column * heads_here, heads_here, 2)
    selected = lax.dynamic_slice_in_dim(selected, here * per_device, per_device, 1)
    arrived = kv_blocks[passage_ids[:, None, None, None], selected]
    arrived = arrived.reshape(
        passages, per_device, heads_here, RANDOM_BLOCKS * BLOCK_TOKENS, 2 * HEAD_SIZE
    )

    query_block_rows = query_rows.reshape(
        passages, per_device, BLOCK_TOKENS, heads_here, HEAD_SIZE
    )
    first_scores = jnp.einsum(
        "sqbgh,sqwh->sqgbw",
        query_block_rows,
        window[..., :HEAD_SIZE],
        preferred_element_type=jnp.float32,
    )
    second_scores = jnp.einsum(
        "sqbgh,swh->sqgbw",
        query_block_rows,
        global_pairs[..., :HEAD_SIZE],
        preferred_element_type=jnp.float32,
    )
    third_scores = jnp.einsum(
        "sqbgh,sqgwh->sqgbw",
        query_block_rows,
        arrived[..., :HEAD_SIZE],
        preferred_element_type=jnp.float32,
    )
    scores = jnp.concatenate([first_scores, second_scores, third_scores], axis=-1) * scale
    mask = jnp.concatenate(
        [
            jnp.repeat(inside, BLOCK_TOKENS, axis=1),
            jnp.ones((per_device, (GLOBAL_BLOCKS + RANDOM_BLOCKS) * BLOCK_TOKENS), dtype=jnp.bool_),
        ],
        axis=1,
    )
    scores = jnp.where(mask[None, :, None, None, :], scores, -jnp.inf)
    top = jnp.max(scores, axis=-1, keepdims=True)
    weights = jnp.exp(scores - top)
    probs = (weights / jnp.sum(weights, axis=-1, keepdims=True)).astype(jnp.bfloat16)
    near_probs = probs[..., : 3 * BLOCK_TOKENS]
    global_probs = probs[..., 3 * BLOCK_TOKENS : (3 + GLOBAL_BLOCKS) * BLOCK_TOKENS]
    random_probs = probs[..., (3 + GLOBAL_BLOCKS) * BLOCK_TOKENS :]
    mixed = jnp.einsum(
        "sqgbw,sqwh->sqbgh",
        near_probs,
        window[..., HEAD_SIZE:],
        preferred_element_type=jnp.float32,
    )
    mixed = mixed + jnp.einsum(
        "sqgbw,swh->sqbgh",
        global_probs,
        global_pairs[..., HEAD_SIZE:],
        preferred_element_type=jnp.float32,
    )
    mixed = mixed + jnp.einsum(
        "sqgbw,sqgwh->sqbgh",
        random_probs,
        arrived[..., HEAD_SIZE:],
        preferred_element_type=jnp.float32,
    )
    return mixed.reshape(passages, length, heads_here * HEAD_SIZE).astype(jnp.bfloat16)


def solution(mesh):
    placed = (
        P("groups", "row", "col"),
        P(),
        P("row", "col"),
        P("col"),
        P("row", "col"),
        P("col"),
        P("row", "col"),
        P("col"),
        P("groups", None, None, None),
        P("groups", None, None),
    )
    return jax.shard_map(
        shards, mesh=mesh, in_specs=placed, out_specs=P("groups", "row", "col"), check_vma=False
    )
```

```python
import math

import jax
import jax.numpy as jnp
from jax import lax
from jax.sharding import PartitionSpec as P

HEAD_SIZE = 128
BLOCK_TOKENS = 64
RANDOM_BLOCKS = 2
GLOBAL_BLOCKS = 2


rope_base = 1000000.0
norm_eps = 1e-06

SWAP = [(0, 1), (1, 0)]


def apply_rotation(values, token_positions):
    half = values.shape[-1] // 2
    freqs = 1.0 / rope_base ** (jnp.arange(half, dtype=jnp.float32) * 2.0 / values.shape[-1])
    angles = token_positions[:, None] * freqs[None, :]
    cosine = jnp.concatenate([jnp.cos(angles), jnp.cos(angles)], axis=-1)[None, :, None, :]
    sine = jnp.concatenate([jnp.sin(angles), jnp.sin(angles)], axis=-1)[None, :, None, :]
    turned = jnp.concatenate([-values[..., half:], values[..., :half]], axis=-1)
    return values * cosine + turned * sine


def shards(
    tokens,
    gain,
    w_query,
    b_query,
    key_weight,
    b_key,
    value_weight,
    value_bias,
    random_block_index,
    global_block_index,
):
    row_count = lax.axis_size("row")
    here = lax.axis_index("row")
    column = lax.axis_index("col")
    group = lax.axis_index("groups")
    passages, length, _ = tokens.shape
    heads_here = w_query.shape[1] // HEAD_SIZE
    pairs_here = key_weight.shape[1] // HEAD_SIZE
    passage_groups = heads_here // pairs_here
    per_device = length // BLOCK_TOKENS
    passage_blocks = row_count * per_device
    scale = 1.0 / math.sqrt(HEAD_SIZE)

    rotary_cols = (heads_here + pairs_here) * HEAD_SIZE
    split = rotary_cols // 2
    value_cols = pairs_here * HEAD_SIZE
    value_split = value_cols // 2
    rotary_w = jnp.concatenate([w_query, key_weight], axis=1)
    rotary_b = jnp.concatenate([b_query, b_key], axis=0)
    first = group == 0
    panel = jnp.where(
        first,
        jnp.concatenate([rotary_w[:, :split], value_weight[:, :value_split]], axis=1),
        jnp.concatenate([rotary_w[:, split:], value_weight[:, value_split:]], axis=1),
    )
    panel_bias = jnp.where(
        first,
        jnp.concatenate([rotary_b[:split], value_bias[:value_split]]),
        jnp.concatenate([rotary_b[split:], value_bias[value_split:]]),
    )
    full_panel = lax.all_gather(panel, "row", axis=0, tiled=True)

    other_half = lax.ppermute(tokens, "col", SWAP)
    partner_half = lax.ppermute(tokens, "groups", SWAP)
    partner_other = lax.ppermute(partner_half, "col", SWAP)
    whole = jnp.where(
        column == 0,
        jnp.concatenate([tokens, other_half], axis=2),
        jnp.concatenate([other_half, tokens], axis=2),
    )
    partner = jnp.where(
        column == 0,
        jnp.concatenate([partner_half, partner_other], axis=2),
        jnp.concatenate([partner_other, partner_half], axis=2),
    )
    both = jnp.concatenate([whole, partner], axis=0)
    widened = both.astype(jnp.float32)
    power = jnp.mean(widened * widened, axis=-1, keepdims=True)
    normed = (
        (widened * lax.rsqrt(power + norm_eps) * gain)
        .astype(jnp.bfloat16)
        .reshape(2 * passages * length, -1)
    )
    token_positions = (here * length + jnp.arange(length, dtype=jnp.int32)).astype(jnp.float32)

    summed = jnp.dot(normed, full_panel, preferred_element_type=jnp.float32) + panel_bias
    summed = summed.reshape(2 * passages, length, split + value_split)
    turned = apply_rotation(
        summed[..., :split].reshape(2 * passages, length, split // HEAD_SIZE, HEAD_SIZE),
        token_positions,
    ).astype(jnp.bfloat16)
    result = jnp.concatenate(
        [turned.reshape(2 * passages, length, split), summed[..., split:].astype(jnp.bfloat16)],
        axis=-1,
    )
    mine = result[:passages]
    returned = lax.ppermute(result[passages:], "groups", SWAP)
    low = jnp.where(first, mine, returned)
    high = jnp.where(first, returned, mine)
    rotary_rows = jnp.concatenate([low[..., :split], high[..., :split]], axis=-1)
    query_rows = rotary_rows[..., : heads_here * HEAD_SIZE]
    key = rotary_rows[..., heads_here * HEAD_SIZE :]
    value_rows = jnp.concatenate([low[..., split:], high[..., split:]], axis=-1)

    pairs = jnp.concatenate([key, value_rows], axis=-1)
    if row_count <= 8:
        by_shift = [pairs] + [
            lax.ppermute(pairs, "row", [(i, (i + k) % row_count) for i in range(row_count)])
            for k in range(1, row_count)
        ]
        gathered = jnp.stack(by_shift)
        owner_slot = (here - jnp.arange(row_count, dtype=jnp.int32)) % row_count
    else:
        gathered = lax.all_gather(pairs, "row", axis=0, tiled=False)
        owner_slot = jnp.arange(row_count, dtype=jnp.int32)
    gathered = gathered.reshape(
        row_count, passages, per_device, BLOCK_TOKENS, pairs_here, 2 * HEAD_SIZE
    )[:, :, :, :, 0]
    gathered = gathered.transpose(1, 0, 2, 3, 4).reshape(
        passages, passage_blocks, BLOCK_TOKENS, 2 * HEAD_SIZE
    )
    block_ids = jnp.arange(passage_blocks, dtype=jnp.int32)
    slot_of_block = owner_slot[block_ids // per_device] * per_device + block_ids % per_device
    kv_blocks = gathered[:, slot_of_block]

    local_blocks = here * per_device + jnp.arange(per_device, dtype=jnp.int32)
    nearby_blocks = local_blocks[:, None] + jnp.arange(3, dtype=jnp.int32)[None, :] - 1
    inside = (nearby_blocks >= 0) & (nearby_blocks < passage_blocks)
    nearby_clamped = jnp.clip(nearby_blocks, 0, passage_blocks - 1)
    passage_ids = jnp.arange(passages, dtype=jnp.int32)
    window = kv_blocks[passage_ids[:, None, None], nearby_clamped[None]]
    window = window.reshape(passages, per_device, 3 * BLOCK_TOKENS, 2 * HEAD_SIZE)

    global_here = lax.dynamic_slice_in_dim(global_block_index, column * pairs_here, pairs_here, 1)
    global_pairs = kv_blocks[passage_ids[:, None], global_here[:, 0, :]]
    global_pairs = global_pairs.reshape(passages, GLOBAL_BLOCKS * BLOCK_TOKENS, 2 * HEAD_SIZE)

    selected = lax.dynamic_slice_in_dim(random_block_index, column * heads_here, heads_here, 2)
    selected = lax.dynamic_slice_in_dim(selected, here * per_device, per_device, 1)
    arrived = kv_blocks[passage_ids[:, None, None, None], selected]
    arrived = arrived.reshape(
        passages, per_device, heads_here, RANDOM_BLOCKS * BLOCK_TOKENS, 2 * HEAD_SIZE
    )

    query_block_rows = query_rows.reshape(
        passages, per_device, BLOCK_TOKENS, heads_here, HEAD_SIZE
    )
    first_scores = jnp.einsum(
        "sqbgh,sqwh->sqgbw",
        query_block_rows,
        window[..., :HEAD_SIZE],
        preferred_element_type=jnp.float32,
    )
    second_scores = jnp.einsum(
        "sqbgh,swh->sqgbw",
        query_block_rows,
        global_pairs[..., :HEAD_SIZE],
        preferred_element_type=jnp.float32,
    )
    third_scores = jnp.einsum(
        "sqbgh,sqgwh->sqgbw",
        query_block_rows,
        arrived[..., :HEAD_SIZE],
        preferred_element_type=jnp.float32,
    )
    first_scores = first_scores * scale
    second_scores = second_scores * scale
    third_scores = third_scores * scale
    near_mask = jnp.repeat(inside, BLOCK_TOKENS, axis=1)
    first_scores = jnp.where(near_mask[None, :, None, None, :], first_scores, -jnp.inf)
    top = jnp.maximum(
        jnp.max(first_scores, axis=-1, keepdims=True),
        jnp.maximum(
            jnp.max(second_scores, axis=-1, keepdims=True),
            jnp.max(third_scores, axis=-1, keepdims=True),
        ),
    )
    near_weights = jnp.exp(first_scores - top)
    global_weights = jnp.exp(second_scores - top)
    random_weights = jnp.exp(third_scores - top)
    total = (
        jnp.sum(near_weights, axis=-1, keepdims=True)
        + jnp.sum(global_weights, axis=-1, keepdims=True)
        + jnp.sum(random_weights, axis=-1, keepdims=True)
    )
    near_probs = (near_weights / total).astype(jnp.bfloat16)
    global_probs = (global_weights / total).astype(jnp.bfloat16)
    random_probs = (random_weights / total).astype(jnp.bfloat16)
    mixed = jnp.einsum(
        "sqgbw,sqwh->sqbgh",
        near_probs,
        window[..., HEAD_SIZE:],
        preferred_element_type=jnp.float32,
    )
    mixed = mixed + jnp.einsum(
        "sqgbw,swh->sqbgh",
        global_probs,
        global_pairs[..., HEAD_SIZE:],
        preferred_element_type=jnp.float32,
    )
    mixed = mixed + jnp.einsum(
        "sqgbw,sqgwh->sqbgh",
        random_probs,
        arrived[..., HEAD_SIZE:],
        preferred_element_type=jnp.float32,
    )
    return mixed.reshape(passages, length, heads_here * HEAD_SIZE).astype(jnp.bfloat16)


def solution(mesh):
    placed = (
        P("groups", "row", "col"),
        P(),
        P("row", "col"),
        P("col"),
        P("row", "col"),
        P("col"),
        P("row", "col"),
        P("col"),
        P("groups", None, None, None),
        P("groups", None, None),
    )
    return jax.shard_map(
        shards, mesh=mesh, in_specs=placed, out_specs=P("groups", "row", "col"), check_vma=False
    )
```

```python
import math

import jax
import jax.numpy as jnp
from jax import lax
from jax.sharding import PartitionSpec as P

HEAD_SIZE = 128
BLOCK_TOKENS = 64
RANDOM_BLOCKS = 2
GLOBAL_BLOCKS = 2


rope_base = 1000000.0
norm_eps = 1e-06

SWAP = [(0, 1), (1, 0)]


def apply_rotation(values, token_positions):
    half = values.shape[-1] // 2
    freqs = 1.0 / rope_base ** (jnp.arange(half, dtype=jnp.float32) * 2.0 / values.shape[-1])
    angles = token_positions[:, None] * freqs[None, :]
    cosine = jnp.concatenate([jnp.cos(angles), jnp.cos(angles)], axis=-1)[None, :, None, :]
    sine = jnp.concatenate([jnp.sin(angles), jnp.sin(angles)], axis=-1)[None, :, None, :]
    turned = jnp.concatenate([-values[..., half:], values[..., :half]], axis=-1)
    return values * cosine + turned * sine


def snake_order(count):
    return [2 * z for z in range(count // 2)] + [2 * z + 1 for z in reversed(range(count // 2))]


def gather_rows(shard, count, here):
    if count != 8:
        return lax.all_gather(shard, "row", axis=0, tiled=True)
    order = snake_order(count)
    position = [0] * count
    for i, d in enumerate(order):
        position[d] = i
    forward = [(order[i], order[(i + 1) % count]) for i in range(count)]
    backward = [(order[i], order[(i - 1) % count]) for i in range(count)]
    half = shard.shape[0] // 2
    ahead, behind = shard[:half], shard[half:]
    ahead_parts, behind_parts = [ahead], [behind]
    for _ in range(count - 1):
        ahead = lax.ppermute(ahead, "row", forward)
        behind = lax.ppermute(behind, "row", backward)
        ahead_parts.append(ahead)
        behind_parts.append(behind)
    table = jnp.array(position, dtype=jnp.int32)
    mine = table[here]
    ahead_pick = (mine - table) % count
    behind_pick = (table - mine) % count
    joined = jnp.concatenate(
        [jnp.stack(ahead_parts)[ahead_pick], jnp.stack(behind_parts)[behind_pick]], axis=1
    )
    return joined.reshape(count * shard.shape[0], shard.shape[1])


def shards(
    tokens,
    gain,
    w_query,
    b_query,
    key_weight,
    b_key,
    value_weight,
    value_bias,
    random_block_index,
    global_block_index,
):
    row_count = lax.axis_size("row")
    here = lax.axis_index("row")
    column = lax.axis_index("col")
    group = lax.axis_index("groups")
    passages, length, _ = tokens.shape
    heads_here = w_query.shape[1] // HEAD_SIZE
    pairs_here = key_weight.shape[1] // HEAD_SIZE
    passage_groups = heads_here // pairs_here
    per_device = length // BLOCK_TOKENS
    passage_blocks = row_count * per_device
    scale = 1.0 / math.sqrt(HEAD_SIZE)

    rotary_cols = (heads_here + pairs_here) * HEAD_SIZE
    split = rotary_cols // 2
    value_cols = pairs_here * HEAD_SIZE
    value_split = value_cols // 2
    rotary_w = jnp.concatenate([w_query, key_weight], axis=1)
    rotary_b = jnp.concatenate([b_query, b_key], axis=0)
    first = group == 0
    panel = jnp.where(
        first,
        jnp.concatenate([rotary_w[:, :split], value_weight[:, :value_split]], axis=1),
        jnp.concatenate([rotary_w[:, split:], value_weight[:, value_split:]], axis=1),
    )
    panel_bias = jnp.where(
        first,
        jnp.concatenate([rotary_b[:split], value_bias[:value_split]]),
        jnp.concatenate([rotary_b[split:], value_bias[value_split:]]),
    )
    full_panel = gather_rows(panel, row_count, here)

    other_half = lax.ppermute(tokens, "col", SWAP)
    partner_half = lax.ppermute(tokens, "groups", SWAP)
    partner_other = lax.ppermute(partner_half, "col", SWAP)
    whole = jnp.where(
        column == 0,
        jnp.concatenate([tokens, other_half], axis=2),
        jnp.concatenate([other_half, tokens], axis=2),
    )
    partner = jnp.where(
        column == 0,
        jnp.concatenate([partner_half, partner_other], axis=2),
        jnp.concatenate([partner_other, partner_half], axis=2),
    )
    both = jnp.concatenate([whole, partner], axis=0)
    widened = both.astype(jnp.float32)
    power = jnp.mean(widened * widened, axis=-1, keepdims=True)
    normed = (
        (widened * lax.rsqrt(power + norm_eps) * gain)
        .astype(jnp.bfloat16)
        .reshape(2 * passages * length, -1)
    )
    token_positions = (here * length + jnp.arange(length, dtype=jnp.int32)).astype(jnp.float32)

    summed = jnp.dot(normed, full_panel, preferred_element_type=jnp.float32) + panel_bias
    summed = summed.reshape(2 * passages, length, split + value_split)
    turned = apply_rotation(
        summed[..., :split].reshape(2 * passages, length, split // HEAD_SIZE, HEAD_SIZE),
        token_positions,
    ).astype(jnp.bfloat16)
    result = jnp.concatenate(
        [turned.reshape(2 * passages, length, split), summed[..., split:].astype(jnp.bfloat16)],
        axis=-1,
    )
    mine = result[:passages]
    returned = lax.ppermute(result[passages:], "groups", SWAP)
    low = jnp.where(first, mine, returned)
    high = jnp.where(first, returned, mine)
    rotary_rows = jnp.concatenate([low[..., :split], high[..., :split]], axis=-1)
    query_rows = rotary_rows[..., : heads_here * HEAD_SIZE]
    key = rotary_rows[..., heads_here * HEAD_SIZE :]
    value_rows = jnp.concatenate([low[..., split:], high[..., split:]], axis=-1)

    pairs = jnp.concatenate([key, value_rows], axis=-1)
    if row_count <= 8:
        by_shift = [pairs] + [
            lax.ppermute(pairs, "row", [(i, (i + k) % row_count) for i in range(row_count)])
            for k in range(1, row_count)
        ]
        gathered = jnp.stack(by_shift)
        owner_slot = (here - jnp.arange(row_count, dtype=jnp.int32)) % row_count
    else:
        gathered = lax.all_gather(pairs, "row", axis=0, tiled=False)
        owner_slot = jnp.arange(row_count, dtype=jnp.int32)
    gathered = gathered.reshape(
        row_count, passages, per_device, BLOCK_TOKENS, pairs_here, 2 * HEAD_SIZE
    )[:, :, :, :, 0]
    gathered = gathered.transpose(1, 0, 2, 3, 4).reshape(
        passages, passage_blocks, BLOCK_TOKENS, 2 * HEAD_SIZE
    )
    block_ids = jnp.arange(passage_blocks, dtype=jnp.int32)
    slot_of_block = owner_slot[block_ids // per_device] * per_device + block_ids % per_device
    kv_blocks = gathered[:, slot_of_block]

    local_blocks = here * per_device + jnp.arange(per_device, dtype=jnp.int32)
    nearby_blocks = local_blocks[:, None] + jnp.arange(3, dtype=jnp.int32)[None, :] - 1
    inside = (nearby_blocks >= 0) & (nearby_blocks < passage_blocks)
    nearby_clamped = jnp.clip(nearby_blocks, 0, passage_blocks - 1)
    passage_ids = jnp.arange(passages, dtype=jnp.int32)
    window = kv_blocks[passage_ids[:, None, None], nearby_clamped[None]]
    window = window.reshape(passages, per_device, 3 * BLOCK_TOKENS, 2 * HEAD_SIZE)

    global_here = lax.dynamic_slice_in_dim(global_block_index, column * pairs_here, pairs_here, 1)
    global_pairs = kv_blocks[passage_ids[:, None], global_here[:, 0, :]]
    global_pairs = global_pairs.reshape(passages, GLOBAL_BLOCKS * BLOCK_TOKENS, 2 * HEAD_SIZE)

    selected = lax.dynamic_slice_in_dim(random_block_index, column * heads_here, heads_here, 2)
    selected = lax.dynamic_slice_in_dim(selected, here * per_device, per_device, 1)
    arrived = kv_blocks[passage_ids[:, None, None, None], selected]
    arrived = arrived.reshape(
        passages, per_device, heads_here, RANDOM_BLOCKS * BLOCK_TOKENS, 2 * HEAD_SIZE
    )

    query_block_rows = query_rows.reshape(
        passages, per_device, BLOCK_TOKENS, heads_here, HEAD_SIZE
    )
    first_scores = jnp.einsum(
        "sqbgh,sqwh->sqgbw",
        query_block_rows,
        window[..., :HEAD_SIZE],
        preferred_element_type=jnp.float32,
    )
    second_scores = jnp.einsum(
        "sqbgh,swh->sqgbw",
        query_block_rows,
        global_pairs[..., :HEAD_SIZE],
        preferred_element_type=jnp.float32,
    )
    third_scores = jnp.einsum(
        "sqbgh,sqgwh->sqgbw",
        query_block_rows,
        arrived[..., :HEAD_SIZE],
        preferred_element_type=jnp.float32,
    )
    first_scores = first_scores * scale
    second_scores = second_scores * scale
    third_scores = third_scores * scale
    near_mask = jnp.repeat(inside, BLOCK_TOKENS, axis=1)
    first_scores = jnp.where(near_mask[None, :, None, None, :], first_scores, -jnp.inf)
    top = jnp.maximum(
        jnp.max(first_scores, axis=-1, keepdims=True),
        jnp.maximum(
            jnp.max(second_scores, axis=-1, keepdims=True),
            jnp.max(third_scores, axis=-1, keepdims=True),
        ),
    )
    near_weights = jnp.exp(first_scores - top)
    global_weights = jnp.exp(second_scores - top)
    random_weights = jnp.exp(third_scores - top)
    total = (
        jnp.sum(near_weights, axis=-1, keepdims=True)
        + jnp.sum(global_weights, axis=-1, keepdims=True)
        + jnp.sum(random_weights, axis=-1, keepdims=True)
    )
    near_probs = (near_weights / total).astype(jnp.bfloat16)
    global_probs = (global_weights / total).astype(jnp.bfloat16)
    random_probs = (random_weights / total).astype(jnp.bfloat16)
    mixed = jnp.einsum(
        "sqgbw,sqwh->sqbgh",
        near_probs,
        window[..., HEAD_SIZE:],
        preferred_element_type=jnp.float32,
    )
    mixed = mixed + jnp.einsum(
        "sqgbw,swh->sqbgh",
        global_probs,
        global_pairs[..., HEAD_SIZE:],
        preferred_element_type=jnp.float32,
    )
    mixed = mixed + jnp.einsum(
        "sqgbw,sqgwh->sqbgh",
        random_probs,
        arrived[..., HEAD_SIZE:],
        preferred_element_type=jnp.float32,
    )
    return mixed.reshape(passages, length, heads_here * HEAD_SIZE).astype(jnp.bfloat16)


def solution(mesh):
    placed = (
        P("groups", "row", "col"),
        P(),
        P("row", "col"),
        P("col"),
        P("row", "col"),
        P("col"),
        P("row", "col"),
        P("col"),
        P("groups", None, None, None),
        P("groups", None, None),
    )
    return jax.shard_map(
        shards, mesh=mesh, in_specs=placed, out_specs=P("groups", "row", "col"), check_vma=False
    )
```

```python
import math

import jax
import jax.numpy as jnp
from jax import lax
from jax.sharding import PartitionSpec as P

HEAD_SIZE = 128
BLOCK_TOKENS = 64
RANDOM_BLOCKS = 2
GLOBAL_BLOCKS = 2


rope_base = 1000000.0
norm_eps = 1e-06

SWAP = [(0, 1), (1, 0)]


def apply_rotation(values, token_positions):
    half = values.shape[-1] // 2
    freqs = 1.0 / rope_base ** (jnp.arange(half, dtype=jnp.float32) * 2.0 / values.shape[-1])
    angles = token_positions[:, None] * freqs[None, :]
    cosine = jnp.concatenate([jnp.cos(angles), jnp.cos(angles)], axis=-1)[None, :, None, :]
    sine = jnp.concatenate([jnp.sin(angles), jnp.sin(angles)], axis=-1)[None, :, None, :]
    turned = jnp.concatenate([-values[..., half:], values[..., :half]], axis=-1)
    return values * cosine + turned * sine


def snake_order(count):
    return [2 * z for z in range(count // 2)] + [2 * z + 1 for z in reversed(range(count // 2))]


def project_rows(normed, shard, count, here, column):
    features = normed.shape[1]
    shift = (count // 2) * column
    if count != 8:
        full = lax.all_gather(shard, "row", axis=0, tiled=True)
        full = jnp.where(
            column == 0,
            full,
            jnp.concatenate([full[features // 2 :], full[: features // 2]], axis=0),
        )
        return jnp.dot(normed, full, preferred_element_type=jnp.float32)
    order = snake_order(count)
    position = [0] * count
    for i, d in enumerate(order):
        position[d] = i
    forward = [(order[i], order[(i + 1) % count]) for i in range(count)]
    backward = [(order[i], order[(i - 1) % count]) for i in range(count)]
    half = shard.shape[0] // 2
    chunks = normed.reshape(normed.shape[0], count, 2, half).transpose(1, 2, 0, 3)
    table = jnp.array(position, dtype=jnp.int32)
    ring = jnp.array(order, dtype=jnp.int32)
    mine = table[here]

    def term(source, part, piece):
        rows = chunks[(source + shift) % count, part]
        return jnp.dot(rows, piece, preferred_element_type=jnp.float32)

    ahead, behind = shard[:half], shard[half:]
    total = term(here, 0, ahead) + term(here, 1, behind)
    for step in range(1, count):
        ahead = lax.ppermute(ahead, "row", forward)
        behind = lax.ppermute(behind, "row", backward)
        total = total + term(ring[(mine - step) % count], 0, ahead)
        total = total + term(ring[(mine + step) % count], 1, behind)
    return total


def shards(
    tokens,
    gain,
    w_query,
    b_query,
    key_weight,
    b_key,
    value_weight,
    value_bias,
    random_block_index,
    global_block_index,
):
    row_count = lax.axis_size("row")
    here = lax.axis_index("row")
    column = lax.axis_index("col")
    group = lax.axis_index("groups")
    passages, length, _ = tokens.shape
    heads_here = w_query.shape[1] // HEAD_SIZE
    pairs_here = key_weight.shape[1] // HEAD_SIZE
    passage_groups = heads_here // pairs_here
    per_device = length // BLOCK_TOKENS
    passage_blocks = row_count * per_device
    scale = 1.0 / math.sqrt(HEAD_SIZE)

    rotary_cols = (heads_here + pairs_here) * HEAD_SIZE
    split = rotary_cols // 2
    value_cols = pairs_here * HEAD_SIZE
    value_split = value_cols // 2
    rotary_w = jnp.concatenate([w_query, key_weight], axis=1)
    rotary_b = jnp.concatenate([b_query, b_key], axis=0)
    first = group == 0
    panel = jnp.where(
        first,
        jnp.concatenate([rotary_w[:, :split], value_weight[:, :value_split]], axis=1),
        jnp.concatenate([rotary_w[:, split:], value_weight[:, value_split:]], axis=1),
    )
    panel_bias = jnp.where(
        first,
        jnp.concatenate([rotary_b[:split], value_bias[:value_split]]),
        jnp.concatenate([rotary_b[split:], value_bias[value_split:]]),
    )

    other_half = lax.ppermute(tokens, "col", SWAP)
    partner_half = lax.ppermute(tokens, "groups", SWAP)
    partner_other = lax.ppermute(partner_half, "col", SWAP)
    both = jnp.concatenate(
        [
            jnp.concatenate([tokens, other_half], axis=2),
            jnp.concatenate([partner_half, partner_other], axis=2),
        ],
        axis=0,
    )
    features = both.shape[2]
    gain_here = jnp.where(
        column == 0,
        gain,
        jnp.concatenate([gain[features // 2 :], gain[: features // 2]]),
    )
    widened = both.astype(jnp.float32)
    power = jnp.mean(widened * widened, axis=-1, keepdims=True)
    normed = (
        (widened * lax.rsqrt(power + norm_eps) * gain_here)
        .astype(jnp.bfloat16)
        .reshape(2 * passages * length, -1)
    )
    token_positions = (here * length + jnp.arange(length, dtype=jnp.int32)).astype(jnp.float32)

    summed = project_rows(normed, panel, row_count, here, column) + panel_bias
    summed = summed.reshape(2 * passages, length, split + value_split)
    turned = apply_rotation(
        summed[..., :split].reshape(2 * passages, length, split // HEAD_SIZE, HEAD_SIZE),
        token_positions,
    ).astype(jnp.bfloat16)
    result = jnp.concatenate(
        [turned.reshape(2 * passages, length, split), summed[..., split:].astype(jnp.bfloat16)],
        axis=-1,
    )
    mine = result[:passages]
    returned = lax.ppermute(result[passages:], "groups", SWAP)
    low = jnp.where(first, mine, returned)
    high = jnp.where(first, returned, mine)
    rotary_rows = jnp.concatenate([low[..., :split], high[..., :split]], axis=-1)
    query_rows = rotary_rows[..., : heads_here * HEAD_SIZE]
    key = rotary_rows[..., heads_here * HEAD_SIZE :]
    value_rows = jnp.concatenate([low[..., split:], high[..., split:]], axis=-1)

    pairs = jnp.concatenate([key, value_rows], axis=-1)
    if row_count <= 8:
        by_shift = [pairs] + [
            lax.ppermute(pairs, "row", [(i, (i + k) % row_count) for i in range(row_count)])
            for k in range(1, row_count)
        ]
        gathered = jnp.stack(by_shift)
        owner_slot = (here - jnp.arange(row_count, dtype=jnp.int32)) % row_count
    else:
        gathered = lax.all_gather(pairs, "row", axis=0, tiled=False)
        owner_slot = jnp.arange(row_count, dtype=jnp.int32)
    gathered = gathered.reshape(
        row_count, passages, per_device, BLOCK_TOKENS, pairs_here, 2 * HEAD_SIZE
    )[:, :, :, :, 0]
    gathered = gathered.transpose(1, 0, 2, 3, 4).reshape(
        passages, passage_blocks, BLOCK_TOKENS, 2 * HEAD_SIZE
    )
    block_ids = jnp.arange(passage_blocks, dtype=jnp.int32)
    slot_of_block = owner_slot[block_ids // per_device] * per_device + block_ids % per_device
    kv_blocks = gathered[:, slot_of_block]

    local_blocks = here * per_device + jnp.arange(per_device, dtype=jnp.int32)
    nearby_blocks = local_blocks[:, None] + jnp.arange(3, dtype=jnp.int32)[None, :] - 1
    inside = (nearby_blocks >= 0) & (nearby_blocks < passage_blocks)
    nearby_clamped = jnp.clip(nearby_blocks, 0, passage_blocks - 1)
    passage_ids = jnp.arange(passages, dtype=jnp.int32)
    window = kv_blocks[passage_ids[:, None, None], nearby_clamped[None]]
    window = window.reshape(passages, per_device, 3 * BLOCK_TOKENS, 2 * HEAD_SIZE)

    global_here = lax.dynamic_slice_in_dim(global_block_index, column * pairs_here, pairs_here, 1)
    global_pairs = kv_blocks[passage_ids[:, None], global_here[:, 0, :]]
    global_pairs = global_pairs.reshape(passages, GLOBAL_BLOCKS * BLOCK_TOKENS, 2 * HEAD_SIZE)

    selected = lax.dynamic_slice_in_dim(random_block_index, column * heads_here, heads_here, 2)
    selected = lax.dynamic_slice_in_dim(selected, here * per_device, per_device, 1)
    arrived = kv_blocks[passage_ids[:, None, None, None], selected]
    arrived = arrived.reshape(
        passages, per_device, heads_here, RANDOM_BLOCKS * BLOCK_TOKENS, 2 * HEAD_SIZE
    )

    query_block_rows = query_rows.reshape(
        passages, per_device, BLOCK_TOKENS, heads_here, HEAD_SIZE
    )
    first_scores = jnp.einsum(
        "sqbgh,sqwh->sqgbw",
        query_block_rows,
        window[..., :HEAD_SIZE],
        preferred_element_type=jnp.float32,
    )
    second_scores = jnp.einsum(
        "sqbgh,swh->sqgbw",
        query_block_rows,
        global_pairs[..., :HEAD_SIZE],
        preferred_element_type=jnp.float32,
    )
    third_scores = jnp.einsum(
        "sqbgh,sqgwh->sqgbw",
        query_block_rows,
        arrived[..., :HEAD_SIZE],
        preferred_element_type=jnp.float32,
    )
    first_scores = first_scores * scale
    second_scores = second_scores * scale
    third_scores = third_scores * scale
    near_mask = jnp.repeat(inside, BLOCK_TOKENS, axis=1)
    first_scores = jnp.where(near_mask[None, :, None, None, :], first_scores, -jnp.inf)
    top = jnp.maximum(
        jnp.max(first_scores, axis=-1, keepdims=True),
        jnp.maximum(
            jnp.max(second_scores, axis=-1, keepdims=True),
            jnp.max(third_scores, axis=-1, keepdims=True),
        ),
    )
    near_weights = jnp.exp(first_scores - top)
    global_weights = jnp.exp(second_scores - top)
    random_weights = jnp.exp(third_scores - top)
    total = (
        jnp.sum(near_weights, axis=-1, keepdims=True)
        + jnp.sum(global_weights, axis=-1, keepdims=True)
        + jnp.sum(random_weights, axis=-1, keepdims=True)
    )
    near_probs = (near_weights / total).astype(jnp.bfloat16)
    global_probs = (global_weights / total).astype(jnp.bfloat16)
    random_probs = (random_weights / total).astype(jnp.bfloat16)
    mixed = jnp.einsum(
        "sqgbw,sqwh->sqbgh",
        near_probs,
        window[..., HEAD_SIZE:],
        preferred_element_type=jnp.float32,
    )
    mixed = mixed + jnp.einsum(
        "sqgbw,swh->sqbgh",
        global_probs,
        global_pairs[..., HEAD_SIZE:],
        preferred_element_type=jnp.float32,
    )
    mixed = mixed + jnp.einsum(
        "sqgbw,sqgwh->sqbgh",
        random_probs,
        arrived[..., HEAD_SIZE:],
        preferred_element_type=jnp.float32,
    )
    return mixed.reshape(passages, length, heads_here * HEAD_SIZE).astype(jnp.bfloat16)


def solution(mesh):
    placed = (
        P("groups", "row", "col"),
        P(),
        P("row", "col"),
        P("col"),
        P("row", "col"),
        P("col"),
        P("row", "col"),
        P("col"),
        P("groups", None, None, None),
        P("groups", None, None),
    )
    return jax.shard_map(
        shards, mesh=mesh, in_specs=placed, out_specs=P("groups", "row", "col"), check_vma=False
    )
```

```python
import math

import jax
import jax.numpy as jnp
from jax import lax
from jax.sharding import PartitionSpec as P

HEAD_SIZE = 128
BLOCK_TOKENS = 64
RANDOM_BLOCKS = 2
GLOBAL_BLOCKS = 2


rope_base = 1000000.0
norm_eps = 1e-06

SWAP = [(0, 1), (1, 0)]


def apply_rotation(values, token_positions):
    half = values.shape[-1] // 2
    freqs = 1.0 / rope_base ** (jnp.arange(half, dtype=jnp.float32) * 2.0 / values.shape[-1])
    angles = token_positions[:, None] * freqs[None, :]
    cosine = jnp.concatenate([jnp.cos(angles), jnp.cos(angles)], axis=-1)[None, :, None, :]
    sine = jnp.concatenate([jnp.sin(angles), jnp.sin(angles)], axis=-1)[None, :, None, :]
    turned = jnp.concatenate([-values[..., half:], values[..., :half]], axis=-1)
    return values * cosine + turned * sine


def snake_order(count):
    return [2 * z for z in range(count // 2)] + [2 * z + 1 for z in reversed(range(count // 2))]


def gather_rows(shard, count, here):
    if count != 8:
        return lax.all_gather(shard, "row", axis=0, tiled=True)
    order = snake_order(count)
    position = [0] * count
    for i, d in enumerate(order):
        position[d] = i
    forward = [(order[i], order[(i + 1) % count]) for i in range(count)]
    backward = [(order[i], order[(i - 1) % count]) for i in range(count)]
    half = shard.shape[0] // 2
    ahead, behind = shard[:half], shard[half:]
    table = jnp.array(position, dtype=jnp.int32)
    ring = jnp.array(order, dtype=jnp.int32)
    mine = table[here]
    joined = jnp.zeros((count, 2, half, shard.shape[1]), shard.dtype)
    joined = lax.dynamic_update_slice(joined, ahead[None, None], (here, 0, 0, 0))
    joined = lax.dynamic_update_slice(joined, behind[None, None], (here, 1, 0, 0))
    for step in range(1, count):
        ahead = lax.ppermute(ahead, "row", forward)
        behind = lax.ppermute(behind, "row", backward)
        ahead_source = ring[(mine - step) % count]
        behind_source = ring[(mine + step) % count]
        joined = lax.dynamic_update_slice(joined, ahead[None, None], (ahead_source, 0, 0, 0))
        joined = lax.dynamic_update_slice(joined, behind[None, None], (behind_source, 1, 0, 0))
    return joined.reshape(count * shard.shape[0], shard.shape[1])


def shards(
    tokens,
    gain,
    w_query,
    b_query,
    key_weight,
    b_key,
    value_weight,
    value_bias,
    random_block_index,
    global_block_index,
):
    row_count = lax.axis_size("row")
    here = lax.axis_index("row")
    column = lax.axis_index("col")
    group = lax.axis_index("groups")
    passages, length, _ = tokens.shape
    heads_here = w_query.shape[1] // HEAD_SIZE
    pairs_here = key_weight.shape[1] // HEAD_SIZE
    passage_groups = heads_here // pairs_here
    per_device = length // BLOCK_TOKENS
    passage_blocks = row_count * per_device
    scale = 1.0 / math.sqrt(HEAD_SIZE)

    rotary_cols = (heads_here + pairs_here) * HEAD_SIZE
    split = rotary_cols // 2
    value_cols = pairs_here * HEAD_SIZE
    value_split = value_cols // 2
    rotary_w = jnp.concatenate([w_query, key_weight], axis=1)
    rotary_b = jnp.concatenate([b_query, b_key], axis=0)
    first = group == 0
    panel = jnp.concatenate(
        [
            lax.dynamic_slice_in_dim(rotary_w, group * split, split, 1),
            lax.dynamic_slice_in_dim(value_weight, group * value_split, value_split, 1),
        ],
        axis=1,
    )
    panel_bias = jnp.where(
        first,
        jnp.concatenate([rotary_b[:split], value_bias[:value_split]]),
        jnp.concatenate([rotary_b[split:], value_bias[value_split:]]),
    )
    full_panel = gather_rows(panel, row_count, here)

    other_half = lax.ppermute(tokens, "col", SWAP)
    partner_half = lax.ppermute(tokens, "groups", SWAP)
    partner_other = lax.ppermute(partner_half, "col", SWAP)
    whole = jnp.where(
        column == 0,
        jnp.concatenate([tokens, other_half], axis=2),
        jnp.concatenate([other_half, tokens], axis=2),
    )
    partner = jnp.where(
        column == 0,
        jnp.concatenate([partner_half, partner_other], axis=2),
        jnp.concatenate([partner_other, partner_half], axis=2),
    )
    both = jnp.concatenate([whole, partner], axis=0)
    widened = both.astype(jnp.float32)
    power = jnp.mean(widened * widened, axis=-1, keepdims=True)
    normed = (
        (widened * lax.rsqrt(power + norm_eps) * gain)
        .astype(jnp.bfloat16)
        .reshape(2 * passages * length, -1)
    )
    token_positions = (here * length + jnp.arange(length, dtype=jnp.int32)).astype(jnp.float32)

    summed = jnp.dot(normed, full_panel, preferred_element_type=jnp.float32) + panel_bias
    summed = summed.reshape(2 * passages, length, split + value_split)
    turned = apply_rotation(
        summed[..., :split].reshape(2 * passages, length, split // HEAD_SIZE, HEAD_SIZE),
        token_positions,
    ).astype(jnp.bfloat16)
    result = jnp.concatenate(
        [turned.reshape(2 * passages, length, split), summed[..., split:].astype(jnp.bfloat16)],
        axis=-1,
    )
    mine = result[:passages]
    returned = lax.ppermute(result[passages:], "groups", SWAP)
    low = jnp.where(first, mine, returned)
    high = jnp.where(first, returned, mine)
    rotary_rows = jnp.concatenate([low[..., :split], high[..., :split]], axis=-1)
    query_rows = rotary_rows[..., : heads_here * HEAD_SIZE]
    key = rotary_rows[..., heads_here * HEAD_SIZE :]
    value_rows = jnp.concatenate([low[..., split:], high[..., split:]], axis=-1)

    pairs = jnp.concatenate([key, value_rows], axis=-1)
    if row_count <= 8:
        by_shift = [pairs] + [
            lax.ppermute(pairs, "row", [(i, (i + k) % row_count) for i in range(row_count)])
            for k in range(1, row_count)
        ]
        gathered = jnp.stack(by_shift)
        owner_slot = (here - jnp.arange(row_count, dtype=jnp.int32)) % row_count
    else:
        gathered = lax.all_gather(pairs, "row", axis=0, tiled=False)
        owner_slot = jnp.arange(row_count, dtype=jnp.int32)
    gathered = gathered.reshape(
        row_count, passages, per_device, BLOCK_TOKENS, pairs_here, 2 * HEAD_SIZE
    )[:, :, :, :, 0]
    gathered = gathered.transpose(1, 0, 2, 3, 4).reshape(
        passages, passage_blocks, BLOCK_TOKENS, 2 * HEAD_SIZE
    )
    block_ids = jnp.arange(passage_blocks, dtype=jnp.int32)
    slot_of_block = owner_slot[block_ids // per_device] * per_device + block_ids % per_device
    kv_blocks = gathered[:, slot_of_block]

    local_blocks = here * per_device + jnp.arange(per_device, dtype=jnp.int32)
    nearby_blocks = local_blocks[:, None] + jnp.arange(3, dtype=jnp.int32)[None, :] - 1
    inside = (nearby_blocks >= 0) & (nearby_blocks < passage_blocks)
    nearby_clamped = jnp.clip(nearby_blocks, 0, passage_blocks - 1)
    passage_ids = jnp.arange(passages, dtype=jnp.int32)
    window = kv_blocks[passage_ids[:, None, None], nearby_clamped[None]]
    window = window.reshape(passages, per_device, 3 * BLOCK_TOKENS, 2 * HEAD_SIZE)

    global_here = lax.dynamic_slice_in_dim(global_block_index, column * pairs_here, pairs_here, 1)
    global_pairs = kv_blocks[passage_ids[:, None], global_here[:, 0, :]]
    global_pairs = global_pairs.reshape(passages, GLOBAL_BLOCKS * BLOCK_TOKENS, 2 * HEAD_SIZE)

    selected = lax.dynamic_slice_in_dim(random_block_index, column * heads_here, heads_here, 2)
    selected = lax.dynamic_slice_in_dim(selected, here * per_device, per_device, 1)
    arrived = kv_blocks[passage_ids[:, None, None, None], selected]
    arrived = arrived.reshape(
        passages, per_device, heads_here, RANDOM_BLOCKS * BLOCK_TOKENS, 2 * HEAD_SIZE
    )

    query_block_rows = query_rows.reshape(
        passages, per_device, BLOCK_TOKENS, heads_here, HEAD_SIZE
    )
    first_scores = jnp.einsum(
        "sqbgh,sqwh->sqgbw",
        query_block_rows,
        window[..., :HEAD_SIZE],
        preferred_element_type=jnp.float32,
    )
    second_scores = jnp.einsum(
        "sqbgh,swh->sqgbw",
        query_block_rows,
        global_pairs[..., :HEAD_SIZE],
        preferred_element_type=jnp.float32,
    )
    third_scores = jnp.einsum(
        "sqbgh,sqgwh->sqgbw",
        query_block_rows,
        arrived[..., :HEAD_SIZE],
        preferred_element_type=jnp.float32,
    )
    first_scores = first_scores * scale
    second_scores = second_scores * scale
    third_scores = third_scores * scale
    near_mask = jnp.repeat(inside, BLOCK_TOKENS, axis=1)
    first_scores = jnp.where(near_mask[None, :, None, None, :], first_scores, -jnp.inf)
    top = jnp.maximum(
        jnp.max(first_scores, axis=-1, keepdims=True),
        jnp.maximum(
            jnp.max(second_scores, axis=-1, keepdims=True),
            jnp.max(third_scores, axis=-1, keepdims=True),
        ),
    )
    near_weights = jnp.exp(first_scores - top)
    global_weights = jnp.exp(second_scores - top)
    random_weights = jnp.exp(third_scores - top)
    total = (
        jnp.sum(near_weights, axis=-1, keepdims=True)
        + jnp.sum(global_weights, axis=-1, keepdims=True)
        + jnp.sum(random_weights, axis=-1, keepdims=True)
    )
    near_probs = (near_weights / total).astype(jnp.bfloat16)
    global_probs = (global_weights / total).astype(jnp.bfloat16)
    random_probs = (random_weights / total).astype(jnp.bfloat16)
    mixed = jnp.einsum(
        "sqgbw,sqwh->sqbgh",
        near_probs,
        window[..., HEAD_SIZE:],
        preferred_element_type=jnp.float32,
    )
    mixed = mixed + jnp.einsum(
        "sqgbw,swh->sqbgh",
        global_probs,
        global_pairs[..., HEAD_SIZE:],
        preferred_element_type=jnp.float32,
    )
    mixed = mixed + jnp.einsum(
        "sqgbw,sqgwh->sqbgh",
        random_probs,
        arrived[..., HEAD_SIZE:],
        preferred_element_type=jnp.float32,
    )
    return mixed.reshape(passages, length, heads_here * HEAD_SIZE).astype(jnp.bfloat16)


def solution(mesh):
    placed = (
        P("groups", "row", "col"),
        P(),
        P("row", "col"),
        P("col"),
        P("row", "col"),
        P("col"),
        P("row", "col"),
        P("col"),
        P("groups", None, None, None),
        P("groups", None, None),
    )
    return jax.shard_map(
        shards, mesh=mesh, in_specs=placed, out_specs=P("groups", "row", "col"), check_vma=False
    )
```

```python
import math

import jax
import jax.numpy as jnp
from jax import lax
from jax.sharding import PartitionSpec as P

HEAD_SIZE = 128
BLOCK_TOKENS = 64
RANDOM_BLOCKS = 2
GLOBAL_BLOCKS = 2


rope_base = 1000000.0
norm_eps = 1e-06

SWAP = [(0, 1), (1, 0)]


def apply_rotation(values, token_positions):
    half = values.shape[-1] // 2
    freqs = 1.0 / rope_base ** (jnp.arange(half, dtype=jnp.float32) * 2.0 / values.shape[-1])
    angles = token_positions[:, None] * freqs[None, :]
    cosine = jnp.concatenate([jnp.cos(angles), jnp.cos(angles)], axis=-1)[None, :, None, :]
    sine = jnp.concatenate([jnp.sin(angles), jnp.sin(angles)], axis=-1)[None, :, None, :]
    turned = jnp.concatenate([-values[..., half:], values[..., :half]], axis=-1)
    return values * cosine + turned * sine


def snake_order(count):
    return [2 * z for z in range(count // 2)] + [2 * z + 1 for z in reversed(range(count // 2))]


def gather_rows(shard, count, here):
    if count != 8:
        return lax.all_gather(shard, "row", axis=0, tiled=True)
    order = snake_order(count)
    position = [0] * count
    for i, d in enumerate(order):
        position[d] = i
    forward = [(order[i], order[(i + 1) % count]) for i in range(count)]
    backward = [(order[i], order[(i - 1) % count]) for i in range(count)]
    half = shard.shape[0] // 2
    ahead, behind = shard[:half], shard[half:]
    ahead_parts, behind_parts = [ahead], [behind]
    for _ in range(count - 1):
        ahead = lax.ppermute(ahead, "row", forward)
        behind = lax.ppermute(behind, "row", backward)
        ahead_parts.append(ahead)
        behind_parts.append(behind)
    table = jnp.array(position, dtype=jnp.int32)
    mine = table[here]
    ahead_pick = (mine - table) % count
    behind_pick = (table - mine) % count
    joined = jnp.concatenate(
        [jnp.stack(ahead_parts)[ahead_pick], jnp.stack(behind_parts)[behind_pick]], axis=1
    )
    return joined.reshape(count * shard.shape[0], shard.shape[1])


def shards(
    tokens,
    gain,
    w_query,
    b_query,
    key_weight,
    b_key,
    value_weight,
    value_bias,
    random_block_index,
    global_block_index,
):
    row_count = lax.axis_size("row")
    here = lax.axis_index("row")
    column = lax.axis_index("col")
    group = lax.axis_index("groups")
    passages, length, _ = tokens.shape
    heads_here = w_query.shape[1] // HEAD_SIZE
    pairs_here = key_weight.shape[1] // HEAD_SIZE
    passage_groups = heads_here // pairs_here
    per_device = length // BLOCK_TOKENS
    passage_blocks = row_count * per_device
    scale = 1.0 / math.sqrt(HEAD_SIZE)

    rotary_cols = (heads_here + pairs_here) * HEAD_SIZE
    split = rotary_cols // 2
    value_cols = pairs_here * HEAD_SIZE
    value_split = value_cols // 2
    rotary_w = jnp.concatenate([w_query, key_weight], axis=1)
    rotary_b = jnp.concatenate([b_query, b_key], axis=0)
    first = group == 0
    late_start = group * split + split - HEAD_SIZE
    early_panel = jnp.concatenate(
        [
            lax.dynamic_slice_in_dim(rotary_w, late_start, HEAD_SIZE, 1),
            lax.dynamic_slice_in_dim(value_weight, group * value_split, value_split, 1),
        ],
        axis=1,
    )
    early_bias = jnp.concatenate(
        [
            lax.dynamic_slice_in_dim(rotary_b, late_start, HEAD_SIZE, 0),
            lax.dynamic_slice_in_dim(value_bias, group * value_split, value_split, 0),
        ]
    )
    late_panel = lax.dynamic_slice_in_dim(rotary_w, group * split, split - HEAD_SIZE, 1)
    late_bias = lax.dynamic_slice_in_dim(rotary_b, group * split, split - HEAD_SIZE, 0)
    early_full = gather_rows(early_panel, row_count, here)
    late_full = gather_rows(late_panel, row_count, here)

    other_half = lax.ppermute(tokens, "col", SWAP)
    partner_half = lax.ppermute(tokens, "groups", SWAP)
    partner_other = lax.ppermute(partner_half, "col", SWAP)
    whole = jnp.where(
        column == 0,
        jnp.concatenate([tokens, other_half], axis=2),
        jnp.concatenate([other_half, tokens], axis=2),
    )
    partner = jnp.where(
        column == 0,
        jnp.concatenate([partner_half, partner_other], axis=2),
        jnp.concatenate([partner_other, partner_half], axis=2),
    )
    both = jnp.concatenate([whole, partner], axis=0)
    widened = both.astype(jnp.float32)
    power = jnp.mean(widened * widened, axis=-1, keepdims=True)
    normed = (
        (widened * lax.rsqrt(power + norm_eps) * gain)
        .astype(jnp.bfloat16)
        .reshape(2 * passages * length, -1)
    )
    token_positions = (here * length + jnp.arange(length, dtype=jnp.int32)).astype(jnp.float32)

    def project(full, bias, rotary_heads):
        summed = jnp.dot(normed, full, preferred_element_type=jnp.float32) + bias
        summed = summed.reshape(2 * passages, length, -1)
        rotary_width = rotary_heads * HEAD_SIZE
        turned = apply_rotation(
            summed[..., :rotary_width].reshape(2 * passages, length, rotary_heads, HEAD_SIZE),
            token_positions,
        ).astype(jnp.bfloat16)
        result = jnp.concatenate(
            [
                turned.reshape(2 * passages, length, rotary_width),
                summed[..., rotary_width:].astype(jnp.bfloat16),
            ],
            axis=-1,
        )
        mine = result[:passages]
        returned = lax.ppermute(result[passages:], "groups", SWAP)
        return jnp.where(first, mine, returned), jnp.where(first, returned, mine)

    early_low, early_high = project(early_full, early_bias, 1)
    key = early_high[..., :HEAD_SIZE]
    value_rows = jnp.concatenate(
        [early_low[..., HEAD_SIZE:], early_high[..., HEAD_SIZE:]], axis=-1
    )
    late_low, late_high = project(late_full, late_bias, split // HEAD_SIZE - 1)
    query_rows = jnp.concatenate([late_low, early_low[..., :HEAD_SIZE], late_high], axis=-1)

    pairs = jnp.concatenate([key, value_rows], axis=-1)
    if row_count <= 8:
        by_shift = [pairs] + [
            lax.ppermute(pairs, "row", [(i, (i + k) % row_count) for i in range(row_count)])
            for k in range(1, row_count)
        ]
        gathered = jnp.stack(by_shift)
        owner_slot = (here - jnp.arange(row_count, dtype=jnp.int32)) % row_count
    else:
        gathered = lax.all_gather(pairs, "row", axis=0, tiled=False)
        owner_slot = jnp.arange(row_count, dtype=jnp.int32)
    gathered = gathered.reshape(
        row_count, passages, per_device, BLOCK_TOKENS, pairs_here, 2 * HEAD_SIZE
    )[:, :, :, :, 0]
    gathered = gathered.transpose(1, 0, 2, 3, 4).reshape(
        passages, passage_blocks, BLOCK_TOKENS, 2 * HEAD_SIZE
    )
    block_ids = jnp.arange(passage_blocks, dtype=jnp.int32)
    slot_of_block = owner_slot[block_ids // per_device] * per_device + block_ids % per_device
    kv_blocks = gathered[:, slot_of_block]

    local_blocks = here * per_device + jnp.arange(per_device, dtype=jnp.int32)
    nearby_blocks = local_blocks[:, None] + jnp.arange(3, dtype=jnp.int32)[None, :] - 1
    inside = (nearby_blocks >= 0) & (nearby_blocks < passage_blocks)
    nearby_clamped = jnp.clip(nearby_blocks, 0, passage_blocks - 1)
    passage_ids = jnp.arange(passages, dtype=jnp.int32)
    window = kv_blocks[passage_ids[:, None, None], nearby_clamped[None]]
    window = window.reshape(passages, per_device, 3 * BLOCK_TOKENS, 2 * HEAD_SIZE)

    global_here = lax.dynamic_slice_in_dim(global_block_index, column * pairs_here, pairs_here, 1)
    global_pairs = kv_blocks[passage_ids[:, None], global_here[:, 0, :]]
    global_pairs = global_pairs.reshape(passages, GLOBAL_BLOCKS * BLOCK_TOKENS, 2 * HEAD_SIZE)

    selected = lax.dynamic_slice_in_dim(random_block_index, column * heads_here, heads_here, 2)
    selected = lax.dynamic_slice_in_dim(selected, here * per_device, per_device, 1)
    arrived = kv_blocks[passage_ids[:, None, None, None], selected]
    arrived = arrived.reshape(
        passages, per_device, heads_here, RANDOM_BLOCKS * BLOCK_TOKENS, 2 * HEAD_SIZE
    )

    query_block_rows = query_rows.reshape(
        passages, per_device, BLOCK_TOKENS, heads_here, HEAD_SIZE
    )
    first_scores = jnp.einsum(
        "sqbgh,sqwh->sqgbw",
        query_block_rows,
        window[..., :HEAD_SIZE],
        preferred_element_type=jnp.float32,
    )
    second_scores = jnp.einsum(
        "sqbgh,swh->sqgbw",
        query_block_rows,
        global_pairs[..., :HEAD_SIZE],
        preferred_element_type=jnp.float32,
    )
    third_scores = jnp.einsum(
        "sqbgh,sqgwh->sqgbw",
        query_block_rows,
        arrived[..., :HEAD_SIZE],
        preferred_element_type=jnp.float32,
    )
    first_scores = first_scores * scale
    second_scores = second_scores * scale
    third_scores = third_scores * scale
    near_mask = jnp.repeat(inside, BLOCK_TOKENS, axis=1)
    first_scores = jnp.where(near_mask[None, :, None, None, :], first_scores, -jnp.inf)
    top = jnp.maximum(
        jnp.max(first_scores, axis=-1, keepdims=True),
        jnp.maximum(
            jnp.max(second_scores, axis=-1, keepdims=True),
            jnp.max(third_scores, axis=-1, keepdims=True),
        ),
    )
    near_weights = jnp.exp(first_scores - top)
    global_weights = jnp.exp(second_scores - top)
    random_weights = jnp.exp(third_scores - top)
    total = (
        jnp.sum(near_weights, axis=-1, keepdims=True)
        + jnp.sum(global_weights, axis=-1, keepdims=True)
        + jnp.sum(random_weights, axis=-1, keepdims=True)
    )
    near_probs = (near_weights / total).astype(jnp.bfloat16)
    global_probs = (global_weights / total).astype(jnp.bfloat16)
    random_probs = (random_weights / total).astype(jnp.bfloat16)
    mixed = jnp.einsum(
        "sqgbw,sqwh->sqbgh",
        near_probs,
        window[..., HEAD_SIZE:],
        preferred_element_type=jnp.float32,
    )
    mixed = mixed + jnp.einsum(
        "sqgbw,swh->sqbgh",
        global_probs,
        global_pairs[..., HEAD_SIZE:],
        preferred_element_type=jnp.float32,
    )
    mixed = mixed + jnp.einsum(
        "sqgbw,sqgwh->sqbgh",
        random_probs,
        arrived[..., HEAD_SIZE:],
        preferred_element_type=jnp.float32,
    )
    return mixed.reshape(passages, length, heads_here * HEAD_SIZE).astype(jnp.bfloat16)


def solution(mesh):
    placed = (
        P("groups", "row", "col"),
        P(),
        P("row", "col"),
        P("col"),
        P("row", "col"),
        P("col"),
        P("row", "col"),
        P("col"),
        P("groups", None, None, None),
        P("groups", None, None),
    )
    return jax.shard_map(
        shards, mesh=mesh, in_specs=placed, out_specs=P("groups", "row", "col"), check_vma=False
    )
```

```python
import math

import jax
import jax.numpy as jnp
from jax import lax
from jax.sharding import PartitionSpec as P

HEAD_SIZE = 128
BLOCK_TOKENS = 64
RANDOM_BLOCKS = 2
GLOBAL_BLOCKS = 2


rope_base = 1000000.0
norm_eps = 1e-06

SWAP = [(0, 1), (1, 0)]


def apply_rotation(values, token_positions):
    half = values.shape[-1] // 2
    freqs = 1.0 / rope_base ** (jnp.arange(half, dtype=jnp.float32) * 2.0 / values.shape[-1])
    angles = token_positions[:, None] * freqs[None, :]
    cosine = jnp.concatenate([jnp.cos(angles), jnp.cos(angles)], axis=-1)[None, :, None, :]
    sine = jnp.concatenate([jnp.sin(angles), jnp.sin(angles)], axis=-1)[None, :, None, :]
    turned = jnp.concatenate([-values[..., half:], values[..., :half]], axis=-1)
    return values * cosine + turned * sine


def snake_order(count):
    return [2 * z for z in range(count // 2)] + [2 * z + 1 for z in reversed(range(count // 2))]


def gather_rows(shard, count, here, rotate):
    if count != 8:
        full = lax.all_gather(shard, "row", axis=0, tiled=True)
        return jnp.roll(full, -rotate * shard.shape[0], axis=0)
    order = snake_order(count)
    position = [0] * count
    for i, d in enumerate(order):
        position[d] = i
    forward = [(order[i], order[(i + 1) % count]) for i in range(count)]
    backward = [(order[i], order[(i - 1) % count]) for i in range(count)]
    half = shard.shape[0] // 2
    ahead, behind = shard[:half], shard[half:]
    ahead_parts, behind_parts = [ahead], [behind]
    for _ in range(count - 1):
        ahead = lax.ppermute(ahead, "row", forward)
        behind = lax.ppermute(behind, "row", backward)
        ahead_parts.append(ahead)
        behind_parts.append(behind)
    table = jnp.array(position, dtype=jnp.int32)
    mine = table[here]
    ahead_stack = jnp.stack(ahead_parts)
    behind_stack = jnp.stack(behind_parts)
    pieces = []
    for j in range(count):
        source = table[(j + rotate) % count]
        pieces.append(lax.dynamic_index_in_dim(ahead_stack, (mine - source) % count, 0, False))
        pieces.append(lax.dynamic_index_in_dim(behind_stack, (source - mine) % count, 0, False))
    return jnp.concatenate(pieces, axis=0)


def shards(
    tokens,
    gain,
    w_query,
    b_query,
    key_weight,
    b_key,
    value_weight,
    value_bias,
    random_block_index,
    global_block_index,
):
    row_count = lax.axis_size("row")
    here = lax.axis_index("row")
    column = lax.axis_index("col")
    group = lax.axis_index("groups")
    passages, length, _ = tokens.shape
    heads_here = w_query.shape[1] // HEAD_SIZE
    pairs_here = key_weight.shape[1] // HEAD_SIZE
    passage_groups = heads_here // pairs_here
    per_device = length // BLOCK_TOKENS
    passage_blocks = row_count * per_device
    scale = 1.0 / math.sqrt(HEAD_SIZE)

    rotary_cols = (heads_here + pairs_here) * HEAD_SIZE
    split = rotary_cols // 2
    value_cols = pairs_here * HEAD_SIZE
    value_split = value_cols // 2
    rotary_w = jnp.concatenate([w_query, key_weight], axis=1)
    rotary_b = jnp.concatenate([b_query, b_key], axis=0)
    first = group == 0
    panel = jnp.where(
        first,
        jnp.concatenate([rotary_w[:, :split], value_weight[:, :value_split]], axis=1),
        jnp.concatenate([rotary_w[:, split:], value_weight[:, value_split:]], axis=1),
    )
    panel_bias = jnp.where(
        first,
        jnp.concatenate([rotary_b[:split], value_bias[:value_split]]),
        jnp.concatenate([rotary_b[split:], value_bias[value_split:]]),
    )
    full_panel = gather_rows(panel, row_count, here, (row_count // 2) * column)

    other_half = lax.ppermute(tokens, "col", SWAP)
    partner_half = lax.ppermute(tokens, "groups", SWAP)
    partner_other = lax.ppermute(partner_half, "col", SWAP)
    both = jnp.concatenate(
        [
            jnp.concatenate([tokens, other_half], axis=2),
            jnp.concatenate([partner_half, partner_other], axis=2),
        ],
        axis=0,
    )
    features = both.shape[2]
    gain_here = jnp.where(
        column == 0,
        gain,
        jnp.concatenate([gain[features // 2 :], gain[: features // 2]]),
    )
    widened = both.astype(jnp.float32)
    power = jnp.mean(widened * widened, axis=-1, keepdims=True)
    normed = (
        (widened * lax.rsqrt(power + norm_eps) * gain_here)
        .astype(jnp.bfloat16)
        .reshape(2 * passages * length, -1)
    )
    token_positions = (here * length + jnp.arange(length, dtype=jnp.int32)).astype(jnp.float32)

    summed = jnp.dot(normed, full_panel, preferred_element_type=jnp.float32) + panel_bias
    summed = summed.reshape(2 * passages, length, split + value_split)
    turned = apply_rotation(
        summed[..., :split].reshape(2 * passages, length, split // HEAD_SIZE, HEAD_SIZE),
        token_positions,
    ).astype(jnp.bfloat16)
    result = jnp.concatenate(
        [turned.reshape(2 * passages, length, split), summed[..., split:].astype(jnp.bfloat16)],
        axis=-1,
    )
    mine = result[:passages]
    returned = lax.ppermute(result[passages:], "groups", SWAP)
    low = jnp.where(first, mine, returned)
    high = jnp.where(first, returned, mine)
    rotary_rows = jnp.concatenate([low[..., :split], high[..., :split]], axis=-1)
    query_rows = rotary_rows[..., : heads_here * HEAD_SIZE]
    key = rotary_rows[..., heads_here * HEAD_SIZE :]
    value_rows = jnp.concatenate([low[..., split:], high[..., split:]], axis=-1)

    pairs = jnp.concatenate([key, value_rows], axis=-1)
    if row_count <= 8:
        by_shift = [pairs] + [
            lax.ppermute(pairs, "row", [(i, (i + k) % row_count) for i in range(row_count)])
            for k in range(1, row_count)
        ]
        gathered = jnp.stack(by_shift)
        owner_slot = (here - jnp.arange(row_count, dtype=jnp.int32)) % row_count
    else:
        gathered = lax.all_gather(pairs, "row", axis=0, tiled=False)
        owner_slot = jnp.arange(row_count, dtype=jnp.int32)
    gathered = gathered.reshape(
        row_count, passages, per_device, BLOCK_TOKENS, pairs_here, 2 * HEAD_SIZE
    )[:, :, :, :, 0]
    gathered = gathered.transpose(1, 0, 2, 3, 4).reshape(
        passages, passage_blocks, BLOCK_TOKENS, 2 * HEAD_SIZE
    )
    block_ids = jnp.arange(passage_blocks, dtype=jnp.int32)
    slot_of_block = owner_slot[block_ids // per_device] * per_device + block_ids % per_device
    kv_blocks = gathered[:, slot_of_block]

    local_blocks = here * per_device + jnp.arange(per_device, dtype=jnp.int32)
    nearby_blocks = local_blocks[:, None] + jnp.arange(3, dtype=jnp.int32)[None, :] - 1
    inside = (nearby_blocks >= 0) & (nearby_blocks < passage_blocks)
    nearby_clamped = jnp.clip(nearby_blocks, 0, passage_blocks - 1)
    passage_ids = jnp.arange(passages, dtype=jnp.int32)
    window = kv_blocks[passage_ids[:, None, None], nearby_clamped[None]]
    window = window.reshape(passages, per_device, 3 * BLOCK_TOKENS, 2 * HEAD_SIZE)

    global_here = lax.dynamic_slice_in_dim(global_block_index, column * pairs_here, pairs_here, 1)
    global_pairs = kv_blocks[passage_ids[:, None], global_here[:, 0, :]]
    global_pairs = global_pairs.reshape(passages, GLOBAL_BLOCKS * BLOCK_TOKENS, 2 * HEAD_SIZE)

    selected = lax.dynamic_slice_in_dim(random_block_index, column * heads_here, heads_here, 2)
    selected = lax.dynamic_slice_in_dim(selected, here * per_device, per_device, 1)
    arrived = kv_blocks[passage_ids[:, None, None, None], selected]
    arrived = arrived.reshape(
        passages, per_device, heads_here, RANDOM_BLOCKS * BLOCK_TOKENS, 2 * HEAD_SIZE
    )

    query_block_rows = query_rows.reshape(
        passages, per_device, BLOCK_TOKENS, heads_here, HEAD_SIZE
    )
    first_scores = jnp.einsum(
        "sqbgh,sqwh->sqgbw",
        query_block_rows,
        window[..., :HEAD_SIZE],
        preferred_element_type=jnp.float32,
    )
    second_scores = jnp.einsum(
        "sqbgh,swh->sqgbw",
        query_block_rows,
        global_pairs[..., :HEAD_SIZE],
        preferred_element_type=jnp.float32,
    )
    third_scores = jnp.einsum(
        "sqbgh,sqgwh->sqgbw",
        query_block_rows,
        arrived[..., :HEAD_SIZE],
        preferred_element_type=jnp.float32,
    )
    first_scores = first_scores * scale
    second_scores = second_scores * scale
    third_scores = third_scores * scale
    near_mask = jnp.repeat(inside, BLOCK_TOKENS, axis=1)
    first_scores = jnp.where(near_mask[None, :, None, None, :], first_scores, -jnp.inf)
    top = jnp.maximum(
        jnp.max(first_scores, axis=-1, keepdims=True),
        jnp.maximum(
            jnp.max(second_scores, axis=-1, keepdims=True),
            jnp.max(third_scores, axis=-1, keepdims=True),
        ),
    )
    near_weights = jnp.exp(first_scores - top)
    global_weights = jnp.exp(second_scores - top)
    random_weights = jnp.exp(third_scores - top)
    total = (
        jnp.sum(near_weights, axis=-1, keepdims=True)
        + jnp.sum(global_weights, axis=-1, keepdims=True)
        + jnp.sum(random_weights, axis=-1, keepdims=True)
    )
    near_probs = (near_weights / total).astype(jnp.bfloat16)
    global_probs = (global_weights / total).astype(jnp.bfloat16)
    random_probs = (random_weights / total).astype(jnp.bfloat16)
    mixed = jnp.einsum(
        "sqgbw,sqwh->sqbgh",
        near_probs,
        window[..., HEAD_SIZE:],
        preferred_element_type=jnp.float32,
    )
    mixed = mixed + jnp.einsum(
        "sqgbw,swh->sqbgh",
        global_probs,
        global_pairs[..., HEAD_SIZE:],
        preferred_element_type=jnp.float32,
    )
    mixed = mixed + jnp.einsum(
        "sqgbw,sqgwh->sqbgh",
        random_probs,
        arrived[..., HEAD_SIZE:],
        preferred_element_type=jnp.float32,
    )
    return mixed.reshape(passages, length, heads_here * HEAD_SIZE).astype(jnp.bfloat16)


def solution(mesh):
    placed = (
        P("groups", "row", "col"),
        P(),
        P("row", "col"),
        P("col"),
        P("row", "col"),
        P("col"),
        P("row", "col"),
        P("col"),
        P("groups", None, None, None),
        P("groups", None, None),
    )
    return jax.shard_map(
        shards, mesh=mesh, in_specs=placed, out_specs=P("groups", "row", "col"), check_vma=False
    )
```

```python
import math

import jax
import jax.numpy as jnp
from jax import lax
from jax.sharding import PartitionSpec as P

HEAD_SIZE = 128
BLOCK_TOKENS = 64
RANDOM_BLOCKS = 2
GLOBAL_BLOCKS = 2


rope_base = 1000000.0
norm_eps = 1e-06

SWAP = [(0, 1), (1, 0)]


def apply_rotation(values, token_positions):
    half = values.shape[-1] // 2
    freqs = 1.0 / rope_base ** (jnp.arange(half, dtype=jnp.float32) * 2.0 / values.shape[-1])
    angles = token_positions[:, None] * freqs[None, :]
    cosine = jnp.concatenate([jnp.cos(angles), jnp.cos(angles)], axis=-1)[None, :, None, :]
    sine = jnp.concatenate([jnp.sin(angles), jnp.sin(angles)], axis=-1)[None, :, None, :]
    turned = jnp.concatenate([-values[..., half:], values[..., :half]], axis=-1)
    return values * cosine + turned * sine


def snake_order(count):
    return [2 * z for z in range(count // 2)] + [2 * z + 1 for z in reversed(range(count // 2))]


def gather_rows(shard, count, here):
    if count != 8:
        return lax.all_gather(shard, "row", axis=0, tiled=True)
    order = snake_order(count)
    position = [0] * count
    for i, d in enumerate(order):
        position[d] = i
    forward = [(order[i], order[(i + 1) % count]) for i in range(count)]
    backward = [(order[i], order[(i - 1) % count]) for i in range(count)]
    half = shard.shape[0] // 2
    ahead, behind = shard[:half], shard[half:]
    ahead_parts, behind_parts = [ahead], [behind]
    for _ in range(count - 1):
        ahead = lax.ppermute(ahead, "row", forward)
        behind = lax.ppermute(behind, "row", backward)
        ahead_parts.append(ahead)
        behind_parts.append(behind)
    table = jnp.array(position, dtype=jnp.int32)
    mine = table[here]
    ahead_pick = (mine - table) % count
    behind_pick = (table - mine) % count
    joined = jnp.concatenate(
        [jnp.stack(ahead_parts)[ahead_pick], jnp.stack(behind_parts)[behind_pick]], axis=1
    )
    return joined.reshape(count * shard.shape[0], shard.shape[1])


def shards(
    tokens,
    gain,
    w_query,
    b_query,
    key_weight,
    b_key,
    value_weight,
    value_bias,
    random_block_index,
    global_block_index,
):
    row_count = lax.axis_size("row")
    here = lax.axis_index("row")
    column = lax.axis_index("col")
    group = lax.axis_index("groups")
    passages, length, _ = tokens.shape
    heads_here = w_query.shape[1] // HEAD_SIZE
    pairs_here = key_weight.shape[1] // HEAD_SIZE
    passage_groups = heads_here // pairs_here
    per_device = length // BLOCK_TOKENS
    passage_blocks = row_count * per_device
    scale = 1.0 / math.sqrt(HEAD_SIZE)

    rotary_cols = (heads_here + pairs_here) * HEAD_SIZE
    split = rotary_cols // 2
    value_cols = pairs_here * HEAD_SIZE
    value_split = value_cols // 2
    rotary_w = jnp.concatenate([w_query, key_weight], axis=1)
    rotary_b = jnp.concatenate([b_query, b_key], axis=0)
    first = group == 0
    panel = jnp.where(
        first,
        jnp.concatenate([rotary_w[:, :split], value_weight[:, :value_split]], axis=1),
        jnp.concatenate([rotary_w[:, split:], value_weight[:, value_split:]], axis=1),
    )
    panel_bias = jnp.where(
        first,
        jnp.concatenate([rotary_b[:split], value_bias[:value_split]]),
        jnp.concatenate([rotary_b[split:], value_bias[value_split:]]),
    )
    full_panel = gather_rows(panel, row_count, here)

    other_half = lax.ppermute(tokens, "col", SWAP)
    partner_half = lax.ppermute(tokens, "groups", SWAP)
    partner_other = lax.ppermute(partner_half, "col", SWAP)
    whole = jnp.where(
        column == 0,
        jnp.concatenate([tokens, other_half], axis=2),
        jnp.concatenate([other_half, tokens], axis=2),
    )
    partner = jnp.where(
        column == 0,
        jnp.concatenate([partner_half, partner_other], axis=2),
        jnp.concatenate([partner_other, partner_half], axis=2),
    )
    token_positions = (here * length + jnp.arange(length, dtype=jnp.int32)).astype(jnp.float32)

    def project(rows):
        widened = rows.astype(jnp.float32)
        power = jnp.mean(widened * widened, axis=-1, keepdims=True)
        normed = (
            (widened * lax.rsqrt(power + norm_eps) * gain)
            .astype(jnp.bfloat16)
            .reshape(passages * length, -1)
        )
        summed = jnp.dot(normed, full_panel, preferred_element_type=jnp.float32) + panel_bias
        summed = summed.reshape(passages, length, split + value_split)
        turned = apply_rotation(
            summed[..., :split].reshape(passages, length, split // HEAD_SIZE, HEAD_SIZE),
            token_positions,
        ).astype(jnp.bfloat16)
        return jnp.concatenate(
            [turned.reshape(passages, length, split), summed[..., split:].astype(jnp.bfloat16)],
            axis=-1,
        )

    returned = lax.ppermute(project(partner), "groups", SWAP)
    mine = project(whole)
    low = jnp.where(first, mine, returned)
    high = jnp.where(first, returned, mine)
    rotary_rows = jnp.concatenate([low[..., :split], high[..., :split]], axis=-1)
    query_rows = rotary_rows[..., : heads_here * HEAD_SIZE]
    key = rotary_rows[..., heads_here * HEAD_SIZE :]
    value_rows = jnp.concatenate([low[..., split:], high[..., split:]], axis=-1)

    pairs = jnp.concatenate([key, value_rows], axis=-1)
    if row_count <= 8:
        by_shift = [pairs] + [
            lax.ppermute(pairs, "row", [(i, (i + k) % row_count) for i in range(row_count)])
            for k in range(1, row_count)
        ]
        gathered = jnp.stack(by_shift)
        owner_slot = (here - jnp.arange(row_count, dtype=jnp.int32)) % row_count
    else:
        gathered = lax.all_gather(pairs, "row", axis=0, tiled=False)
        owner_slot = jnp.arange(row_count, dtype=jnp.int32)
    gathered = gathered.reshape(
        row_count, passages, per_device, BLOCK_TOKENS, pairs_here, 2 * HEAD_SIZE
    )[:, :, :, :, 0]
    gathered = gathered.transpose(1, 0, 2, 3, 4).reshape(
        passages, passage_blocks, BLOCK_TOKENS, 2 * HEAD_SIZE
    )
    block_ids = jnp.arange(passage_blocks, dtype=jnp.int32)
    slot_of_block = owner_slot[block_ids // per_device] * per_device + block_ids % per_device
    kv_blocks = gathered[:, slot_of_block]

    local_blocks = here * per_device + jnp.arange(per_device, dtype=jnp.int32)
    nearby_blocks = local_blocks[:, None] + jnp.arange(3, dtype=jnp.int32)[None, :] - 1
    inside = (nearby_blocks >= 0) & (nearby_blocks < passage_blocks)
    nearby_clamped = jnp.clip(nearby_blocks, 0, passage_blocks - 1)
    passage_ids = jnp.arange(passages, dtype=jnp.int32)
    window = kv_blocks[passage_ids[:, None, None], nearby_clamped[None]]
    window = window.reshape(passages, per_device, 3 * BLOCK_TOKENS, 2 * HEAD_SIZE)

    global_here = lax.dynamic_slice_in_dim(global_block_index, column * pairs_here, pairs_here, 1)
    global_pairs = kv_blocks[passage_ids[:, None], global_here[:, 0, :]]
    global_pairs = global_pairs.reshape(passages, GLOBAL_BLOCKS * BLOCK_TOKENS, 2 * HEAD_SIZE)

    selected = lax.dynamic_slice_in_dim(random_block_index, column * heads_here, heads_here, 2)
    selected = lax.dynamic_slice_in_dim(selected, here * per_device, per_device, 1)
    arrived = kv_blocks[passage_ids[:, None, None, None], selected]
    arrived = arrived.reshape(
        passages, per_device, heads_here, RANDOM_BLOCKS * BLOCK_TOKENS, 2 * HEAD_SIZE
    )

    query_block_rows = query_rows.reshape(
        passages, per_device, BLOCK_TOKENS, heads_here, HEAD_SIZE
    )
    first_scores = jnp.einsum(
        "sqbgh,sqwh->sqgbw",
        query_block_rows,
        window[..., :HEAD_SIZE],
        preferred_element_type=jnp.float32,
    )
    second_scores = jnp.einsum(
        "sqbgh,swh->sqgbw",
        query_block_rows,
        global_pairs[..., :HEAD_SIZE],
        preferred_element_type=jnp.float32,
    )
    third_scores = jnp.einsum(
        "sqbgh,sqgwh->sqgbw",
        query_block_rows,
        arrived[..., :HEAD_SIZE],
        preferred_element_type=jnp.float32,
    )
    first_scores = first_scores * scale
    second_scores = second_scores * scale
    third_scores = third_scores * scale
    near_mask = jnp.repeat(inside, BLOCK_TOKENS, axis=1)
    first_scores = jnp.where(near_mask[None, :, None, None, :], first_scores, -jnp.inf)
    top = jnp.maximum(
        jnp.max(first_scores, axis=-1, keepdims=True),
        jnp.maximum(
            jnp.max(second_scores, axis=-1, keepdims=True),
            jnp.max(third_scores, axis=-1, keepdims=True),
        ),
    )
    near_weights = jnp.exp(first_scores - top)
    global_weights = jnp.exp(second_scores - top)
    random_weights = jnp.exp(third_scores - top)
    total = (
        jnp.sum(near_weights, axis=-1, keepdims=True)
        + jnp.sum(global_weights, axis=-1, keepdims=True)
        + jnp.sum(random_weights, axis=-1, keepdims=True)
    )
    near_probs = (near_weights / total).astype(jnp.bfloat16)
    global_probs = (global_weights / total).astype(jnp.bfloat16)
    random_probs = (random_weights / total).astype(jnp.bfloat16)
    mixed = jnp.einsum(
        "sqgbw,sqwh->sqbgh",
        near_probs,
        window[..., HEAD_SIZE:],
        preferred_element_type=jnp.float32,
    )
    mixed = mixed + jnp.einsum(
        "sqgbw,swh->sqbgh",
        global_probs,
        global_pairs[..., HEAD_SIZE:],
        preferred_element_type=jnp.float32,
    )
    mixed = mixed + jnp.einsum(
        "sqgbw,sqgwh->sqbgh",
        random_probs,
        arrived[..., HEAD_SIZE:],
        preferred_element_type=jnp.float32,
    )
    return mixed.reshape(passages, length, heads_here * HEAD_SIZE).astype(jnp.bfloat16)


def solution(mesh):
    placed = (
        P("groups", "row", "col"),
        P(),
        P("row", "col"),
        P("col"),
        P("row", "col"),
        P("col"),
        P("row", "col"),
        P("col"),
        P("groups", None, None, None),
        P("groups", None, None),
    )
    return jax.shard_map(
        shards, mesh=mesh, in_specs=placed, out_specs=P("groups", "row", "col"), check_vma=False
    )
```

```python
import math

import jax
import jax.numpy as jnp
from jax import lax
from jax.sharding import PartitionSpec as P

HEAD_SIZE = 128
BLOCK_TOKENS = 64
RANDOM_BLOCKS = 2
GLOBAL_BLOCKS = 2


rope_base = 1000000.0
norm_eps = 1e-06

SWAP = [(0, 1), (1, 0)]


def apply_rotation(values, token_positions):
    half = values.shape[-1] // 2
    freqs = 1.0 / rope_base ** (jnp.arange(half, dtype=jnp.float32) * 2.0 / values.shape[-1])
    angles = token_positions[:, None] * freqs[None, :]
    cosine = jnp.concatenate([jnp.cos(angles), jnp.cos(angles)], axis=-1)[None, :, None, :]
    sine = jnp.concatenate([jnp.sin(angles), jnp.sin(angles)], axis=-1)[None, :, None, :]
    turned = jnp.concatenate([-values[..., half:], values[..., :half]], axis=-1)
    return values * cosine + turned * sine


def snake_order(count):
    return [2 * z for z in range(count // 2)] + [2 * z + 1 for z in reversed(range(count // 2))]


def gather_rows(shard, count, here, tie=None, tie_step=0):
    if count != 8:
        return lax.all_gather(shard, "row", axis=0, tiled=True), tie
    order = snake_order(count)
    position = [0] * count
    for i, d in enumerate(order):
        position[d] = i
    forward = [(order[i], order[(i + 1) % count]) for i in range(count)]
    backward = [(order[i], order[(i - 1) % count]) for i in range(count)]
    half = shard.shape[0] // 2
    ahead, behind = shard[:half], shard[half:]
    ahead_parts, behind_parts = [ahead], [behind]
    for step in range(1, count):
        if step == tie_step:
            ahead, tie = lax.optimization_barrier((ahead, tie))
        ahead = lax.ppermute(ahead, "row", forward)
        behind = lax.ppermute(behind, "row", backward)
        ahead_parts.append(ahead)
        behind_parts.append(behind)
    table = jnp.array(position, dtype=jnp.int32)
    mine = table[here]
    ahead_pick = (mine - table) % count
    behind_pick = (table - mine) % count
    joined = jnp.concatenate(
        [jnp.stack(ahead_parts)[ahead_pick], jnp.stack(behind_parts)[behind_pick]], axis=1
    )
    return joined.reshape(count * shard.shape[0], shard.shape[1]), tie


def shards(
    tokens,
    gain,
    w_query,
    b_query,
    key_weight,
    b_key,
    value_weight,
    value_bias,
    random_block_index,
    global_block_index,
):
    row_count = lax.axis_size("row")
    here = lax.axis_index("row")
    column = lax.axis_index("col")
    group = lax.axis_index("groups")
    passages, length, _ = tokens.shape
    heads_here = w_query.shape[1] // HEAD_SIZE
    pairs_here = key_weight.shape[1] // HEAD_SIZE
    passage_groups = heads_here // pairs_here
    per_device = length // BLOCK_TOKENS
    passage_blocks = row_count * per_device
    scale = 1.0 / math.sqrt(HEAD_SIZE)

    rotary_cols = (heads_here + pairs_here) * HEAD_SIZE
    split = rotary_cols // 2
    value_cols = pairs_here * HEAD_SIZE
    value_split = value_cols // 2
    rotary_w = jnp.concatenate([w_query, key_weight], axis=1)
    rotary_b = jnp.concatenate([b_query, b_key], axis=0)
    first = group == 0
    panel = jnp.where(
        first,
        jnp.concatenate([rotary_w[:, :split], value_weight[:, :value_split]], axis=1),
        jnp.concatenate([rotary_w[:, split:], value_weight[:, value_split:]], axis=1),
    )
    panel_bias = jnp.where(
        first,
        jnp.concatenate([rotary_b[:split], value_bias[:value_split]]),
        jnp.concatenate([rotary_b[split:], value_bias[value_split:]]),
    )

    other_half = lax.ppermute(tokens, "col", SWAP)
    partner_half = lax.ppermute(tokens, "groups", SWAP)
    partner_other = lax.ppermute(partner_half, "col", SWAP)
    whole = jnp.where(
        column == 0,
        jnp.concatenate([tokens, other_half], axis=2),
        jnp.concatenate([other_half, tokens], axis=2),
    )
    partner = jnp.where(
        column == 0,
        jnp.concatenate([partner_half, partner_other], axis=2),
        jnp.concatenate([partner_other, partner_half], axis=2),
    )
    both = jnp.concatenate([whole, partner], axis=0)
    widened = both.astype(jnp.float32)
    power = jnp.mean(widened * widened, axis=-1, keepdims=True)
    normed = (
        (widened * lax.rsqrt(power + norm_eps) * gain)
        .astype(jnp.bfloat16)
        .reshape(2 * passages * length, -1)
    )
    token_positions = (here * length + jnp.arange(length, dtype=jnp.int32)).astype(jnp.float32)

    full_panel, normed = gather_rows(panel, row_count, here, normed, 6)
    summed = jnp.dot(normed, full_panel, preferred_element_type=jnp.float32) + panel_bias
    summed = summed.reshape(2 * passages, length, split + value_split)
    turned = apply_rotation(
        summed[..., :split].reshape(2 * passages, length, split // HEAD_SIZE, HEAD_SIZE),
        token_positions,
    ).astype(jnp.bfloat16)
    result = jnp.concatenate(
        [turned.reshape(2 * passages, length, split), summed[..., split:].astype(jnp.bfloat16)],
        axis=-1,
    )
    mine = result[:passages]
    returned = lax.ppermute(result[passages:], "groups", SWAP)
    low = jnp.where(first, mine, returned)
    high = jnp.where(first, returned, mine)
    rotary_rows = jnp.concatenate([low[..., :split], high[..., :split]], axis=-1)
    query_rows = rotary_rows[..., : heads_here * HEAD_SIZE]
    key = rotary_rows[..., heads_here * HEAD_SIZE :]
    value_rows = jnp.concatenate([low[..., split:], high[..., split:]], axis=-1)

    pairs = jnp.concatenate([key, value_rows], axis=-1)
    if row_count <= 8:
        by_shift = [pairs] + [
            lax.ppermute(pairs, "row", [(i, (i + k) % row_count) for i in range(row_count)])
            for k in range(1, row_count)
        ]
        gathered = jnp.stack(by_shift)
        owner_slot = (here - jnp.arange(row_count, dtype=jnp.int32)) % row_count
    else:
        gathered = lax.all_gather(pairs, "row", axis=0, tiled=False)
        owner_slot = jnp.arange(row_count, dtype=jnp.int32)
    gathered = gathered.reshape(
        row_count, passages, per_device, BLOCK_TOKENS, pairs_here, 2 * HEAD_SIZE
    )[:, :, :, :, 0]
    gathered = gathered.transpose(1, 0, 2, 3, 4).reshape(
        passages, passage_blocks, BLOCK_TOKENS, 2 * HEAD_SIZE
    )
    block_ids = jnp.arange(passage_blocks, dtype=jnp.int32)
    slot_of_block = owner_slot[block_ids // per_device] * per_device + block_ids % per_device
    kv_blocks = gathered[:, slot_of_block]

    local_blocks = here * per_device + jnp.arange(per_device, dtype=jnp.int32)
    nearby_blocks = local_blocks[:, None] + jnp.arange(3, dtype=jnp.int32)[None, :] - 1
    inside = (nearby_blocks >= 0) & (nearby_blocks < passage_blocks)
    nearby_clamped = jnp.clip(nearby_blocks, 0, passage_blocks - 1)
    passage_ids = jnp.arange(passages, dtype=jnp.int32)
    window = kv_blocks[passage_ids[:, None, None], nearby_clamped[None]]
    window = window.reshape(passages, per_device, 3 * BLOCK_TOKENS, 2 * HEAD_SIZE)

    global_here = lax.dynamic_slice_in_dim(global_block_index, column * pairs_here, pairs_here, 1)
    global_pairs = kv_blocks[passage_ids[:, None], global_here[:, 0, :]]
    global_pairs = global_pairs.reshape(passages, GLOBAL_BLOCKS * BLOCK_TOKENS, 2 * HEAD_SIZE)

    selected = lax.dynamic_slice_in_dim(random_block_index, column * heads_here, heads_here, 2)
    selected = lax.dynamic_slice_in_dim(selected, here * per_device, per_device, 1)
    arrived = kv_blocks[passage_ids[:, None, None, None], selected]
    arrived = arrived.reshape(
        passages, per_device, heads_here, RANDOM_BLOCKS * BLOCK_TOKENS, 2 * HEAD_SIZE
    )

    query_block_rows = query_rows.reshape(
        passages, per_device, BLOCK_TOKENS, heads_here, HEAD_SIZE
    )
    first_scores = jnp.einsum(
        "sqbgh,sqwh->sqgbw",
        query_block_rows,
        window[..., :HEAD_SIZE],
        preferred_element_type=jnp.float32,
    )
    second_scores = jnp.einsum(
        "sqbgh,swh->sqgbw",
        query_block_rows,
        global_pairs[..., :HEAD_SIZE],
        preferred_element_type=jnp.float32,
    )
    third_scores = jnp.einsum(
        "sqbgh,sqgwh->sqgbw",
        query_block_rows,
        arrived[..., :HEAD_SIZE],
        preferred_element_type=jnp.float32,
    )
    first_scores = first_scores * scale
    second_scores = second_scores * scale
    third_scores = third_scores * scale
    near_mask = jnp.repeat(inside, BLOCK_TOKENS, axis=1)
    first_scores = jnp.where(near_mask[None, :, None, None, :], first_scores, -jnp.inf)
    top = jnp.maximum(
        jnp.max(first_scores, axis=-1, keepdims=True),
        jnp.maximum(
            jnp.max(second_scores, axis=-1, keepdims=True),
            jnp.max(third_scores, axis=-1, keepdims=True),
        ),
    )
    near_weights = jnp.exp(first_scores - top)
    global_weights = jnp.exp(second_scores - top)
    random_weights = jnp.exp(third_scores - top)
    total = (
        jnp.sum(near_weights, axis=-1, keepdims=True)
        + jnp.sum(global_weights, axis=-1, keepdims=True)
        + jnp.sum(random_weights, axis=-1, keepdims=True)
    )
    near_probs = (near_weights / total).astype(jnp.bfloat16)
    global_probs = (global_weights / total).astype(jnp.bfloat16)
    random_probs = (random_weights / total).astype(jnp.bfloat16)
    mixed = jnp.einsum(
        "sqgbw,sqwh->sqbgh",
        near_probs,
        window[..., HEAD_SIZE:],
        preferred_element_type=jnp.float32,
    )
    mixed = mixed + jnp.einsum(
        "sqgbw,swh->sqbgh",
        global_probs,
        global_pairs[..., HEAD_SIZE:],
        preferred_element_type=jnp.float32,
    )
    mixed = mixed + jnp.einsum(
        "sqgbw,sqgwh->sqbgh",
        random_probs,
        arrived[..., HEAD_SIZE:],
        preferred_element_type=jnp.float32,
    )
    return mixed.reshape(passages, length, heads_here * HEAD_SIZE).astype(jnp.bfloat16)


def solution(mesh):
    placed = (
        P("groups", "row", "col"),
        P(),
        P("row", "col"),
        P("col"),
        P("row", "col"),
        P("col"),
        P("row", "col"),
        P("col"),
        P("groups", None, None, None),
        P("groups", None, None),
    )
    return jax.shard_map(
        shards, mesh=mesh, in_specs=placed, out_specs=P("groups", "row", "col"), check_vma=False
    )
```

```python
import math

import jax
import jax.numpy as jnp
from jax import lax
from jax.sharding import PartitionSpec as P

HEAD_SIZE = 128
BLOCK_TOKENS = 64
RANDOM_BLOCKS = 2
GLOBAL_BLOCKS = 2


rope_base = 1000000.0
norm_eps = 1e-06

SWAP = [(0, 1), (1, 0)]


def apply_rotation(values, token_positions):
    half = values.shape[-1] // 2
    freqs = 1.0 / rope_base ** (jnp.arange(half, dtype=jnp.float32) * 2.0 / values.shape[-1])
    angles = token_positions[:, None] * freqs[None, :]
    cosine = jnp.concatenate([jnp.cos(angles), jnp.cos(angles)], axis=-1)[None, :, None, :]
    sine = jnp.concatenate([jnp.sin(angles), jnp.sin(angles)], axis=-1)[None, :, None, :]
    turned = jnp.concatenate([-values[..., half:], values[..., :half]], axis=-1)
    return values * cosine + turned * sine


def snake_order(count):
    return [2 * z for z in range(count // 2)] + [2 * z + 1 for z in reversed(range(count // 2))]


def gather_rows(shard, count, here):
    if count != 8:
        return lax.all_gather(shard, "row", axis=0, tiled=True)
    order = snake_order(count)
    position = [0] * count
    for i, d in enumerate(order):
        position[d] = i
    forward = [(order[i], order[(i + 1) % count]) for i in range(count)]
    backward = [(order[i], order[(i - 1) % count]) for i in range(count)]
    half = shard.shape[0] // 2
    ahead, behind = shard[:half], shard[half:]
    ahead_parts, behind_parts = [ahead], [behind]
    for _ in range(count - 1):
        ahead = lax.ppermute(ahead, "row", forward)
        behind = lax.ppermute(behind, "row", backward)
        ahead_parts.append(ahead)
        behind_parts.append(behind)
    table = jnp.array(position, dtype=jnp.int32)
    mine = table[here]
    ahead_pick = (mine - table) % count
    behind_pick = (table - mine) % count
    joined = jnp.concatenate(
        [jnp.stack(ahead_parts)[ahead_pick], jnp.stack(behind_parts)[behind_pick]], axis=1
    )
    return joined.reshape(count * shard.shape[0], shard.shape[1])


def shards(
    tokens,
    gain,
    w_query,
    b_query,
    key_weight,
    b_key,
    value_weight,
    value_bias,
    random_block_index,
    global_block_index,
):
    row_count = lax.axis_size("row")
    here = lax.axis_index("row")
    column = lax.axis_index("col")
    group = lax.axis_index("groups")
    passages, length, _ = tokens.shape
    heads_here = w_query.shape[1] // HEAD_SIZE
    pairs_here = key_weight.shape[1] // HEAD_SIZE
    passage_groups = heads_here // pairs_here
    per_device = length // BLOCK_TOKENS
    passage_blocks = row_count * per_device
    scale = 1.0 / math.sqrt(HEAD_SIZE)

    rotary_cols = (heads_here + pairs_here) * HEAD_SIZE
    split = rotary_cols // 2
    value_cols = pairs_here * HEAD_SIZE
    value_split = value_cols // 2
    rotary_w = jnp.concatenate([w_query, key_weight], axis=1)
    rotary_b = jnp.concatenate([b_query, b_key], axis=0)
    first = group == 0
    panel = jnp.where(
        first,
        jnp.concatenate([rotary_w[:, :split], value_weight[:, :value_split]], axis=1),
        jnp.concatenate([rotary_w[:, split:], value_weight[:, value_split:]], axis=1),
    )
    panel_bias = jnp.where(
        first,
        jnp.concatenate([rotary_b[:split], value_bias[:value_split]]),
        jnp.concatenate([rotary_b[split:], value_bias[value_split:]]),
    )
    full_panel = gather_rows(panel, row_count, here)

    other_half = lax.ppermute(tokens, "col", SWAP)
    partner_half = lax.ppermute(tokens, "groups", SWAP)
    partner_other = lax.ppermute(partner_half, "col", SWAP)
    whole = jnp.where(
        column == 0,
        jnp.concatenate([tokens, other_half], axis=2),
        jnp.concatenate([other_half, tokens], axis=2),
    )
    partner = jnp.where(
        column == 0,
        jnp.concatenate([partner_half, partner_other], axis=2),
        jnp.concatenate([partner_other, partner_half], axis=2),
    )
    both = jnp.concatenate([whole, partner], axis=0)
    widened = both.astype(jnp.float32)
    power = jnp.mean(widened * widened, axis=-1, keepdims=True)
    normed = (
        (widened * lax.rsqrt(power + norm_eps) * gain)
        .astype(jnp.bfloat16)
        .reshape(2 * passages * length, -1)
    )
    token_positions = (here * length + jnp.arange(length, dtype=jnp.int32)).astype(jnp.float32)

    summed = jnp.dot(normed, full_panel, preferred_element_type=jnp.float32) + panel_bias
    summed = summed.reshape(2 * passages, length, split + value_split)
    turned = apply_rotation(
        summed[..., :split].reshape(2 * passages, length, split // HEAD_SIZE, HEAD_SIZE),
        token_positions,
    ).astype(jnp.bfloat16)
    result = jnp.concatenate(
        [turned.reshape(2 * passages, length, split), summed[..., split:].astype(jnp.bfloat16)],
        axis=-1,
    )
    mine = result[:passages]
    returned = lax.ppermute(result[passages:], "groups", SWAP)
    low = jnp.where(first, mine, returned)
    high = jnp.where(first, returned, mine)
    rotary_rows = jnp.concatenate([low[..., :split], high[..., :split]], axis=-1)
    query_rows = rotary_rows[..., : heads_here * HEAD_SIZE]
    key = rotary_rows[..., heads_here * HEAD_SIZE :]
    value_rows = jnp.concatenate([low[..., split:], high[..., split:]], axis=-1)

    pairs = jnp.concatenate([key, value_rows], axis=-1)
    if row_count == 8:
        beside = lax.ppermute(pairs, "row", [(i, i ^ 1) for i in range(row_count)])
        couple = jnp.where(
            here % 2 == 0, jnp.stack([pairs, beside]), jnp.stack([beside, pairs])
        )
        lines = row_count // 2
        by_shift = [couple] + [
            lax.ppermute(
                couple, "row", [(i, (i + 2 * k) % row_count) for i in range(row_count)]
            )
            for k in range(1, lines)
        ]
        gathered = jnp.stack(by_shift)
        rows = jnp.arange(row_count, dtype=jnp.int32)
        owner_slot = ((here // 2 - rows // 2) % lines) * 2 + rows % 2
    else:
        gathered = lax.all_gather(pairs, "row", axis=0, tiled=False)
        owner_slot = jnp.arange(row_count, dtype=jnp.int32)
    gathered = gathered.reshape(
        row_count, passages, per_device, BLOCK_TOKENS, pairs_here, 2 * HEAD_SIZE
    )[:, :, :, :, 0]
    gathered = gathered.transpose(1, 0, 2, 3, 4).reshape(
        passages, passage_blocks, BLOCK_TOKENS, 2 * HEAD_SIZE
    )
    block_ids = jnp.arange(passage_blocks, dtype=jnp.int32)
    slot_of_block = owner_slot[block_ids // per_device] * per_device + block_ids % per_device
    kv_blocks = gathered[:, slot_of_block]

    local_blocks = here * per_device + jnp.arange(per_device, dtype=jnp.int32)
    nearby_blocks = local_blocks[:, None] + jnp.arange(3, dtype=jnp.int32)[None, :] - 1
    inside = (nearby_blocks >= 0) & (nearby_blocks < passage_blocks)
    nearby_clamped = jnp.clip(nearby_blocks, 0, passage_blocks - 1)
    passage_ids = jnp.arange(passages, dtype=jnp.int32)
    window = kv_blocks[passage_ids[:, None, None], nearby_clamped[None]]
    window = window.reshape(passages, per_device, 3 * BLOCK_TOKENS, 2 * HEAD_SIZE)

    global_here = lax.dynamic_slice_in_dim(global_block_index, column * pairs_here, pairs_here, 1)
    global_pairs = kv_blocks[passage_ids[:, None], global_here[:, 0, :]]
    global_pairs = global_pairs.reshape(passages, GLOBAL_BLOCKS * BLOCK_TOKENS, 2 * HEAD_SIZE)

    selected = lax.dynamic_slice_in_dim(random_block_index, column * heads_here, heads_here, 2)
    selected = lax.dynamic_slice_in_dim(selected, here * per_device, per_device, 1)
    arrived = kv_blocks[passage_ids[:, None, None, None], selected]
    arrived = arrived.reshape(
        passages, per_device, heads_here, RANDOM_BLOCKS * BLOCK_TOKENS, 2 * HEAD_SIZE
    )

    query_block_rows = query_rows.reshape(
        passages, per_device, BLOCK_TOKENS, heads_here, HEAD_SIZE
    )
    first_scores = jnp.einsum(
        "sqbgh,sqwh->sqgbw",
        query_block_rows,
        window[..., :HEAD_SIZE],
        preferred_element_type=jnp.float32,
    )
    second_scores = jnp.einsum(
        "sqbgh,swh->sqgbw",
        query_block_rows,
        global_pairs[..., :HEAD_SIZE],
        preferred_element_type=jnp.float32,
    )
    third_scores = jnp.einsum(
        "sqbgh,sqgwh->sqgbw",
        query_block_rows,
        arrived[..., :HEAD_SIZE],
        preferred_element_type=jnp.float32,
    )
    first_scores = first_scores * scale
    second_scores = second_scores * scale
    third_scores = third_scores * scale
    near_mask = jnp.repeat(inside, BLOCK_TOKENS, axis=1)
    first_scores = jnp.where(near_mask[None, :, None, None, :], first_scores, -jnp.inf)
    top = jnp.maximum(
        jnp.max(first_scores, axis=-1, keepdims=True),
        jnp.maximum(
            jnp.max(second_scores, axis=-1, keepdims=True),
            jnp.max(third_scores, axis=-1, keepdims=True),
        ),
    )
    near_weights = jnp.exp(first_scores - top)
    global_weights = jnp.exp(second_scores - top)
    random_weights = jnp.exp(third_scores - top)
    total = (
        jnp.sum(near_weights, axis=-1, keepdims=True)
        + jnp.sum(global_weights, axis=-1, keepdims=True)
        + jnp.sum(random_weights, axis=-1, keepdims=True)
    )
    near_probs = (near_weights / total).astype(jnp.bfloat16)
    global_probs = (global_weights / total).astype(jnp.bfloat16)
    random_probs = (random_weights / total).astype(jnp.bfloat16)
    mixed = jnp.einsum(
        "sqgbw,sqwh->sqbgh",
        near_probs,
        window[..., HEAD_SIZE:],
        preferred_element_type=jnp.float32,
    )
    mixed = mixed + jnp.einsum(
        "sqgbw,swh->sqbgh",
        global_probs,
        global_pairs[..., HEAD_SIZE:],
        preferred_element_type=jnp.float32,
    )
    mixed = mixed + jnp.einsum(
        "sqgbw,sqgwh->sqbgh",
        random_probs,
        arrived[..., HEAD_SIZE:],
        preferred_element_type=jnp.float32,
    )
    return mixed.reshape(passages, length, heads_here * HEAD_SIZE).astype(jnp.bfloat16)


def solution(mesh):
    placed = (
        P("groups", "row", "col"),
        P(),
        P("row", "col"),
        P("col"),
        P("row", "col"),
        P("col"),
        P("row", "col"),
        P("col"),
        P("groups", None, None, None),
        P("groups", None, None),
    )
    return jax.shard_map(
        shards, mesh=mesh, in_specs=placed, out_specs=P("groups", "row", "col"), check_vma=False
    )
```

```python
import math

import jax
import jax.numpy as jnp
from jax import lax
from jax.sharding import PartitionSpec as P

HEAD_SIZE = 128
BLOCK_TOKENS = 64
RANDOM_BLOCKS = 2
GLOBAL_BLOCKS = 2


rope_base = 1000000.0
norm_eps = 1e-06

SWAP = [(0, 1), (1, 0)]


def apply_rotation(values, token_positions):
    half = values.shape[-1] // 2
    freqs = 1.0 / rope_base ** (jnp.arange(half, dtype=jnp.float32) * 2.0 / values.shape[-1])
    angles = token_positions[:, None] * freqs[None, :]
    cosine = jnp.concatenate([jnp.cos(angles), jnp.cos(angles)], axis=-1)[None, :, None, :]
    sine = jnp.concatenate([jnp.sin(angles), jnp.sin(angles)], axis=-1)[None, :, None, :]
    turned = jnp.concatenate([-values[..., half:], values[..., :half]], axis=-1)
    return values * cosine + turned * sine


def snake_order(count):
    return [2 * z for z in range(count // 2)] + [2 * z + 1 for z in reversed(range(count // 2))]


def gather_rows(shard, count, here):
    if count != 8:
        return lax.all_gather(shard, "row", axis=0, tiled=True)
    order = snake_order(count)
    position = [0] * count
    for i, d in enumerate(order):
        position[d] = i
    forward = [(order[i], order[(i + 1) % count]) for i in range(count)]
    backward = [(order[i], order[(i - 1) % count]) for i in range(count)]
    half = shard.shape[0] // 2
    ahead, behind = shard[:half], shard[half:]
    ahead_parts, behind_parts = [ahead], [behind]
    for _ in range(count - 1):
        ahead = lax.ppermute(ahead, "row", forward)
        behind = lax.ppermute(behind, "row", backward)
        ahead_parts.append(ahead)
        behind_parts.append(behind)
    table = jnp.array(position, dtype=jnp.int32)
    mine = table[here]
    ahead_pick = (mine - table) % count
    behind_pick = (table - mine) % count
    slots = jnp.arange(count, dtype=jnp.int32)

    def reorder(parts, pick):
        stacked = jnp.stack(parts).reshape(count, -1)
        choose = (slots[None, :] == pick[:, None]).astype(stacked.dtype)
        moved = jnp.dot(choose, stacked, preferred_element_type=stacked.dtype)
        return moved.reshape(count, half, shard.shape[1])

    joined = jnp.concatenate(
        [reorder(ahead_parts, ahead_pick), reorder(behind_parts, behind_pick)], axis=1
    )
    return joined.reshape(count * shard.shape[0], shard.shape[1])


def shards(
    tokens,
    gain,
    w_query,
    b_query,
    key_weight,
    b_key,
    value_weight,
    value_bias,
    random_block_index,
    global_block_index,
):
    row_count = lax.axis_size("row")
    here = lax.axis_index("row")
    column = lax.axis_index("col")
    group = lax.axis_index("groups")
    passages, length, _ = tokens.shape
    heads_here = w_query.shape[1] // HEAD_SIZE
    pairs_here = key_weight.shape[1] // HEAD_SIZE
    passage_groups = heads_here // pairs_here
    per_device = length // BLOCK_TOKENS
    passage_blocks = row_count * per_device
    scale = 1.0 / math.sqrt(HEAD_SIZE)

    rotary_cols = (heads_here + pairs_here) * HEAD_SIZE
    split = rotary_cols // 2
    value_cols = pairs_here * HEAD_SIZE
    value_split = value_cols // 2
    rotary_w = jnp.concatenate([w_query, key_weight], axis=1)
    rotary_b = jnp.concatenate([b_query, b_key], axis=0)
    first = group == 0
    panel = jnp.where(
        first,
        jnp.concatenate([rotary_w[:, :split], value_weight[:, :value_split]], axis=1),
        jnp.concatenate([rotary_w[:, split:], value_weight[:, value_split:]], axis=1),
    )
    panel_bias = jnp.where(
        first,
        jnp.concatenate([rotary_b[:split], value_bias[:value_split]]),
        jnp.concatenate([rotary_b[split:], value_bias[value_split:]]),
    )
    full_panel = gather_rows(panel, row_count, here)

    other_half = lax.ppermute(tokens, "col", SWAP)
    partner_half = lax.ppermute(tokens, "groups", SWAP)
    partner_other = lax.ppermute(partner_half, "col", SWAP)
    whole = jnp.where(
        column == 0,
        jnp.concatenate([tokens, other_half], axis=2),
        jnp.concatenate([other_half, tokens], axis=2),
    )
    partner = jnp.where(
        column == 0,
        jnp.concatenate([partner_half, partner_other], axis=2),
        jnp.concatenate([partner_other, partner_half], axis=2),
    )
    both = jnp.concatenate([whole, partner], axis=0)
    widened = both.astype(jnp.float32)
    power = jnp.mean(widened * widened, axis=-1, keepdims=True)
    normed = (
        (widened * lax.rsqrt(power + norm_eps) * gain)
        .astype(jnp.bfloat16)
        .reshape(2 * passages * length, -1)
    )
    token_positions = (here * length + jnp.arange(length, dtype=jnp.int32)).astype(jnp.float32)

    summed = jnp.dot(normed, full_panel, preferred_element_type=jnp.float32) + panel_bias
    summed = summed.reshape(2 * passages, length, split + value_split)
    turned = apply_rotation(
        summed[..., :split].reshape(2 * passages, length, split // HEAD_SIZE, HEAD_SIZE),
        token_positions,
    ).astype(jnp.bfloat16)
    result = jnp.concatenate(
        [turned.reshape(2 * passages, length, split), summed[..., split:].astype(jnp.bfloat16)],
        axis=-1,
    )
    mine = result[:passages]
    returned = lax.ppermute(result[passages:], "groups", SWAP)
    low = jnp.where(first, mine, returned)
    high = jnp.where(first, returned, mine)
    rotary_rows = jnp.concatenate([low[..., :split], high[..., :split]], axis=-1)
    query_rows = rotary_rows[..., : heads_here * HEAD_SIZE]
    key = rotary_rows[..., heads_here * HEAD_SIZE :]
    value_rows = jnp.concatenate([low[..., split:], high[..., split:]], axis=-1)

    pairs = jnp.concatenate([key, value_rows], axis=-1)
    if row_count <= 8:
        by_shift = [pairs] + [
            lax.ppermute(pairs, "row", [(i, (i + k) % row_count) for i in range(row_count)])
            for k in range(1, row_count)
        ]
        gathered = jnp.stack(by_shift)
        owner_slot = (here - jnp.arange(row_count, dtype=jnp.int32)) % row_count
    else:
        gathered = lax.all_gather(pairs, "row", axis=0, tiled=False)
        owner_slot = jnp.arange(row_count, dtype=jnp.int32)
    gathered = gathered.reshape(
        row_count, passages, per_device, BLOCK_TOKENS, pairs_here, 2 * HEAD_SIZE
    )[:, :, :, :, 0]
    gathered = gathered.transpose(1, 0, 2, 3, 4).reshape(
        passages, passage_blocks, BLOCK_TOKENS, 2 * HEAD_SIZE
    )
    block_ids = jnp.arange(passage_blocks, dtype=jnp.int32)
    slot_of_block = owner_slot[block_ids // per_device] * per_device + block_ids % per_device
    kv_blocks = gathered[:, slot_of_block]

    local_blocks = here * per_device + jnp.arange(per_device, dtype=jnp.int32)
    nearby_blocks = local_blocks[:, None] + jnp.arange(3, dtype=jnp.int32)[None, :] - 1
    inside = (nearby_blocks >= 0) & (nearby_blocks < passage_blocks)
    nearby_clamped = jnp.clip(nearby_blocks, 0, passage_blocks - 1)
    passage_ids = jnp.arange(passages, dtype=jnp.int32)
    window = kv_blocks[passage_ids[:, None, None], nearby_clamped[None]]
    window = window.reshape(passages, per_device, 3 * BLOCK_TOKENS, 2 * HEAD_SIZE)

    global_here = lax.dynamic_slice_in_dim(global_block_index, column * pairs_here, pairs_here, 1)
    global_pairs = kv_blocks[passage_ids[:, None], global_here[:, 0, :]]
    global_pairs = global_pairs.reshape(passages, GLOBAL_BLOCKS * BLOCK_TOKENS, 2 * HEAD_SIZE)

    selected = lax.dynamic_slice_in_dim(random_block_index, column * heads_here, heads_here, 2)
    selected = lax.dynamic_slice_in_dim(selected, here * per_device, per_device, 1)
    arrived = kv_blocks[passage_ids[:, None, None, None], selected]
    arrived = arrived.reshape(
        passages, per_device, heads_here, RANDOM_BLOCKS * BLOCK_TOKENS, 2 * HEAD_SIZE
    )

    query_block_rows = query_rows.reshape(
        passages, per_device, BLOCK_TOKENS, heads_here, HEAD_SIZE
    )
    first_scores = jnp.einsum(
        "sqbgh,sqwh->sqgbw",
        query_block_rows,
        window[..., :HEAD_SIZE],
        preferred_element_type=jnp.float32,
    )
    second_scores = jnp.einsum(
        "sqbgh,swh->sqgbw",
        query_block_rows,
        global_pairs[..., :HEAD_SIZE],
        preferred_element_type=jnp.float32,
    )
    third_scores = jnp.einsum(
        "sqbgh,sqgwh->sqgbw",
        query_block_rows,
        arrived[..., :HEAD_SIZE],
        preferred_element_type=jnp.float32,
    )
    first_scores = first_scores * scale
    second_scores = second_scores * scale
    third_scores = third_scores * scale
    near_mask = jnp.repeat(inside, BLOCK_TOKENS, axis=1)
    first_scores = jnp.where(near_mask[None, :, None, None, :], first_scores, -jnp.inf)
    top = jnp.maximum(
        jnp.max(first_scores, axis=-1, keepdims=True),
        jnp.maximum(
            jnp.max(second_scores, axis=-1, keepdims=True),
            jnp.max(third_scores, axis=-1, keepdims=True),
        ),
    )
    near_weights = jnp.exp(first_scores - top)
    global_weights = jnp.exp(second_scores - top)
    random_weights = jnp.exp(third_scores - top)
    total = (
        jnp.sum(near_weights, axis=-1, keepdims=True)
        + jnp.sum(global_weights, axis=-1, keepdims=True)
        + jnp.sum(random_weights, axis=-1, keepdims=True)
    )
    near_probs = (near_weights / total).astype(jnp.bfloat16)
    global_probs = (global_weights / total).astype(jnp.bfloat16)
    random_probs = (random_weights / total).astype(jnp.bfloat16)
    mixed = jnp.einsum(
        "sqgbw,sqwh->sqbgh",
        near_probs,
        window[..., HEAD_SIZE:],
        preferred_element_type=jnp.float32,
    )
    mixed = mixed + jnp.einsum(
        "sqgbw,swh->sqbgh",
        global_probs,
        global_pairs[..., HEAD_SIZE:],
        preferred_element_type=jnp.float32,
    )
    mixed = mixed + jnp.einsum(
        "sqgbw,sqgwh->sqbgh",
        random_probs,
        arrived[..., HEAD_SIZE:],
        preferred_element_type=jnp.float32,
    )
    return mixed.reshape(passages, length, heads_here * HEAD_SIZE).astype(jnp.bfloat16)


def solution(mesh):
    placed = (
        P("groups", "row", "col"),
        P(),
        P("row", "col"),
        P("col"),
        P("row", "col"),
        P("col"),
        P("row", "col"),
        P("col"),
        P("groups", None, None, None),
        P("groups", None, None),
    )
    return jax.shard_map(
        shards, mesh=mesh, in_specs=placed, out_specs=P("groups", "row", "col"), check_vma=False
    )
```

```python
import math

import jax
import jax.numpy as jnp
from jax import lax
from jax.sharding import PartitionSpec as P

HEAD_SIZE = 128
BLOCK_TOKENS = 64
RANDOM_BLOCKS = 2
GLOBAL_BLOCKS = 2


rope_base = 1000000.0
norm_eps = 1e-06

SWAP = [(0, 1), (1, 0)]


def apply_rotation(values, token_positions):
    half = values.shape[-1] // 2
    freqs = 1.0 / rope_base ** (jnp.arange(half, dtype=jnp.float32) * 2.0 / values.shape[-1])
    angles = token_positions[:, None] * freqs[None, :]
    cosine = jnp.concatenate([jnp.cos(angles), jnp.cos(angles)], axis=-1)[None, :, None, :]
    sine = jnp.concatenate([jnp.sin(angles), jnp.sin(angles)], axis=-1)[None, :, None, :]
    turned = jnp.concatenate([-values[..., half:], values[..., :half]], axis=-1)
    return values * cosine + turned * sine


def snake_order(count):
    return [2 * z for z in range(count // 2)] + [2 * z + 1 for z in reversed(range(count // 2))]


def gather_rows(shard, count, here):
    if count != 8:
        return lax.all_gather(shard, "row", axis=0, tiled=True)
    order = snake_order(count)
    position = [0] * count
    for i, d in enumerate(order):
        position[d] = i
    forward = [(order[i], order[(i + 1) % count]) for i in range(count)]
    backward = [(order[i], order[(i - 1) % count]) for i in range(count)]
    half = shard.shape[0] // 2
    ahead, behind = shard[:half], shard[half:]
    ahead_parts, behind_parts = [ahead], [behind]
    for _ in range(count - 1):
        ahead = lax.ppermute(ahead, "row", forward)
        behind = lax.ppermute(behind, "row", backward)
        ahead_parts.append(ahead)
        behind_parts.append(behind)
    table = jnp.array(position, dtype=jnp.int32)
    mine = table[here]
    ahead_stack, behind_stack = jnp.stack(ahead_parts), jnp.stack(behind_parts)

    def placed(at):
        def build(ahead_stack, behind_stack):
            return jnp.concatenate(
                [
                    jnp.stack([ahead_stack[(at - position[d]) % count] for d in range(count)]),
                    jnp.stack([behind_stack[(position[d] - at) % count] for d in range(count)]),
                ],
                axis=1,
            )

        return build

    joined = lax.switch(mine, [placed(at) for at in range(count)], ahead_stack, behind_stack)
    return joined.reshape(count * shard.shape[0], shard.shape[1])


def shards(
    tokens,
    gain,
    w_query,
    b_query,
    key_weight,
    b_key,
    value_weight,
    value_bias,
    random_block_index,
    global_block_index,
):
    row_count = lax.axis_size("row")
    here = lax.axis_index("row")
    column = lax.axis_index("col")
    group = lax.axis_index("groups")
    passages, length, _ = tokens.shape
    heads_here = w_query.shape[1] // HEAD_SIZE
    pairs_here = key_weight.shape[1] // HEAD_SIZE
    passage_groups = heads_here // pairs_here
    per_device = length // BLOCK_TOKENS
    passage_blocks = row_count * per_device
    scale = 1.0 / math.sqrt(HEAD_SIZE)

    rotary_cols = (heads_here + pairs_here) * HEAD_SIZE
    split = rotary_cols // 2
    value_cols = pairs_here * HEAD_SIZE
    value_split = value_cols // 2
    rotary_w = jnp.concatenate([w_query, key_weight], axis=1)
    rotary_b = jnp.concatenate([b_query, b_key], axis=0)
    first = group == 0
    panel = jnp.where(
        first,
        jnp.concatenate([rotary_w[:, :split], value_weight[:, :value_split]], axis=1),
        jnp.concatenate([rotary_w[:, split:], value_weight[:, value_split:]], axis=1),
    )
    panel_bias = jnp.where(
        first,
        jnp.concatenate([rotary_b[:split], value_bias[:value_split]]),
        jnp.concatenate([rotary_b[split:], value_bias[value_split:]]),
    )
    full_panel = gather_rows(panel, row_count, here)

    other_half = lax.ppermute(tokens, "col", SWAP)
    partner_half = lax.ppermute(tokens, "groups", SWAP)
    partner_other = lax.ppermute(partner_half, "col", SWAP)
    whole = jnp.where(
        column == 0,
        jnp.concatenate([tokens, other_half], axis=2),
        jnp.concatenate([other_half, tokens], axis=2),
    )
    partner = jnp.where(
        column == 0,
        jnp.concatenate([partner_half, partner_other], axis=2),
        jnp.concatenate([partner_other, partner_half], axis=2),
    )
    both = jnp.concatenate([whole, partner], axis=0)
    widened = both.astype(jnp.float32)
    power = jnp.mean(widened * widened, axis=-1, keepdims=True)
    normed = (
        (widened * lax.rsqrt(power + norm_eps) * gain)
        .astype(jnp.bfloat16)
        .reshape(2 * passages * length, -1)
    )
    token_positions = (here * length + jnp.arange(length, dtype=jnp.int32)).astype(jnp.float32)

    summed = jnp.dot(normed, full_panel, preferred_element_type=jnp.float32) + panel_bias
    summed = summed.reshape(2 * passages, length, split + value_split)
    turned = apply_rotation(
        summed[..., :split].reshape(2 * passages, length, split // HEAD_SIZE, HEAD_SIZE),
        token_positions,
    ).astype(jnp.bfloat16)
    result = jnp.concatenate(
        [turned.reshape(2 * passages, length, split), summed[..., split:].astype(jnp.bfloat16)],
        axis=-1,
    )
    mine = result[:passages]
    returned = lax.ppermute(result[passages:], "groups", SWAP)
    low = jnp.where(first, mine, returned)
    high = jnp.where(first, returned, mine)
    rotary_rows = jnp.concatenate([low[..., :split], high[..., :split]], axis=-1)
    query_rows = rotary_rows[..., : heads_here * HEAD_SIZE]
    key = rotary_rows[..., heads_here * HEAD_SIZE :]
    value_rows = jnp.concatenate([low[..., split:], high[..., split:]], axis=-1)

    pairs = jnp.concatenate([key, value_rows], axis=-1)
    if row_count <= 8:
        by_shift = [pairs] + [
            lax.ppermute(pairs, "row", [(i, (i + k) % row_count) for i in range(row_count)])
            for k in range(1, row_count)
        ]
        gathered = jnp.stack(by_shift)
        owner_slot = (here - jnp.arange(row_count, dtype=jnp.int32)) % row_count
    else:
        gathered = lax.all_gather(pairs, "row", axis=0, tiled=False)
        owner_slot = jnp.arange(row_count, dtype=jnp.int32)
    gathered = gathered.reshape(
        row_count, passages, per_device, BLOCK_TOKENS, pairs_here, 2 * HEAD_SIZE
    )[:, :, :, :, 0]
    gathered = gathered.transpose(1, 0, 2, 3, 4).reshape(
        passages, passage_blocks, BLOCK_TOKENS, 2 * HEAD_SIZE
    )
    block_ids = jnp.arange(passage_blocks, dtype=jnp.int32)
    slot_of_block = owner_slot[block_ids // per_device] * per_device + block_ids % per_device
    kv_blocks = gathered[:, slot_of_block]

    local_blocks = here * per_device + jnp.arange(per_device, dtype=jnp.int32)
    nearby_blocks = local_blocks[:, None] + jnp.arange(3, dtype=jnp.int32)[None, :] - 1
    inside = (nearby_blocks >= 0) & (nearby_blocks < passage_blocks)
    nearby_clamped = jnp.clip(nearby_blocks, 0, passage_blocks - 1)
    passage_ids = jnp.arange(passages, dtype=jnp.int32)
    window = kv_blocks[passage_ids[:, None, None], nearby_clamped[None]]
    window = window.reshape(passages, per_device, 3 * BLOCK_TOKENS, 2 * HEAD_SIZE)

    global_here = lax.dynamic_slice_in_dim(global_block_index, column * pairs_here, pairs_here, 1)
    global_pairs = kv_blocks[passage_ids[:, None], global_here[:, 0, :]]
    global_pairs = global_pairs.reshape(passages, GLOBAL_BLOCKS * BLOCK_TOKENS, 2 * HEAD_SIZE)

    selected = lax.dynamic_slice_in_dim(random_block_index, column * heads_here, heads_here, 2)
    selected = lax.dynamic_slice_in_dim(selected, here * per_device, per_device, 1)
    arrived = kv_blocks[passage_ids[:, None, None, None], selected]
    arrived = arrived.reshape(
        passages, per_device, heads_here, RANDOM_BLOCKS * BLOCK_TOKENS, 2 * HEAD_SIZE
    )

    query_block_rows = query_rows.reshape(
        passages, per_device, BLOCK_TOKENS, heads_here, HEAD_SIZE
    )
    first_scores = jnp.einsum(
        "sqbgh,sqwh->sqgbw",
        query_block_rows,
        window[..., :HEAD_SIZE],
        preferred_element_type=jnp.float32,
    )
    second_scores = jnp.einsum(
        "sqbgh,swh->sqgbw",
        query_block_rows,
        global_pairs[..., :HEAD_SIZE],
        preferred_element_type=jnp.float32,
    )
    third_scores = jnp.einsum(
        "sqbgh,sqgwh->sqgbw",
        query_block_rows,
        arrived[..., :HEAD_SIZE],
        preferred_element_type=jnp.float32,
    )
    first_scores = first_scores * scale
    second_scores = second_scores * scale
    third_scores = third_scores * scale
    near_mask = jnp.repeat(inside, BLOCK_TOKENS, axis=1)
    first_scores = jnp.where(near_mask[None, :, None, None, :], first_scores, -jnp.inf)
    top = jnp.maximum(
        jnp.max(first_scores, axis=-1, keepdims=True),
        jnp.maximum(
            jnp.max(second_scores, axis=-1, keepdims=True),
            jnp.max(third_scores, axis=-1, keepdims=True),
        ),
    )
    near_weights = jnp.exp(first_scores - top)
    global_weights = jnp.exp(second_scores - top)
    random_weights = jnp.exp(third_scores - top)
    total = (
        jnp.sum(near_weights, axis=-1, keepdims=True)
        + jnp.sum(global_weights, axis=-1, keepdims=True)
        + jnp.sum(random_weights, axis=-1, keepdims=True)
    )
    near_probs = (near_weights / total).astype(jnp.bfloat16)
    global_probs = (global_weights / total).astype(jnp.bfloat16)
    random_probs = (random_weights / total).astype(jnp.bfloat16)
    mixed = jnp.einsum(
        "sqgbw,sqwh->sqbgh",
        near_probs,
        window[..., HEAD_SIZE:],
        preferred_element_type=jnp.float32,
    )
    mixed = mixed + jnp.einsum(
        "sqgbw,swh->sqbgh",
        global_probs,
        global_pairs[..., HEAD_SIZE:],
        preferred_element_type=jnp.float32,
    )
    mixed = mixed + jnp.einsum(
        "sqgbw,sqgwh->sqbgh",
        random_probs,
        arrived[..., HEAD_SIZE:],
        preferred_element_type=jnp.float32,
    )
    return mixed.reshape(passages, length, heads_here * HEAD_SIZE).astype(jnp.bfloat16)


def solution(mesh):
    placed = (
        P("groups", "row", "col"),
        P(),
        P("row", "col"),
        P("col"),
        P("row", "col"),
        P("col"),
        P("row", "col"),
        P("col"),
        P("groups", None, None, None),
        P("groups", None, None),
    )
    return jax.shard_map(
        shards, mesh=mesh, in_specs=placed, out_specs=P("groups", "row", "col"), check_vma=False
    )
```

```python
import math

import jax
import jax.numpy as jnp
from jax import lax
from jax.sharding import PartitionSpec as P

HEAD_SIZE = 128
BLOCK_TOKENS = 64
RANDOM_BLOCKS = 2
GLOBAL_BLOCKS = 2


rope_base = 1000000.0
norm_eps = 1e-06

SWAP = [(0, 1), (1, 0)]


def apply_rotation(values, token_positions):
    half = values.shape[-1] // 2
    freqs = 1.0 / rope_base ** (jnp.arange(half, dtype=jnp.float32) * 2.0 / values.shape[-1])
    angles = token_positions[:, None] * freqs[None, :]
    cosine = jnp.concatenate([jnp.cos(angles), jnp.cos(angles)], axis=-1)[None, :, None, :]
    sine = jnp.concatenate([jnp.sin(angles), jnp.sin(angles)], axis=-1)[None, :, None, :]
    turned = jnp.concatenate([-values[..., half:], values[..., :half]], axis=-1)
    return values * cosine + turned * sine


def snake_order(count):
    return [2 * z for z in range(count // 2)] + [2 * z + 1 for z in reversed(range(count // 2))]


def gather_rows(shard, count, here):
    if count != 8:
        return lax.all_gather(shard, "row", axis=0, tiled=True)
    order = snake_order(count)
    position = [0] * count
    for i, d in enumerate(order):
        position[d] = i
    forward = [(order[i], order[(i + 1) % count]) for i in range(count)]
    backward = [(order[i], order[(i - 1) % count]) for i in range(count)]
    half = shard.shape[0] // 2
    ahead, behind = shard[:half], shard[half:]
    ahead_parts, behind_parts = [ahead], [behind]
    for _ in range(count - 1):
        ahead = lax.ppermute(ahead, "row", forward)
        behind = lax.ppermute(behind, "row", backward)
        ahead_parts.append(ahead)
        behind_parts.append(behind)
    table = jnp.array(position, dtype=jnp.int32)
    mine = table[here]
    ahead_pick = (mine - table) % count
    behind_pick = (table - mine) % count
    joined = jnp.concatenate(
        [jnp.stack(ahead_parts)[ahead_pick], jnp.stack(behind_parts)[behind_pick]], axis=1
    )
    return joined.reshape(count * shard.shape[0], shard.shape[1])


def shards(
    tokens,
    gain,
    w_query,
    b_query,
    key_weight,
    b_key,
    value_weight,
    value_bias,
    random_block_index,
    global_block_index,
):
    row_count = lax.axis_size("row")
    here = lax.axis_index("row")
    column = lax.axis_index("col")
    group = lax.axis_index("groups")
    passages, length, _ = tokens.shape
    heads_here = w_query.shape[1] // HEAD_SIZE
    pairs_here = key_weight.shape[1] // HEAD_SIZE
    passage_groups = heads_here // pairs_here
    per_device = length // BLOCK_TOKENS
    passage_blocks = row_count * per_device
    scale = 1.0 / math.sqrt(HEAD_SIZE)

    rotary_cols = (heads_here + pairs_here) * HEAD_SIZE
    split = rotary_cols // 2
    value_cols = pairs_here * HEAD_SIZE
    value_split = value_cols // 2
    rotary_w = jnp.concatenate([w_query, key_weight], axis=1)
    rotary_b = jnp.concatenate([b_query, b_key], axis=0)
    first = group == 0
    panel = jnp.where(
        first,
        jnp.concatenate([rotary_w[:, :split], value_weight[:, :value_split]], axis=1),
        jnp.concatenate([rotary_w[:, split:], value_weight[:, value_split:]], axis=1),
    )
    panel_bias = jnp.where(
        first,
        jnp.concatenate([rotary_b[:split], value_bias[:value_split]]),
        jnp.concatenate([rotary_b[split:], value_bias[value_split:]]),
    )
    full_panel = gather_rows(panel, row_count, here)

    other_half = lax.ppermute(tokens, "col", SWAP)
    partner_half = lax.ppermute(tokens, "groups", SWAP)
    partner_other = lax.ppermute(partner_half, "col", SWAP)
    whole = jnp.where(
        column == 0,
        jnp.concatenate([tokens, other_half], axis=2),
        jnp.concatenate([other_half, tokens], axis=2),
    )
    partner = jnp.where(
        column == 0,
        jnp.concatenate([partner_half, partner_other], axis=2),
        jnp.concatenate([partner_other, partner_half], axis=2),
    )
    both = jnp.concatenate([whole, partner], axis=0)
    widened = both.astype(jnp.float32)
    power = jnp.mean(widened * widened, axis=-1, keepdims=True)
    normed = (
        (widened * lax.rsqrt(power + norm_eps) * gain)
        .astype(jnp.bfloat16)
        .reshape(2 * passages * length, -1)
    )
    token_positions = (here * length + jnp.arange(length, dtype=jnp.int32)).astype(jnp.float32)

    summed = jnp.dot(normed, full_panel, preferred_element_type=jnp.float32) + panel_bias
    summed = summed.reshape(2 * passages, length, split + value_split)
    turned = apply_rotation(
        summed[..., :split].reshape(2 * passages, length, split // HEAD_SIZE, HEAD_SIZE),
        token_positions,
    ).astype(jnp.bfloat16)
    result = jnp.concatenate(
        [turned.reshape(2 * passages, length, split), summed[..., split:].astype(jnp.bfloat16)],
        axis=-1,
    )
    mine = result[:passages]
    returned = lax.ppermute(result[passages:], "groups", SWAP)
    low = jnp.where(first, mine, returned)
    high = jnp.where(first, returned, mine)
    rotary_rows = jnp.concatenate([low[..., :split], high[..., :split]], axis=-1)
    query_rows = rotary_rows[..., : heads_here * HEAD_SIZE]
    key = rotary_rows[..., heads_here * HEAD_SIZE :]
    value_rows = jnp.concatenate([low[..., split:], high[..., split:]], axis=-1)

    pairs = jnp.concatenate([key, value_rows], axis=-1)
    if row_count <= 8:
        spread = jnp.broadcast_to(pairs[None], (row_count,) + pairs.shape)
        gathered = lax.all_to_all(spread, "row", 0, 0, tiled=True)
    else:
        gathered = lax.all_gather(pairs, "row", axis=0, tiled=False)
    owner_slot = jnp.arange(row_count, dtype=jnp.int32)
    gathered = gathered.reshape(
        row_count, passages, per_device, BLOCK_TOKENS, pairs_here, 2 * HEAD_SIZE
    )[:, :, :, :, 0]
    gathered = gathered.transpose(1, 0, 2, 3, 4).reshape(
        passages, passage_blocks, BLOCK_TOKENS, 2 * HEAD_SIZE
    )
    block_ids = jnp.arange(passage_blocks, dtype=jnp.int32)
    slot_of_block = owner_slot[block_ids // per_device] * per_device + block_ids % per_device
    kv_blocks = gathered[:, slot_of_block]

    local_blocks = here * per_device + jnp.arange(per_device, dtype=jnp.int32)
    nearby_blocks = local_blocks[:, None] + jnp.arange(3, dtype=jnp.int32)[None, :] - 1
    inside = (nearby_blocks >= 0) & (nearby_blocks < passage_blocks)
    nearby_clamped = jnp.clip(nearby_blocks, 0, passage_blocks - 1)
    passage_ids = jnp.arange(passages, dtype=jnp.int32)
    window = kv_blocks[passage_ids[:, None, None], nearby_clamped[None]]
    window = window.reshape(passages, per_device, 3 * BLOCK_TOKENS, 2 * HEAD_SIZE)

    global_here = lax.dynamic_slice_in_dim(global_block_index, column * pairs_here, pairs_here, 1)
    global_pairs = kv_blocks[passage_ids[:, None], global_here[:, 0, :]]
    global_pairs = global_pairs.reshape(passages, GLOBAL_BLOCKS * BLOCK_TOKENS, 2 * HEAD_SIZE)

    selected = lax.dynamic_slice_in_dim(random_block_index, column * heads_here, heads_here, 2)
    selected = lax.dynamic_slice_in_dim(selected, here * per_device, per_device, 1)
    arrived = kv_blocks[passage_ids[:, None, None, None], selected]
    arrived = arrived.reshape(
        passages, per_device, heads_here, RANDOM_BLOCKS * BLOCK_TOKENS, 2 * HEAD_SIZE
    )

    query_block_rows = query_rows.reshape(
        passages, per_device, BLOCK_TOKENS, heads_here, HEAD_SIZE
    )
    first_scores = jnp.einsum(
        "sqbgh,sqwh->sqgbw",
        query_block_rows,
        window[..., :HEAD_SIZE],
        preferred_element_type=jnp.float32,
    )
    second_scores = jnp.einsum(
        "sqbgh,swh->sqgbw",
        query_block_rows,
        global_pairs[..., :HEAD_SIZE],
        preferred_element_type=jnp.float32,
    )
    third_scores = jnp.einsum(
        "sqbgh,sqgwh->sqgbw",
        query_block_rows,
        arrived[..., :HEAD_SIZE],
        preferred_element_type=jnp.float32,
    )
    first_scores = first_scores * scale
    second_scores = second_scores * scale
    third_scores = third_scores * scale
    near_mask = jnp.repeat(inside, BLOCK_TOKENS, axis=1)
    first_scores = jnp.where(near_mask[None, :, None, None, :], first_scores, -jnp.inf)
    top = jnp.maximum(
        jnp.max(first_scores, axis=-1, keepdims=True),
        jnp.maximum(
            jnp.max(second_scores, axis=-1, keepdims=True),
            jnp.max(third_scores, axis=-1, keepdims=True),
        ),
    )
    near_weights = jnp.exp(first_scores - top)
    global_weights = jnp.exp(second_scores - top)
    random_weights = jnp.exp(third_scores - top)
    total = (
        jnp.sum(near_weights, axis=-1, keepdims=True)
        + jnp.sum(global_weights, axis=-1, keepdims=True)
        + jnp.sum(random_weights, axis=-1, keepdims=True)
    )
    near_probs = (near_weights / total).astype(jnp.bfloat16)
    global_probs = (global_weights / total).astype(jnp.bfloat16)
    random_probs = (random_weights / total).astype(jnp.bfloat16)
    mixed = jnp.einsum(
        "sqgbw,sqwh->sqbgh",
        near_probs,
        window[..., HEAD_SIZE:],
        preferred_element_type=jnp.float32,
    )
    mixed = mixed + jnp.einsum(
        "sqgbw,swh->sqbgh",
        global_probs,
        global_pairs[..., HEAD_SIZE:],
        preferred_element_type=jnp.float32,
    )
    mixed = mixed + jnp.einsum(
        "sqgbw,sqgwh->sqbgh",
        random_probs,
        arrived[..., HEAD_SIZE:],
        preferred_element_type=jnp.float32,
    )
    return mixed.reshape(passages, length, heads_here * HEAD_SIZE).astype(jnp.bfloat16)


def solution(mesh):
    placed = (
        P("groups", "row", "col"),
        P(),
        P("row", "col"),
        P("col"),
        P("row", "col"),
        P("col"),
        P("row", "col"),
        P("col"),
        P("groups", None, None, None),
        P("groups", None, None),
    )
    return jax.shard_map(
        shards, mesh=mesh, in_specs=placed, out_specs=P("groups", "row", "col"), check_vma=False
    )
```

```python
import math

import jax
import jax.numpy as jnp
from jax import lax
from jax.sharding import PartitionSpec as P

HEAD_SIZE = 128
BLOCK_TOKENS = 64
RANDOM_BLOCKS = 2
GLOBAL_BLOCKS = 2


rope_base = 1000000.0
norm_eps = 1e-06

SWAP = [(0, 1), (1, 0)]


def apply_rotation(values, token_positions):
    half = values.shape[-1] // 2
    freqs = 1.0 / rope_base ** (jnp.arange(half, dtype=jnp.float32) * 2.0 / values.shape[-1])
    angles = token_positions[:, None] * freqs[None, :]
    cosine = jnp.concatenate([jnp.cos(angles), jnp.cos(angles)], axis=-1)[None, :, None, :]
    sine = jnp.concatenate([jnp.sin(angles), jnp.sin(angles)], axis=-1)[None, :, None, :]
    turned = jnp.concatenate([-values[..., half:], values[..., :half]], axis=-1)
    return values * cosine + turned * sine


def snake_order(count):
    return [2 * z for z in range(count // 2)] + [2 * z + 1 for z in reversed(range(count // 2))]


def gather_rows(ahead, behind, count, here):
    if count != 8:
        shard = jnp.concatenate([ahead, behind], axis=0)
        return lax.all_gather(shard, "row", axis=0, tiled=True), ahead
    order = snake_order(count)
    position = [0] * count
    for i, d in enumerate(order):
        position[d] = i
    forward = [(order[i], order[(i + 1) % count]) for i in range(count)]
    backward = [(order[i], order[(i - 1) % count]) for i in range(count)]
    half = ahead.shape[0]
    ahead_parts, behind_parts = [ahead], [behind]
    for _ in range(count - 1):
        ahead = lax.ppermute(ahead, "row", forward)
        behind = lax.ppermute(behind, "row", backward)
        ahead_parts.append(ahead)
        behind_parts.append(behind)
    table = jnp.array(position, dtype=jnp.int32)
    mine = table[here]
    ahead_pick = (mine - table) % count
    behind_pick = (table - mine) % count
    joined = jnp.concatenate(
        [jnp.stack(ahead_parts)[ahead_pick], jnp.stack(behind_parts)[behind_pick]], axis=1
    )
    return joined.reshape(count * 2 * half, ahead.shape[1]), ahead_parts[1]


def shards(
    tokens,
    gain,
    w_query,
    b_query,
    key_weight,
    b_key,
    value_weight,
    value_bias,
    random_block_index,
    global_block_index,
):
    row_count = lax.axis_size("row")
    here = lax.axis_index("row")
    column = lax.axis_index("col")
    group = lax.axis_index("groups")
    passages, length, _ = tokens.shape
    heads_here = w_query.shape[1] // HEAD_SIZE
    pairs_here = key_weight.shape[1] // HEAD_SIZE
    passage_groups = heads_here // pairs_here
    per_device = length // BLOCK_TOKENS
    passage_blocks = row_count * per_device
    scale = 1.0 / math.sqrt(HEAD_SIZE)

    rotary_cols = (heads_here + pairs_here) * HEAD_SIZE
    split = rotary_cols // 2
    value_cols = pairs_here * HEAD_SIZE
    value_split = value_cols // 2
    rotary_w = jnp.concatenate([w_query, key_weight], axis=1)
    rotary_b = jnp.concatenate([b_query, b_key], axis=0)
    first = group == 0
    rows_here = w_query.shape[0]

    def panel_rows(start, stop):
        return jnp.concatenate(
            [
                lax.dynamic_slice_in_dim(rotary_w[start:stop], group * split, split, 1),
                lax.dynamic_slice_in_dim(
                    value_weight[start:stop], group * value_split, value_split, 1
                ),
            ],
            axis=1,
        )

    full_panel, first_arrival = gather_rows(
        panel_rows(0, rows_here // 2),
        panel_rows(rows_here // 2, rows_here),
        row_count,
        here,
    )
    panel_bias = jnp.where(
        first,
        jnp.concatenate([rotary_b[:split], value_bias[:value_split]]),
        jnp.concatenate([rotary_b[split:], value_bias[value_split:]]),
    )

    other_half = lax.ppermute(tokens, "col", SWAP)
    late_tokens, _ = lax.optimization_barrier((tokens, first_arrival))
    partner_half = lax.ppermute(late_tokens, "groups", SWAP)
    partner_other = lax.ppermute(partner_half, "col", SWAP)
    whole = jnp.where(
        column == 0,
        jnp.concatenate([tokens, other_half], axis=2),
        jnp.concatenate([other_half, tokens], axis=2),
    )
    partner = jnp.where(
        column == 0,
        jnp.concatenate([partner_half, partner_other], axis=2),
        jnp.concatenate([partner_other, partner_half], axis=2),
    )
    both = jnp.concatenate([whole, partner], axis=0)
    widened = both.astype(jnp.float32)
    power = jnp.mean(widened * widened, axis=-1, keepdims=True)
    normed = (
        (widened * lax.rsqrt(power + norm_eps) * gain)
        .astype(jnp.bfloat16)
        .reshape(2 * passages * length, -1)
    )
    token_positions = (here * length + jnp.arange(length, dtype=jnp.int32)).astype(jnp.float32)

    summed = jnp.dot(normed, full_panel, preferred_element_type=jnp.float32) + panel_bias
    summed = summed.reshape(2 * passages, length, split + value_split)
    turned = apply_rotation(
        summed[..., :split].reshape(2 * passages, length, split // HEAD_SIZE, HEAD_SIZE),
        token_positions,
    ).astype(jnp.bfloat16)
    result = jnp.concatenate(
        [turned.reshape(2 * passages, length, split), summed[..., split:].astype(jnp.bfloat16)],
        axis=-1,
    )
    mine = result[:passages]
    returned = lax.ppermute(result[passages:], "groups", SWAP)
    low = jnp.where(first, mine, returned)
    high = jnp.where(first, returned, mine)
    rotary_rows = jnp.concatenate([low[..., :split], high[..., :split]], axis=-1)
    query_rows = rotary_rows[..., : heads_here * HEAD_SIZE]
    key = rotary_rows[..., heads_here * HEAD_SIZE :]
    value_rows = jnp.concatenate([low[..., split:], high[..., split:]], axis=-1)

    pairs = jnp.concatenate([key, value_rows], axis=-1)
    if row_count <= 8:
        by_shift = [pairs] + [
            lax.ppermute(pairs, "row", [(i, (i + k) % row_count) for i in range(row_count)])
            for k in range(1, row_count)
        ]
        gathered = jnp.stack(by_shift)
        owner_slot = (here - jnp.arange(row_count, dtype=jnp.int32)) % row_count
    else:
        gathered = lax.all_gather(pairs, "row", axis=0, tiled=False)
        owner_slot = jnp.arange(row_count, dtype=jnp.int32)
    gathered = gathered.reshape(
        row_count, passages, per_device, BLOCK_TOKENS, pairs_here, 2 * HEAD_SIZE
    )[:, :, :, :, 0]
    gathered = gathered.transpose(1, 0, 2, 3, 4).reshape(
        passages, passage_blocks, BLOCK_TOKENS, 2 * HEAD_SIZE
    )
    block_ids = jnp.arange(passage_blocks, dtype=jnp.int32)
    slot_of_block = owner_slot[block_ids // per_device] * per_device + block_ids % per_device
    kv_blocks = gathered[:, slot_of_block]

    local_blocks = here * per_device + jnp.arange(per_device, dtype=jnp.int32)
    nearby_blocks = local_blocks[:, None] + jnp.arange(3, dtype=jnp.int32)[None, :] - 1
    inside = (nearby_blocks >= 0) & (nearby_blocks < passage_blocks)
    nearby_clamped = jnp.clip(nearby_blocks, 0, passage_blocks - 1)
    passage_ids = jnp.arange(passages, dtype=jnp.int32)
    window = kv_blocks[passage_ids[:, None, None], nearby_clamped[None]]
    window = window.reshape(passages, per_device, 3 * BLOCK_TOKENS, 2 * HEAD_SIZE)

    global_here = lax.dynamic_slice_in_dim(global_block_index, column * pairs_here, pairs_here, 1)
    global_pairs = kv_blocks[passage_ids[:, None], global_here[:, 0, :]]
    global_pairs = global_pairs.reshape(passages, GLOBAL_BLOCKS * BLOCK_TOKENS, 2 * HEAD_SIZE)

    selected = lax.dynamic_slice_in_dim(random_block_index, column * heads_here, heads_here, 2)
    selected = lax.dynamic_slice_in_dim(selected, here * per_device, per_device, 1)
    arrived = kv_blocks[passage_ids[:, None, None, None], selected]
    arrived = arrived.reshape(
        passages, per_device, heads_here, RANDOM_BLOCKS * BLOCK_TOKENS, 2 * HEAD_SIZE
    )

    query_block_rows = query_rows.reshape(
        passages, per_device, BLOCK_TOKENS, heads_here, HEAD_SIZE
    )
    first_scores = jnp.einsum(
        "sqbgh,sqwh->sqgbw",
        query_block_rows,
        window[..., :HEAD_SIZE],
        preferred_element_type=jnp.float32,
    )
    second_scores = jnp.einsum(
        "sqbgh,swh->sqgbw",
        query_block_rows,
        global_pairs[..., :HEAD_SIZE],
        preferred_element_type=jnp.float32,
    )
    third_scores = jnp.einsum(
        "sqbgh,sqgwh->sqgbw",
        query_block_rows,
        arrived[..., :HEAD_SIZE],
        preferred_element_type=jnp.float32,
    )
    first_scores = first_scores * scale
    second_scores = second_scores * scale
    third_scores = third_scores * scale
    near_mask = jnp.repeat(inside, BLOCK_TOKENS, axis=1)
    first_scores = jnp.where(near_mask[None, :, None, None, :], first_scores, -jnp.inf)
    top = jnp.maximum(
        jnp.max(first_scores, axis=-1, keepdims=True),
        jnp.maximum(
            jnp.max(second_scores, axis=-1, keepdims=True),
            jnp.max(third_scores, axis=-1, keepdims=True),
        ),
    )
    near_weights = jnp.exp(first_scores - top)
    global_weights = jnp.exp(second_scores - top)
    random_weights = jnp.exp(third_scores - top)
    total = (
        jnp.sum(near_weights, axis=-1, keepdims=True)
        + jnp.sum(global_weights, axis=-1, keepdims=True)
        + jnp.sum(random_weights, axis=-1, keepdims=True)
    )
    near_probs = (near_weights / total).astype(jnp.bfloat16)
    global_probs = (global_weights / total).astype(jnp.bfloat16)
    random_probs = (random_weights / total).astype(jnp.bfloat16)
    mixed = jnp.einsum(
        "sqgbw,sqwh->sqbgh",
        near_probs,
        window[..., HEAD_SIZE:],
        preferred_element_type=jnp.float32,
    )
    mixed = mixed + jnp.einsum(
        "sqgbw,swh->sqbgh",
        global_probs,
        global_pairs[..., HEAD_SIZE:],
        preferred_element_type=jnp.float32,
    )
    mixed = mixed + jnp.einsum(
        "sqgbw,sqgwh->sqbgh",
        random_probs,
        arrived[..., HEAD_SIZE:],
        preferred_element_type=jnp.float32,
    )
    return mixed.reshape(passages, length, heads_here * HEAD_SIZE).astype(jnp.bfloat16)


def solution(mesh):
    placed = (
        P("groups", "row", "col"),
        P(),
        P("row", "col"),
        P("col"),
        P("row", "col"),
        P("col"),
        P("row", "col"),
        P("col"),
        P("groups", None, None, None),
        P("groups", None, None),
    )
    return jax.shard_map(
        shards, mesh=mesh, in_specs=placed, out_specs=P("groups", "row", "col"), check_vma=False
    )
```

```python
import math

import jax
import jax.numpy as jnp
from jax import lax
from jax.sharding import PartitionSpec as P

HEAD_SIZE = 128
BLOCK_TOKENS = 64
RANDOM_BLOCKS = 2
GLOBAL_BLOCKS = 2


rope_base = 1000000.0
norm_eps = 1e-06

SWAP = [(0, 1), (1, 0)]


def apply_rotation(values, token_positions):
    half = values.shape[-1] // 2
    freqs = 1.0 / rope_base ** (jnp.arange(half, dtype=jnp.float32) * 2.0 / values.shape[-1])
    angles = token_positions[:, None] * freqs[None, :]
    cosine = jnp.concatenate([jnp.cos(angles), jnp.cos(angles)], axis=-1)[None, :, None, :]
    sine = jnp.concatenate([jnp.sin(angles), jnp.sin(angles)], axis=-1)[None, :, None, :]
    turned = jnp.concatenate([-values[..., half:], values[..., :half]], axis=-1)
    return values * cosine + turned * sine


def snake_order(count):
    return [2 * z for z in range(count // 2)] + [2 * z + 1 for z in reversed(range(count // 2))]


def gather_rows(ahead, behind, count, here, rotate):
    if count != 8:
        shard = jnp.concatenate([ahead, behind], axis=0)
        full = lax.all_gather(shard, "row", axis=0, tiled=True)
        return jnp.roll(full, -rotate * shard.shape[0], axis=0), ahead
    order = snake_order(count)
    position = [0] * count
    for i, d in enumerate(order):
        position[d] = i
    forward = [(order[i], order[(i + 1) % count]) for i in range(count)]
    backward = [(order[i], order[(i - 1) % count]) for i in range(count)]
    half = ahead.shape[0]
    ahead_parts, behind_parts = [ahead], [behind]
    for _ in range(count - 1):
        ahead = lax.ppermute(ahead, "row", forward)
        behind = lax.ppermute(behind, "row", backward)
        ahead_parts.append(ahead)
        behind_parts.append(behind)
    table = jnp.array(position, dtype=jnp.int32)
    mine = table[here]
    source = table[(jnp.arange(count, dtype=jnp.int32) + rotate) % count]
    ahead_pick = (mine - source) % count
    behind_pick = (source - mine) % count
    joined = jnp.concatenate(
        [jnp.stack(ahead_parts)[ahead_pick], jnp.stack(behind_parts)[behind_pick]], axis=1
    )
    return joined.reshape(count * 2 * half, ahead.shape[1]), ahead_parts[1]


def shards(
    tokens,
    gain,
    w_query,
    b_query,
    key_weight,
    b_key,
    value_weight,
    value_bias,
    random_block_index,
    global_block_index,
):
    row_count = lax.axis_size("row")
    here = lax.axis_index("row")
    column = lax.axis_index("col")
    group = lax.axis_index("groups")
    passages, length, _ = tokens.shape
    heads_here = w_query.shape[1] // HEAD_SIZE
    pairs_here = key_weight.shape[1] // HEAD_SIZE
    passage_groups = heads_here // pairs_here
    per_device = length // BLOCK_TOKENS
    passage_blocks = row_count * per_device
    scale = 1.0 / math.sqrt(HEAD_SIZE)

    rotary_cols = (heads_here + pairs_here) * HEAD_SIZE
    split = rotary_cols // 2
    value_cols = pairs_here * HEAD_SIZE
    value_split = value_cols // 2
    rotary_w = jnp.concatenate([w_query, key_weight], axis=1)
    rotary_b = jnp.concatenate([b_query, b_key], axis=0)
    first = group == 0
    rows_here = w_query.shape[0]

    def panel_rows(start, stop):
        return jnp.concatenate(
            [
                lax.dynamic_slice_in_dim(rotary_w[start:stop], group * split, split, 1),
                lax.dynamic_slice_in_dim(
                    value_weight[start:stop], group * value_split, value_split, 1
                ),
            ],
            axis=1,
        )

    full_panel, first_arrival = gather_rows(
        panel_rows(0, rows_here // 2),
        panel_rows(rows_here // 2, rows_here),
        row_count,
        here,
        (row_count // 2) * column,
    )
    panel_bias = jnp.where(
        first,
        jnp.concatenate([rotary_b[:split], value_bias[:value_split]]),
        jnp.concatenate([rotary_b[split:], value_bias[value_split:]]),
    )

    other_half = lax.ppermute(tokens, "col", SWAP)
    late_tokens, _ = lax.optimization_barrier((tokens, first_arrival))
    partner_half = lax.ppermute(late_tokens, "groups", SWAP)
    partner_other = lax.ppermute(partner_half, "col", SWAP)
    both = jnp.concatenate(
        [
            jnp.concatenate([tokens, other_half], axis=2),
            jnp.concatenate([partner_half, partner_other], axis=2),
        ],
        axis=0,
    )
    features = both.shape[2]
    gain_here = jnp.where(
        column == 0,
        gain,
        jnp.concatenate([gain[features // 2 :], gain[: features // 2]]),
    )
    widened = both.astype(jnp.float32)
    power = jnp.mean(widened * widened, axis=-1, keepdims=True)
    normed = (
        (widened * lax.rsqrt(power + norm_eps) * gain_here)
        .astype(jnp.bfloat16)
        .reshape(2 * passages * length, -1)
    )
    token_positions = (here * length + jnp.arange(length, dtype=jnp.int32)).astype(jnp.float32)

    summed = jnp.dot(normed, full_panel, preferred_element_type=jnp.float32) + panel_bias
    summed = summed.reshape(2 * passages, length, split + value_split)
    turned = apply_rotation(
        summed[..., :split].reshape(2 * passages, length, split // HEAD_SIZE, HEAD_SIZE),
        token_positions,
    ).astype(jnp.bfloat16)
    result = jnp.concatenate(
        [turned.reshape(2 * passages, length, split), summed[..., split:].astype(jnp.bfloat16)],
        axis=-1,
    )
    mine = result[:passages]
    returned = lax.ppermute(result[passages:], "groups", SWAP)
    low = jnp.where(first, mine, returned)
    high = jnp.where(first, returned, mine)
    rotary_rows = jnp.concatenate([low[..., :split], high[..., :split]], axis=-1)
    query_rows = rotary_rows[..., : heads_here * HEAD_SIZE]
    key = rotary_rows[..., heads_here * HEAD_SIZE :]
    value_rows = jnp.concatenate([low[..., split:], high[..., split:]], axis=-1)

    pairs = jnp.concatenate([key, value_rows], axis=-1)
    if row_count <= 8:
        by_shift = [pairs] + [
            lax.ppermute(pairs, "row", [(i, (i + k) % row_count) for i in range(row_count)])
            for k in range(1, row_count)
        ]
        gathered = jnp.stack(by_shift)
        owner_slot = (here - jnp.arange(row_count, dtype=jnp.int32)) % row_count
    else:
        gathered = lax.all_gather(pairs, "row", axis=0, tiled=False)
        owner_slot = jnp.arange(row_count, dtype=jnp.int32)
    gathered = gathered.reshape(
        row_count, passages, per_device, BLOCK_TOKENS, pairs_here, 2 * HEAD_SIZE
    )[:, :, :, :, 0]
    gathered = gathered.transpose(1, 0, 2, 3, 4).reshape(
        passages, passage_blocks, BLOCK_TOKENS, 2 * HEAD_SIZE
    )
    block_ids = jnp.arange(passage_blocks, dtype=jnp.int32)
    slot_of_block = owner_slot[block_ids // per_device] * per_device + block_ids % per_device
    kv_blocks = gathered[:, slot_of_block]

    local_blocks = here * per_device + jnp.arange(per_device, dtype=jnp.int32)
    nearby_blocks = local_blocks[:, None] + jnp.arange(3, dtype=jnp.int32)[None, :] - 1
    inside = (nearby_blocks >= 0) & (nearby_blocks < passage_blocks)
    nearby_clamped = jnp.clip(nearby_blocks, 0, passage_blocks - 1)
    passage_ids = jnp.arange(passages, dtype=jnp.int32)
    window = kv_blocks[passage_ids[:, None, None], nearby_clamped[None]]
    window = window.reshape(passages, per_device, 3 * BLOCK_TOKENS, 2 * HEAD_SIZE)

    global_here = lax.dynamic_slice_in_dim(global_block_index, column * pairs_here, pairs_here, 1)
    global_pairs = kv_blocks[passage_ids[:, None], global_here[:, 0, :]]
    global_pairs = global_pairs.reshape(passages, GLOBAL_BLOCKS * BLOCK_TOKENS, 2 * HEAD_SIZE)

    selected = lax.dynamic_slice_in_dim(random_block_index, column * heads_here, heads_here, 2)
    selected = lax.dynamic_slice_in_dim(selected, here * per_device, per_device, 1)
    arrived = kv_blocks[passage_ids[:, None, None, None], selected]
    arrived = arrived.reshape(
        passages, per_device, heads_here, RANDOM_BLOCKS * BLOCK_TOKENS, 2 * HEAD_SIZE
    )

    query_block_rows = query_rows.reshape(
        passages, per_device, BLOCK_TOKENS, heads_here, HEAD_SIZE
    )
    first_scores = jnp.einsum(
        "sqbgh,sqwh->sqgbw",
        query_block_rows,
        window[..., :HEAD_SIZE],
        preferred_element_type=jnp.float32,
    )
    second_scores = jnp.einsum(
        "sqbgh,swh->sqgbw",
        query_block_rows,
        global_pairs[..., :HEAD_SIZE],
        preferred_element_type=jnp.float32,
    )
    third_scores = jnp.einsum(
        "sqbgh,sqgwh->sqgbw",
        query_block_rows,
        arrived[..., :HEAD_SIZE],
        preferred_element_type=jnp.float32,
    )
    first_scores = first_scores * scale
    second_scores = second_scores * scale
    third_scores = third_scores * scale
    near_mask = jnp.repeat(inside, BLOCK_TOKENS, axis=1)
    first_scores = jnp.where(near_mask[None, :, None, None, :], first_scores, -jnp.inf)
    top = jnp.maximum(
        jnp.max(first_scores, axis=-1, keepdims=True),
        jnp.maximum(
            jnp.max(second_scores, axis=-1, keepdims=True),
            jnp.max(third_scores, axis=-1, keepdims=True),
        ),
    )
    near_weights = jnp.exp(first_scores - top)
    global_weights = jnp.exp(second_scores - top)
    random_weights = jnp.exp(third_scores - top)
    total = (
        jnp.sum(near_weights, axis=-1, keepdims=True)
        + jnp.sum(global_weights, axis=-1, keepdims=True)
        + jnp.sum(random_weights, axis=-1, keepdims=True)
    )
    near_probs = (near_weights / total).astype(jnp.bfloat16)
    global_probs = (global_weights / total).astype(jnp.bfloat16)
    random_probs = (random_weights / total).astype(jnp.bfloat16)
    mixed = jnp.einsum(
        "sqgbw,sqwh->sqbgh",
        near_probs,
        window[..., HEAD_SIZE:],
        preferred_element_type=jnp.float32,
    )
    mixed = mixed + jnp.einsum(
        "sqgbw,swh->sqbgh",
        global_probs,
        global_pairs[..., HEAD_SIZE:],
        preferred_element_type=jnp.float32,
    )
    mixed = mixed + jnp.einsum(
        "sqgbw,sqgwh->sqbgh",
        random_probs,
        arrived[..., HEAD_SIZE:],
        preferred_element_type=jnp.float32,
    )
    return mixed.reshape(passages, length, heads_here * HEAD_SIZE).astype(jnp.bfloat16)


def solution(mesh):
    placed = (
        P("groups", "row", "col"),
        P(),
        P("row", "col"),
        P("col"),
        P("row", "col"),
        P("col"),
        P("row", "col"),
        P("col"),
        P("groups", None, None, None),
        P("groups", None, None),
    )
    return jax.shard_map(
        shards, mesh=mesh, in_specs=placed, out_specs=P("groups", "row", "col"), check_vma=False
    )
```

```python
import math

import jax
import jax.numpy as jnp
from jax import lax
from jax.sharding import PartitionSpec as P

HEAD_SIZE = 128
BLOCK_TOKENS = 64
RANDOM_BLOCKS = 2
GLOBAL_BLOCKS = 2


rope_base = 1000000.0
norm_eps = 1e-06

SWAP = [(0, 1), (1, 0)]


def apply_rotation(values, token_positions):
    half = values.shape[-1] // 2
    freqs = 1.0 / rope_base ** (jnp.arange(half, dtype=jnp.float32) * 2.0 / values.shape[-1])
    angles = token_positions[:, None] * freqs[None, :]
    cosine = jnp.concatenate([jnp.cos(angles), jnp.cos(angles)], axis=-1)[None, :, None, :]
    sine = jnp.concatenate([jnp.sin(angles), jnp.sin(angles)], axis=-1)[None, :, None, :]
    turned = jnp.concatenate([-values[..., half:], values[..., :half]], axis=-1)
    return values * cosine + turned * sine


def snake_order(count):
    return [2 * z for z in range(count // 2)] + [2 * z + 1 for z in reversed(range(count // 2))]


def gather_rows(ahead, behind, count, here):
    if count != 8:
        shard = jnp.concatenate([ahead, behind], axis=0)
        return lax.all_gather(shard, "row", axis=0, tiled=True), ahead
    order = snake_order(count)
    position = [0] * count
    for i, d in enumerate(order):
        position[d] = i
    forward = [(order[i], order[(i + 1) % count]) for i in range(count)]
    backward = [(order[i], order[(i - 1) % count]) for i in range(count)]
    half = ahead.shape[0]
    ahead_parts, behind_parts = [ahead], [behind]
    for _ in range(count - 1):
        ahead = lax.ppermute(ahead, "row", forward)
        behind = lax.ppermute(behind, "row", backward)
        ahead_parts.append(ahead)
        behind_parts.append(behind)
    table = jnp.array(position, dtype=jnp.int32)
    mine = table[here]
    ahead_stack, behind_stack = jnp.stack(ahead_parts), jnp.stack(behind_parts)

    def placed(at):
        def build(ahead_stack, behind_stack):
            return jnp.concatenate(
                [
                    jnp.stack([ahead_stack[(at - position[d]) % count] for d in range(count)]),
                    jnp.stack([behind_stack[(position[d] - at) % count] for d in range(count)]),
                ],
                axis=1,
            )

        return build

    joined = lax.switch(mine, [placed(at) for at in range(count)], ahead_stack, behind_stack)
    return joined.reshape(count * 2 * half, ahead.shape[1]), ahead_parts[1]


def shards(
    tokens,
    gain,
    w_query,
    b_query,
    key_weight,
    b_key,
    value_weight,
    value_bias,
    random_block_index,
    global_block_index,
):
    row_count = lax.axis_size("row")
    here = lax.axis_index("row")
    column = lax.axis_index("col")
    group = lax.axis_index("groups")
    passages, length, _ = tokens.shape
    heads_here = w_query.shape[1] // HEAD_SIZE
    pairs_here = key_weight.shape[1] // HEAD_SIZE
    passage_groups = heads_here // pairs_here
    per_device = length // BLOCK_TOKENS
    passage_blocks = row_count * per_device
    scale = 1.0 / math.sqrt(HEAD_SIZE)

    rotary_cols = (heads_here + pairs_here) * HEAD_SIZE
    split = rotary_cols // 2
    value_cols = pairs_here * HEAD_SIZE
    value_split = value_cols // 2
    rotary_w = jnp.concatenate([w_query, key_weight], axis=1)
    rotary_b = jnp.concatenate([b_query, b_key], axis=0)
    first = group == 0
    rows_here = w_query.shape[0]

    def panel_rows(start, stop):
        return jnp.concatenate(
            [
                lax.dynamic_slice_in_dim(rotary_w[start:stop], group * split, split, 1),
                lax.dynamic_slice_in_dim(
                    value_weight[start:stop], group * value_split, value_split, 1
                ),
            ],
            axis=1,
        )

    full_panel, first_arrival = gather_rows(
        panel_rows(0, rows_here // 2),
        panel_rows(rows_here // 2, rows_here),
        row_count,
        here,
    )
    panel_bias = jnp.where(
        first,
        jnp.concatenate([rotary_b[:split], value_bias[:value_split]]),
        jnp.concatenate([rotary_b[split:], value_bias[value_split:]]),
    )

    other_half = lax.ppermute(tokens, "col", SWAP)
    late_tokens, _ = lax.optimization_barrier((tokens, first_arrival))
    partner_half = lax.ppermute(late_tokens, "groups", SWAP)
    partner_other = lax.ppermute(partner_half, "col", SWAP)
    whole = jnp.where(
        column == 0,
        jnp.concatenate([tokens, other_half], axis=2),
        jnp.concatenate([other_half, tokens], axis=2),
    )
    partner = jnp.where(
        column == 0,
        jnp.concatenate([partner_half, partner_other], axis=2),
        jnp.concatenate([partner_other, partner_half], axis=2),
    )
    both = jnp.concatenate([whole, partner], axis=0)
    widened = both.astype(jnp.float32)
    power = jnp.mean(widened * widened, axis=-1, keepdims=True)
    normed = (
        (widened * lax.rsqrt(power + norm_eps) * gain)
        .astype(jnp.bfloat16)
        .reshape(2 * passages * length, -1)
    )
    token_positions = (here * length + jnp.arange(length, dtype=jnp.int32)).astype(jnp.float32)

    summed = jnp.dot(normed, full_panel, preferred_element_type=jnp.float32) + panel_bias
    summed = summed.reshape(2 * passages, length, split + value_split)
    turned = apply_rotation(
        summed[..., :split].reshape(2 * passages, length, split // HEAD_SIZE, HEAD_SIZE),
        token_positions,
    ).astype(jnp.bfloat16)
    result = jnp.concatenate(
        [turned.reshape(2 * passages, length, split), summed[..., split:].astype(jnp.bfloat16)],
        axis=-1,
    )
    mine = result[:passages]
    returned = lax.ppermute(result[passages:], "groups", SWAP)
    low = jnp.where(first, mine, returned)
    high = jnp.where(first, returned, mine)
    rotary_rows = jnp.concatenate([low[..., :split], high[..., :split]], axis=-1)
    query_rows = rotary_rows[..., : heads_here * HEAD_SIZE]
    key = rotary_rows[..., heads_here * HEAD_SIZE :]
    value_rows = jnp.concatenate([low[..., split:], high[..., split:]], axis=-1)

    pairs = jnp.concatenate([key, value_rows], axis=-1)
    if row_count <= 8:
        by_shift = [pairs] + [
            lax.ppermute(pairs, "row", [(i, (i + k) % row_count) for i in range(row_count)])
            for k in range(1, row_count)
        ]
        gathered = jnp.stack(by_shift)
        owner_slot = (here - jnp.arange(row_count, dtype=jnp.int32)) % row_count
    else:
        gathered = lax.all_gather(pairs, "row", axis=0, tiled=False)
        owner_slot = jnp.arange(row_count, dtype=jnp.int32)
    gathered = gathered.reshape(
        row_count, passages, per_device, BLOCK_TOKENS, pairs_here, 2 * HEAD_SIZE
    )[:, :, :, :, 0]
    gathered = gathered.transpose(1, 0, 2, 3, 4).reshape(
        passages, passage_blocks, BLOCK_TOKENS, 2 * HEAD_SIZE
    )
    block_ids = jnp.arange(passage_blocks, dtype=jnp.int32)
    slot_of_block = owner_slot[block_ids // per_device] * per_device + block_ids % per_device
    kv_blocks = gathered[:, slot_of_block]

    local_blocks = here * per_device + jnp.arange(per_device, dtype=jnp.int32)
    nearby_blocks = local_blocks[:, None] + jnp.arange(3, dtype=jnp.int32)[None, :] - 1
    inside = (nearby_blocks >= 0) & (nearby_blocks < passage_blocks)
    nearby_clamped = jnp.clip(nearby_blocks, 0, passage_blocks - 1)
    passage_ids = jnp.arange(passages, dtype=jnp.int32)
    window = kv_blocks[passage_ids[:, None, None], nearby_clamped[None]]
    window = window.reshape(passages, per_device, 3 * BLOCK_TOKENS, 2 * HEAD_SIZE)

    global_here = lax.dynamic_slice_in_dim(global_block_index, column * pairs_here, pairs_here, 1)
    global_pairs = kv_blocks[passage_ids[:, None], global_here[:, 0, :]]
    global_pairs = global_pairs.reshape(passages, GLOBAL_BLOCKS * BLOCK_TOKENS, 2 * HEAD_SIZE)

    selected = lax.dynamic_slice_in_dim(random_block_index, column * heads_here, heads_here, 2)
    selected = lax.dynamic_slice_in_dim(selected, here * per_device, per_device, 1)
    arrived = kv_blocks[passage_ids[:, None, None, None], selected]
    arrived = arrived.reshape(
        passages, per_device, heads_here, RANDOM_BLOCKS * BLOCK_TOKENS, 2 * HEAD_SIZE
    )

    query_block_rows = query_rows.reshape(
        passages, per_device, BLOCK_TOKENS, heads_here, HEAD_SIZE
    )
    first_scores = jnp.einsum(
        "sqbgh,sqwh->sqgbw",
        query_block_rows,
        window[..., :HEAD_SIZE],
        preferred_element_type=jnp.float32,
    )
    second_scores = jnp.einsum(
        "sqbgh,swh->sqgbw",
        query_block_rows,
        global_pairs[..., :HEAD_SIZE],
        preferred_element_type=jnp.float32,
    )
    third_scores = jnp.einsum(
        "sqbgh,sqgwh->sqgbw",
        query_block_rows,
        arrived[..., :HEAD_SIZE],
        preferred_element_type=jnp.float32,
    )
    first_scores = first_scores * scale
    second_scores = second_scores * scale
    third_scores = third_scores * scale
    near_mask = jnp.repeat(inside, BLOCK_TOKENS, axis=1)
    first_scores = jnp.where(near_mask[None, :, None, None, :], first_scores, -jnp.inf)
    top = jnp.maximum(
        jnp.max(first_scores, axis=-1, keepdims=True),
        jnp.maximum(
            jnp.max(second_scores, axis=-1, keepdims=True),
            jnp.max(third_scores, axis=-1, keepdims=True),
        ),
    )
    near_weights = jnp.exp(first_scores - top)
    global_weights = jnp.exp(second_scores - top)
    random_weights = jnp.exp(third_scores - top)
    total = (
        jnp.sum(near_weights, axis=-1, keepdims=True)
        + jnp.sum(global_weights, axis=-1, keepdims=True)
        + jnp.sum(random_weights, axis=-1, keepdims=True)
    )
    near_probs = (near_weights / total).astype(jnp.bfloat16)
    global_probs = (global_weights / total).astype(jnp.bfloat16)
    random_probs = (random_weights / total).astype(jnp.bfloat16)
    mixed = jnp.einsum(
        "sqgbw,sqwh->sqbgh",
        near_probs,
        window[..., HEAD_SIZE:],
        preferred_element_type=jnp.float32,
    )
    mixed = mixed + jnp.einsum(
        "sqgbw,swh->sqbgh",
        global_probs,
        global_pairs[..., HEAD_SIZE:],
        preferred_element_type=jnp.float32,
    )
    mixed = mixed + jnp.einsum(
        "sqgbw,sqgwh->sqbgh",
        random_probs,
        arrived[..., HEAD_SIZE:],
        preferred_element_type=jnp.float32,
    )
    return mixed.reshape(passages, length, heads_here * HEAD_SIZE).astype(jnp.bfloat16)


def solution(mesh):
    placed = (
        P("groups", "row", "col"),
        P(),
        P("row", "col"),
        P("col"),
        P("row", "col"),
        P("col"),
        P("row", "col"),
        P("col"),
        P("groups", None, None, None),
        P("groups", None, None),
    )
    return jax.shard_map(
        shards, mesh=mesh, in_specs=placed, out_specs=P("groups", "row", "col"), check_vma=False
    )
```

```python
import math

import jax
import jax.numpy as jnp
from jax import lax
from jax.sharding import PartitionSpec as P

HEAD_SIZE = 128
BLOCK_TOKENS = 64
RANDOM_BLOCKS = 2
GLOBAL_BLOCKS = 2


rope_base = 1000000.0
norm_eps = 1e-06

SWAP = [(0, 1), (1, 0)]


def apply_rotation(values, token_positions):
    half = values.shape[-1] // 2
    freqs = 1.0 / rope_base ** (jnp.arange(half, dtype=jnp.float32) * 2.0 / values.shape[-1])
    angles = token_positions[:, None] * freqs[None, :]
    cosine = jnp.concatenate([jnp.cos(angles), jnp.cos(angles)], axis=-1)[None, :, None, :]
    sine = jnp.concatenate([jnp.sin(angles), jnp.sin(angles)], axis=-1)[None, :, None, :]
    turned = jnp.concatenate([-values[..., half:], values[..., :half]], axis=-1)
    return values * cosine + turned * sine


def snake_order(count):
    return [2 * z for z in range(count // 2)] + [2 * z + 1 for z in reversed(range(count // 2))]


def gather_rows(ahead, behind, count, here):
    if count != 8:
        shard = jnp.concatenate([ahead, behind], axis=0)
        return lax.all_gather(shard, "row", axis=0, tiled=True), ahead
    order = snake_order(count)
    position = [0] * count
    for i, d in enumerate(order):
        position[d] = i
    forward = [(order[i], order[(i + 1) % count]) for i in range(count)]
    backward = [(order[i], order[(i - 1) % count]) for i in range(count)]
    half = ahead.shape[0]
    ahead_parts, behind_parts = [ahead], [behind]
    for _ in range(count - 1):
        ahead = lax.ppermute(ahead, "row", forward)
        behind = lax.ppermute(behind, "row", backward)
        ahead_parts.append(ahead)
        behind_parts.append(behind)
    table = jnp.array(position, dtype=jnp.int32)
    mine = table[here]
    ahead_pick = (mine - table) % count
    behind_pick = (table - mine) % count
    joined = jnp.concatenate(
        [jnp.stack(ahead_parts)[ahead_pick], jnp.stack(behind_parts)[behind_pick]], axis=1
    )
    return joined.reshape(count * 2 * half, ahead.shape[1]), ahead_parts[1]


def shards(
    tokens,
    gain,
    w_query,
    b_query,
    key_weight,
    b_key,
    value_weight,
    value_bias,
    random_block_index,
    global_block_index,
):
    row_count = lax.axis_size("row")
    here = lax.axis_index("row")
    column = lax.axis_index("col")
    group = lax.axis_index("groups")
    passages, length, _ = tokens.shape
    heads_here = w_query.shape[1] // HEAD_SIZE
    pairs_here = key_weight.shape[1] // HEAD_SIZE
    passage_groups = heads_here // pairs_here
    per_device = length // BLOCK_TOKENS
    passage_blocks = row_count * per_device
    scale = 1.0 / math.sqrt(HEAD_SIZE)

    rotary_cols = (heads_here + pairs_here) * HEAD_SIZE
    split = rotary_cols // 2
    value_cols = pairs_here * HEAD_SIZE
    value_split = value_cols // 2
    rotary_w = jnp.concatenate([w_query, key_weight], axis=1)
    rotary_b = jnp.concatenate([b_query, b_key], axis=0)
    first = group == 0
    rows_here = w_query.shape[0]

    def panel_rows(start, stop):
        return jnp.concatenate(
            [
                lax.dynamic_slice_in_dim(rotary_w[start:stop], group * split, split, 1),
                lax.dynamic_slice_in_dim(
                    value_weight[start:stop], group * value_split, value_split, 1
                ),
            ],
            axis=1,
        )

    full_panel, first_arrival = gather_rows(
        panel_rows(0, rows_here // 2),
        panel_rows(rows_here // 2, rows_here),
        row_count,
        here,
    )
    panel_bias = jnp.where(
        first,
        jnp.concatenate([rotary_b[:split], value_bias[:value_split]]),
        jnp.concatenate([rotary_b[split:], value_bias[value_split:]]),
    )

    other_half = lax.ppermute(tokens, "col", SWAP)
    late_tokens, _ = lax.optimization_barrier((tokens, first_arrival))
    partner_half = lax.ppermute(late_tokens, "groups", SWAP)
    partner_other = lax.ppermute(partner_half, "col", SWAP)
    whole = jnp.where(
        column == 0,
        jnp.concatenate([tokens, other_half], axis=2),
        jnp.concatenate([other_half, tokens], axis=2),
    )
    partner = jnp.where(
        column == 0,
        jnp.concatenate([partner_half, partner_other], axis=2),
        jnp.concatenate([partner_other, partner_half], axis=2),
    )
    both = jnp.concatenate([whole, partner], axis=0)
    widened = both.astype(jnp.float32)
    power = jnp.mean(widened * widened, axis=-1, keepdims=True)
    normed = (
        (widened * lax.rsqrt(power + norm_eps) * gain)
        .astype(jnp.bfloat16)
        .reshape(2 * passages * length, -1)
    )
    token_positions = (here * length + jnp.arange(length, dtype=jnp.int32)).astype(jnp.float32)

    summed = jnp.dot(normed, full_panel, preferred_element_type=jnp.float32) + panel_bias
    summed = summed.reshape(2 * passages, length, split + value_split)
    turned = apply_rotation(
        summed[..., :split].reshape(2 * passages, length, split // HEAD_SIZE, HEAD_SIZE),
        token_positions,
    ).astype(jnp.bfloat16)
    result = jnp.concatenate(
        [turned.reshape(2 * passages, length, split), summed[..., split:].astype(jnp.bfloat16)],
        axis=-1,
    )
    mine = result[:passages]
    returned = lax.ppermute(result[passages:], "groups", SWAP)
    low = jnp.where(first, mine, returned)
    high = jnp.where(first, returned, mine)
    rotary_rows = jnp.concatenate([low[..., :split], high[..., :split]], axis=-1)
    query_rows = rotary_rows[..., : heads_here * HEAD_SIZE]
    key = rotary_rows[..., heads_here * HEAD_SIZE :]
    value_rows = jnp.concatenate([low[..., split:], high[..., split:]], axis=-1)

    pairs = jnp.concatenate([key, value_rows], axis=-1)
    if row_count == 8:
        order = snake_order(row_count)
        position = [0] * row_count
        for i, d in enumerate(order):
            position[d] = i
        forward = [(order[i], order[(i + 1) % row_count]) for i in range(row_count)]
        backward = [(order[i], order[(i - 1) % row_count]) for i in range(row_count)]
        ahead, behind = pairs, pairs
        ahead_parts, behind_parts = [], []
        for step in range(1, row_count // 2 + 1):
            ahead = lax.ppermute(ahead, "row", forward)
            ahead_parts.append(ahead)
            if step < row_count // 2:
                behind = lax.ppermute(behind, "row", backward)
                behind_parts.append(behind)
        gathered = jnp.stack([pairs] + ahead_parts + behind_parts)
        table = jnp.array(position, dtype=jnp.int32)
        delta = (table[here] - table) % row_count
        owner_slot = jnp.where(delta <= row_count // 2, delta, row_count // 2 + row_count - delta)
    else:
        gathered = lax.all_gather(pairs, "row", axis=0, tiled=False)
        owner_slot = jnp.arange(row_count, dtype=jnp.int32)
    gathered = gathered.reshape(
        row_count, passages, per_device, BLOCK_TOKENS, pairs_here, 2 * HEAD_SIZE
    )[:, :, :, :, 0]
    gathered = gathered.transpose(1, 0, 2, 3, 4).reshape(
        passages, passage_blocks, BLOCK_TOKENS, 2 * HEAD_SIZE
    )
    block_ids = jnp.arange(passage_blocks, dtype=jnp.int32)
    slot_of_block = owner_slot[block_ids // per_device] * per_device + block_ids % per_device
    kv_blocks = gathered[:, slot_of_block]

    local_blocks = here * per_device + jnp.arange(per_device, dtype=jnp.int32)
    nearby_blocks = local_blocks[:, None] + jnp.arange(3, dtype=jnp.int32)[None, :] - 1
    inside = (nearby_blocks >= 0) & (nearby_blocks < passage_blocks)
    nearby_clamped = jnp.clip(nearby_blocks, 0, passage_blocks - 1)
    passage_ids = jnp.arange(passages, dtype=jnp.int32)
    window = kv_blocks[passage_ids[:, None, None], nearby_clamped[None]]
    window = window.reshape(passages, per_device, 3 * BLOCK_TOKENS, 2 * HEAD_SIZE)

    global_here = lax.dynamic_slice_in_dim(global_block_index, column * pairs_here, pairs_here, 1)
    global_pairs = kv_blocks[passage_ids[:, None], global_here[:, 0, :]]
    global_pairs = global_pairs.reshape(passages, GLOBAL_BLOCKS * BLOCK_TOKENS, 2 * HEAD_SIZE)

    selected = lax.dynamic_slice_in_dim(random_block_index, column * heads_here, heads_here, 2)
    selected = lax.dynamic_slice_in_dim(selected, here * per_device, per_device, 1)
    arrived = kv_blocks[passage_ids[:, None, None, None], selected]
    arrived = arrived.reshape(
        passages, per_device, heads_here, RANDOM_BLOCKS * BLOCK_TOKENS, 2 * HEAD_SIZE
    )

    query_block_rows = query_rows.reshape(
        passages, per_device, BLOCK_TOKENS, heads_here, HEAD_SIZE
    )
    first_scores = jnp.einsum(
        "sqbgh,sqwh->sqgbw",
        query_block_rows,
        window[..., :HEAD_SIZE],
        preferred_element_type=jnp.float32,
    )
    second_scores = jnp.einsum(
        "sqbgh,swh->sqgbw",
        query_block_rows,
        global_pairs[..., :HEAD_SIZE],
        preferred_element_type=jnp.float32,
    )
    third_scores = jnp.einsum(
        "sqbgh,sqgwh->sqgbw",
        query_block_rows,
        arrived[..., :HEAD_SIZE],
        preferred_element_type=jnp.float32,
    )
    first_scores = first_scores * scale
    second_scores = second_scores * scale
    third_scores = third_scores * scale
    near_mask = jnp.repeat(inside, BLOCK_TOKENS, axis=1)
    first_scores = jnp.where(near_mask[None, :, None, None, :], first_scores, -jnp.inf)
    top = jnp.maximum(
        jnp.max(first_scores, axis=-1, keepdims=True),
        jnp.maximum(
            jnp.max(second_scores, axis=-1, keepdims=True),
            jnp.max(third_scores, axis=-1, keepdims=True),
        ),
    )
    near_weights = jnp.exp(first_scores - top)
    global_weights = jnp.exp(second_scores - top)
    random_weights = jnp.exp(third_scores - top)
    total = (
        jnp.sum(near_weights, axis=-1, keepdims=True)
        + jnp.sum(global_weights, axis=-1, keepdims=True)
        + jnp.sum(random_weights, axis=-1, keepdims=True)
    )
    near_probs = (near_weights / total).astype(jnp.bfloat16)
    global_probs = (global_weights / total).astype(jnp.bfloat16)
    random_probs = (random_weights / total).astype(jnp.bfloat16)
    mixed = jnp.einsum(
        "sqgbw,sqwh->sqbgh",
        near_probs,
        window[..., HEAD_SIZE:],
        preferred_element_type=jnp.float32,
    )
    mixed = mixed + jnp.einsum(
        "sqgbw,swh->sqbgh",
        global_probs,
        global_pairs[..., HEAD_SIZE:],
        preferred_element_type=jnp.float32,
    )
    mixed = mixed + jnp.einsum(
        "sqgbw,sqgwh->sqbgh",
        random_probs,
        arrived[..., HEAD_SIZE:],
        preferred_element_type=jnp.float32,
    )
    return mixed.reshape(passages, length, heads_here * HEAD_SIZE).astype(jnp.bfloat16)


def solution(mesh):
    placed = (
        P("groups", "row", "col"),
        P(),
        P("row", "col"),
        P("col"),
        P("row", "col"),
        P("col"),
        P("row", "col"),
        P("col"),
        P("groups", None, None, None),
        P("groups", None, None),
    )
    return jax.shard_map(
        shards, mesh=mesh, in_specs=placed, out_specs=P("groups", "row", "col"), check_vma=False
    )
```

```python
import math

import jax
import jax.numpy as jnp
from jax import lax
from jax.sharding import PartitionSpec as P

HEAD_SIZE = 128
BLOCK_TOKENS = 64
RANDOM_BLOCKS = 2
GLOBAL_BLOCKS = 2


rope_base = 1000000.0
norm_eps = 1e-06

SWAP = [(0, 1), (1, 0)]


def apply_rotation(values, token_positions):
    half = values.shape[-1] // 2
    freqs = 1.0 / rope_base ** (jnp.arange(half, dtype=jnp.float32) * 2.0 / values.shape[-1])
    angles = token_positions[:, None] * freqs[None, :]
    cosine = jnp.concatenate([jnp.cos(angles), jnp.cos(angles)], axis=-1)[None, :, None, :]
    sine = jnp.concatenate([jnp.sin(angles), jnp.sin(angles)], axis=-1)[None, :, None, :]
    turned = jnp.concatenate([-values[..., half:], values[..., :half]], axis=-1)
    return values * cosine + turned * sine


def snake_order(count):
    return [2 * z for z in range(count // 2)] + [2 * z + 1 for z in reversed(range(count // 2))]


def gather_rows(ahead, behind, count, here):
    if count != 8:
        shard = jnp.concatenate([ahead, behind], axis=0)
        return lax.all_gather(shard, "row", axis=0, tiled=True), ahead
    order = snake_order(count)
    position = [0] * count
    for i, d in enumerate(order):
        position[d] = i
    forward = [(order[i], order[(i + 1) % count]) for i in range(count)]
    backward = [(order[i], order[(i - 1) % count]) for i in range(count)]
    half = ahead.shape[0]
    ahead_parts, behind_parts = [ahead], [behind]
    for _ in range(count - 1):
        ahead = lax.ppermute(ahead, "row", forward)
        behind = lax.ppermute(behind, "row", backward)
        ahead_parts.append(ahead)
        behind_parts.append(behind)
    table = jnp.array(position, dtype=jnp.int32)
    mine = table[here]
    ahead_pick = (mine - table) % count
    behind_pick = (table - mine) % count
    joined = jnp.concatenate(
        [jnp.stack(ahead_parts)[ahead_pick], jnp.stack(behind_parts)[behind_pick]], axis=1
    )
    return joined.reshape(count * 2 * half, ahead.shape[1]), ahead_parts[1]


def shards(
    tokens,
    gain,
    w_query,
    b_query,
    key_weight,
    b_key,
    value_weight,
    value_bias,
    random_block_index,
    global_block_index,
):
    row_count = lax.axis_size("row")
    here = lax.axis_index("row")
    column = lax.axis_index("col")
    group = lax.axis_index("groups")
    passages, length, _ = tokens.shape
    heads_here = w_query.shape[1] // HEAD_SIZE
    pairs_here = key_weight.shape[1] // HEAD_SIZE
    passage_groups = heads_here // pairs_here
    per_device = length // BLOCK_TOKENS
    passage_blocks = row_count * per_device
    scale = 1.0 / math.sqrt(HEAD_SIZE)

    rotary_cols = (heads_here + pairs_here) * HEAD_SIZE
    split = rotary_cols // 2
    value_cols = pairs_here * HEAD_SIZE
    value_split = value_cols // 2
    rotary_w = jnp.concatenate([w_query, key_weight], axis=1)
    rotary_b = jnp.concatenate([b_query, b_key], axis=0)
    first = group == 0
    rows_here = w_query.shape[0]

    def panel_rows(start, stop):
        return jnp.concatenate(
            [
                lax.dynamic_slice_in_dim(rotary_w[start:stop], group * split, split, 1),
                lax.dynamic_slice_in_dim(
                    value_weight[start:stop], group * value_split, value_split, 1
                ),
            ],
            axis=1,
        )

    full_panel, first_arrival = gather_rows(
        panel_rows(0, rows_here // 2),
        panel_rows(rows_here // 2, rows_here),
        row_count,
        here,
    )
    panel_bias = jnp.where(
        first,
        jnp.concatenate([rotary_b[:split], value_bias[:value_split]]),
        jnp.concatenate([rotary_b[split:], value_bias[value_split:]]),
    )

    other_half = lax.ppermute(tokens, "col", SWAP)
    late_tokens, _ = lax.optimization_barrier((tokens, first_arrival))
    partner_half = lax.ppermute(late_tokens, "groups", SWAP)
    partner_other = lax.ppermute(partner_half, "col", SWAP)
    whole = jnp.where(
        column == 0,
        jnp.concatenate([tokens, other_half], axis=2),
        jnp.concatenate([other_half, tokens], axis=2),
    )
    partner = jnp.where(
        column == 0,
        jnp.concatenate([partner_half, partner_other], axis=2),
        jnp.concatenate([partner_other, partner_half], axis=2),
    )
    both = jnp.concatenate([whole, partner], axis=0)
    widened = both.astype(jnp.float32)
    power = jnp.mean(widened * widened, axis=-1, keepdims=True)
    normed = (
        (widened * lax.rsqrt(power + norm_eps) * gain)
        .astype(jnp.bfloat16)
        .reshape(2 * passages * length, -1)
    )
    token_positions = (here * length + jnp.arange(length, dtype=jnp.int32)).astype(jnp.float32)

    summed = jnp.dot(normed, full_panel, preferred_element_type=jnp.float32) + panel_bias
    summed = summed.reshape(2 * passages, length, split + value_split)
    turned = apply_rotation(
        summed[..., :split].reshape(2 * passages, length, split // HEAD_SIZE, HEAD_SIZE),
        token_positions,
    ).astype(jnp.bfloat16)
    result = jnp.concatenate(
        [turned.reshape(2 * passages, length, split), summed[..., split:].astype(jnp.bfloat16)],
        axis=-1,
    )
    mine = result[:passages]
    returned = lax.ppermute(result[passages:], "groups", SWAP)
    low = jnp.where(first, mine, returned)
    high = jnp.where(first, returned, mine)
    rotary_rows = jnp.concatenate([low[..., :split], high[..., :split]], axis=-1)
    query_rows = rotary_rows[..., : heads_here * HEAD_SIZE]
    key = rotary_rows[..., heads_here * HEAD_SIZE :]
    value_rows = jnp.concatenate([low[..., split:], high[..., split:]], axis=-1)

    pairs = jnp.concatenate([key, value_rows], axis=-1)
    if row_count == 8:
        order = snake_order(row_count)
        position = [0] * row_count
        for i, d in enumerate(order):
            position[d] = i
        forward = [(order[i], order[(i + 1) % row_count]) for i in range(row_count)]
        backward = [(order[i], order[(i - 1) % row_count]) for i in range(row_count)]
        across = [(order[i], order[(i + row_count // 2) % row_count]) for i in range(row_count)]
        opposite = lax.ppermute(pairs, "row", across)
        ahead, behind = pairs, pairs
        ahead_parts, behind_parts = [], []
        for step in range(1, row_count // 2):
            ahead = lax.ppermute(ahead, "row", forward)
            behind = lax.ppermute(behind, "row", backward)
            ahead_parts.append(ahead)
            behind_parts.append(behind)
        gathered = jnp.stack([pairs] + ahead_parts + [opposite] + behind_parts)
        table = jnp.array(position, dtype=jnp.int32)
        delta = (table[here] - table) % row_count
        owner_slot = jnp.where(delta <= row_count // 2, delta, row_count // 2 + row_count - delta)
    else:
        gathered = lax.all_gather(pairs, "row", axis=0, tiled=False)
        owner_slot = jnp.arange(row_count, dtype=jnp.int32)
    gathered = gathered.reshape(
        row_count, passages, per_device, BLOCK_TOKENS, pairs_here, 2 * HEAD_SIZE
    )[:, :, :, :, 0]
    gathered = gathered.transpose(1, 0, 2, 3, 4).reshape(
        passages, passage_blocks, BLOCK_TOKENS, 2 * HEAD_SIZE
    )
    block_ids = jnp.arange(passage_blocks, dtype=jnp.int32)
    slot_of_block = owner_slot[block_ids // per_device] * per_device + block_ids % per_device
    kv_blocks = gathered[:, slot_of_block]

    local_blocks = here * per_device + jnp.arange(per_device, dtype=jnp.int32)
    nearby_blocks = local_blocks[:, None] + jnp.arange(3, dtype=jnp.int32)[None, :] - 1
    inside = (nearby_blocks >= 0) & (nearby_blocks < passage_blocks)
    nearby_clamped = jnp.clip(nearby_blocks, 0, passage_blocks - 1)
    passage_ids = jnp.arange(passages, dtype=jnp.int32)
    window = kv_blocks[passage_ids[:, None, None], nearby_clamped[None]]
    window = window.reshape(passages, per_device, 3 * BLOCK_TOKENS, 2 * HEAD_SIZE)

    global_here = lax.dynamic_slice_in_dim(global_block_index, column * pairs_here, pairs_here, 1)
    global_pairs = kv_blocks[passage_ids[:, None], global_here[:, 0, :]]
    global_pairs = global_pairs.reshape(passages, GLOBAL_BLOCKS * BLOCK_TOKENS, 2 * HEAD_SIZE)

    selected = lax.dynamic_slice_in_dim(random_block_index, column * heads_here, heads_here, 2)
    selected = lax.dynamic_slice_in_dim(selected, here * per_device, per_device, 1)
    arrived = kv_blocks[passage_ids[:, None, None, None], selected]
    arrived = arrived.reshape(
        passages, per_device, heads_here, RANDOM_BLOCKS * BLOCK_TOKENS, 2 * HEAD_SIZE
    )

    query_block_rows = query_rows.reshape(
        passages, per_device, BLOCK_TOKENS, heads_here, HEAD_SIZE
    )
    first_scores = jnp.einsum(
        "sqbgh,sqwh->sqgbw",
        query_block_rows,
        window[..., :HEAD_SIZE],
        preferred_element_type=jnp.float32,
    )
    second_scores = jnp.einsum(
        "sqbgh,swh->sqgbw",
        query_block_rows,
        global_pairs[..., :HEAD_SIZE],
        preferred_element_type=jnp.float32,
    )
    third_scores = jnp.einsum(
        "sqbgh,sqgwh->sqgbw",
        query_block_rows,
        arrived[..., :HEAD_SIZE],
        preferred_element_type=jnp.float32,
    )
    first_scores = first_scores * scale
    second_scores = second_scores * scale
    third_scores = third_scores * scale
    near_mask = jnp.repeat(inside, BLOCK_TOKENS, axis=1)
    first_scores = jnp.where(near_mask[None, :, None, None, :], first_scores, -jnp.inf)
    top = jnp.maximum(
        jnp.max(first_scores, axis=-1, keepdims=True),
        jnp.maximum(
            jnp.max(second_scores, axis=-1, keepdims=True),
            jnp.max(third_scores, axis=-1, keepdims=True),
        ),
    )
    near_weights = jnp.exp(first_scores - top)
    global_weights = jnp.exp(second_scores - top)
    random_weights = jnp.exp(third_scores - top)
    total = (
        jnp.sum(near_weights, axis=-1, keepdims=True)
        + jnp.sum(global_weights, axis=-1, keepdims=True)
        + jnp.sum(random_weights, axis=-1, keepdims=True)
    )
    near_probs = (near_weights / total).astype(jnp.bfloat16)
    global_probs = (global_weights / total).astype(jnp.bfloat16)
    random_probs = (random_weights / total).astype(jnp.bfloat16)
    mixed = jnp.einsum(
        "sqgbw,sqwh->sqbgh",
        near_probs,
        window[..., HEAD_SIZE:],
        preferred_element_type=jnp.float32,
    )
    mixed = mixed + jnp.einsum(
        "sqgbw,swh->sqbgh",
        global_probs,
        global_pairs[..., HEAD_SIZE:],
        preferred_element_type=jnp.float32,
    )
    mixed = mixed + jnp.einsum(
        "sqgbw,sqgwh->sqbgh",
        random_probs,
        arrived[..., HEAD_SIZE:],
        preferred_element_type=jnp.float32,
    )
    return mixed.reshape(passages, length, heads_here * HEAD_SIZE).astype(jnp.bfloat16)


def solution(mesh):
    placed = (
        P("groups", "row", "col"),
        P(),
        P("row", "col"),
        P("col"),
        P("row", "col"),
        P("col"),
        P("row", "col"),
        P("col"),
        P("groups", None, None, None),
        P("groups", None, None),
    )
    return jax.shard_map(
        shards, mesh=mesh, in_specs=placed, out_specs=P("groups", "row", "col"), check_vma=False
    )
```

```python
import math

import jax
import jax.numpy as jnp
from jax import lax
from jax.sharding import PartitionSpec as P

HEAD_SIZE = 128
BLOCK_TOKENS = 64
RANDOM_BLOCKS = 2
GLOBAL_BLOCKS = 2


rope_base = 1000000.0
norm_eps = 1e-06

SWAP = [(0, 1), (1, 0)]


def apply_rotation(values, token_positions):
    half = values.shape[-1] // 2
    freqs = 1.0 / rope_base ** (jnp.arange(half, dtype=jnp.float32) * 2.0 / values.shape[-1])
    angles = token_positions[:, None] * freqs[None, :]
    cosine = jnp.concatenate([jnp.cos(angles), jnp.cos(angles)], axis=-1)[None, :, None, :]
    sine = jnp.concatenate([jnp.sin(angles), jnp.sin(angles)], axis=-1)[None, :, None, :]
    turned = jnp.concatenate([-values[..., half:], values[..., :half]], axis=-1)
    return values * cosine + turned * sine


def snake_order(count):
    return [2 * z for z in range(count // 2)] + [2 * z + 1 for z in reversed(range(count // 2))]


def gather_rows(ahead, behind, count, here, between, tie_step):
    if count != 8:
        shard = jnp.concatenate([ahead, behind], axis=0)
        return lax.all_gather(shard, "row", axis=0, tiled=True), between(ahead)
    order = snake_order(count)
    position = [0] * count
    for i, d in enumerate(order):
        position[d] = i
    forward = [(order[i], order[(i + 1) % count]) for i in range(count)]
    backward = [(order[i], order[(i - 1) % count]) for i in range(count)]
    half = ahead.shape[0]
    ahead_parts, behind_parts = [ahead], [behind]
    tied = None
    for step in range(1, count):
        if step == tie_step:
            ahead, tied = lax.optimization_barrier((ahead, tied))
        ahead = lax.ppermute(ahead, "row", forward)
        behind = lax.ppermute(behind, "row", backward)
        ahead_parts.append(ahead)
        behind_parts.append(behind)
        if step == 1:
            tied = between(ahead)
    table = jnp.array(position, dtype=jnp.int32)
    mine = table[here]
    ahead_pick = (mine - table) % count
    behind_pick = (table - mine) % count
    joined = jnp.concatenate(
        [jnp.stack(ahead_parts)[ahead_pick], jnp.stack(behind_parts)[behind_pick]], axis=1
    )
    return joined.reshape(count * 2 * half, ahead.shape[1]), tied


def shards(
    tokens,
    gain,
    w_query,
    b_query,
    key_weight,
    b_key,
    value_weight,
    value_bias,
    random_block_index,
    global_block_index,
):
    row_count = lax.axis_size("row")
    here = lax.axis_index("row")
    column = lax.axis_index("col")
    group = lax.axis_index("groups")
    passages, length, _ = tokens.shape
    heads_here = w_query.shape[1] // HEAD_SIZE
    pairs_here = key_weight.shape[1] // HEAD_SIZE
    passage_groups = heads_here // pairs_here
    per_device = length // BLOCK_TOKENS
    passage_blocks = row_count * per_device
    scale = 1.0 / math.sqrt(HEAD_SIZE)

    rotary_cols = (heads_here + pairs_here) * HEAD_SIZE
    split = rotary_cols // 2
    value_cols = pairs_here * HEAD_SIZE
    value_split = value_cols // 2
    rotary_w = jnp.concatenate([w_query, key_weight], axis=1)
    rotary_b = jnp.concatenate([b_query, b_key], axis=0)
    first = group == 0
    rows_here = w_query.shape[0]

    def panel_rows(start, stop):
        return jnp.concatenate(
            [
                lax.dynamic_slice_in_dim(rotary_w[start:stop], group * split, split, 1),
                lax.dynamic_slice_in_dim(
                    value_weight[start:stop], group * value_split, value_split, 1
                ),
            ],
            axis=1,
        )

    panel_bias = jnp.where(
        first,
        jnp.concatenate([rotary_b[:split], value_bias[:value_split]]),
        jnp.concatenate([rotary_b[split:], value_bias[value_split:]]),
    )

    def tokens_normed(first_arrival):
        other_half = lax.ppermute(tokens, "col", SWAP)
        late_tokens, _ = lax.optimization_barrier((tokens, first_arrival))
        partner_half = lax.ppermute(late_tokens, "groups", SWAP)
        partner_other = lax.ppermute(partner_half, "col", SWAP)
        whole = jnp.where(
            column == 0,
            jnp.concatenate([tokens, other_half], axis=2),
            jnp.concatenate([other_half, tokens], axis=2),
        )
        partner = jnp.where(
            column == 0,
            jnp.concatenate([partner_half, partner_other], axis=2),
            jnp.concatenate([partner_other, partner_half], axis=2),
        )
        both = jnp.concatenate([whole, partner], axis=0)
        widened = both.astype(jnp.float32)
        power = jnp.mean(widened * widened, axis=-1, keepdims=True)
        normed = (
            (widened * lax.rsqrt(power + norm_eps) * gain)
            .astype(jnp.bfloat16)
            .reshape(2 * passages * length, -1)
        )
        return normed

    full_panel, normed = gather_rows(
        panel_rows(0, rows_here // 2),
        panel_rows(rows_here // 2, rows_here),
        row_count,
        here,
        tokens_normed,
        row_count - 1,
    )
    token_positions = (here * length + jnp.arange(length, dtype=jnp.int32)).astype(jnp.float32)
    summed = jnp.dot(normed, full_panel, preferred_element_type=jnp.float32) + panel_bias
    summed = summed.reshape(2 * passages, length, split + value_split)
    turned = apply_rotation(
        summed[..., :split].reshape(2 * passages, length, split // HEAD_SIZE, HEAD_SIZE),
        token_positions,
    ).astype(jnp.bfloat16)
    result = jnp.concatenate(
        [turned.reshape(2 * passages, length, split), summed[..., split:].astype(jnp.bfloat16)],
        axis=-1,
    )
    mine = result[:passages]
    returned = lax.ppermute(result[passages:], "groups", SWAP)
    low = jnp.where(first, mine, returned)
    high = jnp.where(first, returned, mine)
    rotary_rows = jnp.concatenate([low[..., :split], high[..., :split]], axis=-1)
    query_rows = rotary_rows[..., : heads_here * HEAD_SIZE]
    key = rotary_rows[..., heads_here * HEAD_SIZE :]
    value_rows = jnp.concatenate([low[..., split:], high[..., split:]], axis=-1)

    pairs = jnp.concatenate([key, value_rows], axis=-1)
    if row_count == 8:
        order = snake_order(row_count)
        position = [0] * row_count
        for i, d in enumerate(order):
            position[d] = i
        forward = [(order[i], order[(i + 1) % row_count]) for i in range(row_count)]
        backward = [(order[i], order[(i - 1) % row_count]) for i in range(row_count)]
        ahead, behind = pairs, pairs
        ahead_parts, behind_parts = [], []
        for step in range(1, row_count // 2 + 1):
            ahead = lax.ppermute(ahead, "row", forward)
            ahead_parts.append(ahead)
            if step < row_count // 2:
                behind = lax.ppermute(behind, "row", backward)
                behind_parts.append(behind)
        gathered = jnp.stack([pairs] + ahead_parts + behind_parts)
        table = jnp.array(position, dtype=jnp.int32)
        delta = (table[here] - table) % row_count
        owner_slot = jnp.where(delta <= row_count // 2, delta, row_count // 2 + row_count - delta)
    else:
        gathered = lax.all_gather(pairs, "row", axis=0, tiled=False)
        owner_slot = jnp.arange(row_count, dtype=jnp.int32)
    gathered = gathered.reshape(
        row_count, passages, per_device, BLOCK_TOKENS, pairs_here, 2 * HEAD_SIZE
    )[:, :, :, :, 0]
    gathered = gathered.transpose(1, 0, 2, 3, 4).reshape(
        passages, passage_blocks, BLOCK_TOKENS, 2 * HEAD_SIZE
    )
    block_ids = jnp.arange(passage_blocks, dtype=jnp.int32)
    slot_of_block = owner_slot[block_ids // per_device] * per_device + block_ids % per_device
    kv_blocks = gathered[:, slot_of_block]

    local_blocks = here * per_device + jnp.arange(per_device, dtype=jnp.int32)
    nearby_blocks = local_blocks[:, None] + jnp.arange(3, dtype=jnp.int32)[None, :] - 1
    inside = (nearby_blocks >= 0) & (nearby_blocks < passage_blocks)
    nearby_clamped = jnp.clip(nearby_blocks, 0, passage_blocks - 1)
    passage_ids = jnp.arange(passages, dtype=jnp.int32)
    window = kv_blocks[passage_ids[:, None, None], nearby_clamped[None]]
    window = window.reshape(passages, per_device, 3 * BLOCK_TOKENS, 2 * HEAD_SIZE)

    global_here = lax.dynamic_slice_in_dim(global_block_index, column * pairs_here, pairs_here, 1)
    global_pairs = kv_blocks[passage_ids[:, None], global_here[:, 0, :]]
    global_pairs = global_pairs.reshape(passages, GLOBAL_BLOCKS * BLOCK_TOKENS, 2 * HEAD_SIZE)

    selected = lax.dynamic_slice_in_dim(random_block_index, column * heads_here, heads_here, 2)
    selected = lax.dynamic_slice_in_dim(selected, here * per_device, per_device, 1)
    arrived = kv_blocks[passage_ids[:, None, None, None], selected]
    arrived = arrived.reshape(
        passages, per_device, heads_here, RANDOM_BLOCKS * BLOCK_TOKENS, 2 * HEAD_SIZE
    )

    query_block_rows = query_rows.reshape(
        passages, per_device, BLOCK_TOKENS, heads_here, HEAD_SIZE
    )
    first_scores = jnp.einsum(
        "sqbgh,sqwh->sqgbw",
        query_block_rows,
        window[..., :HEAD_SIZE],
        preferred_element_type=jnp.float32,
    )
    second_scores = jnp.einsum(
        "sqbgh,swh->sqgbw",
        query_block_rows,
        global_pairs[..., :HEAD_SIZE],
        preferred_element_type=jnp.float32,
    )
    third_scores = jnp.einsum(
        "sqbgh,sqgwh->sqgbw",
        query_block_rows,
        arrived[..., :HEAD_SIZE],
        preferred_element_type=jnp.float32,
    )
    first_scores = first_scores * scale
    second_scores = second_scores * scale
    third_scores = third_scores * scale
    near_mask = jnp.repeat(inside, BLOCK_TOKENS, axis=1)
    first_scores = jnp.where(near_mask[None, :, None, None, :], first_scores, -jnp.inf)
    top = jnp.maximum(
        jnp.max(first_scores, axis=-1, keepdims=True),
        jnp.maximum(
            jnp.max(second_scores, axis=-1, keepdims=True),
            jnp.max(third_scores, axis=-1, keepdims=True),
        ),
    )
    near_weights = jnp.exp(first_scores - top)
    global_weights = jnp.exp(second_scores - top)
    random_weights = jnp.exp(third_scores - top)
    total = (
        jnp.sum(near_weights, axis=-1, keepdims=True)
        + jnp.sum(global_weights, axis=-1, keepdims=True)
        + jnp.sum(random_weights, axis=-1, keepdims=True)
    )
    near_probs = (near_weights / total).astype(jnp.bfloat16)
    global_probs = (global_weights / total).astype(jnp.bfloat16)
    random_probs = (random_weights / total).astype(jnp.bfloat16)
    mixed = jnp.einsum(
        "sqgbw,sqwh->sqbgh",
        near_probs,
        window[..., HEAD_SIZE:],
        preferred_element_type=jnp.float32,
    )
    mixed = mixed + jnp.einsum(
        "sqgbw,swh->sqbgh",
        global_probs,
        global_pairs[..., HEAD_SIZE:],
        preferred_element_type=jnp.float32,
    )
    mixed = mixed + jnp.einsum(
        "sqgbw,sqgwh->sqbgh",
        random_probs,
        arrived[..., HEAD_SIZE:],
        preferred_element_type=jnp.float32,
    )
    return mixed.reshape(passages, length, heads_here * HEAD_SIZE).astype(jnp.bfloat16)


def solution(mesh):
    placed = (
        P("groups", "row", "col"),
        P(),
        P("row", "col"),
        P("col"),
        P("row", "col"),
        P("col"),
        P("row", "col"),
        P("col"),
        P("groups", None, None, None),
        P("groups", None, None),
    )
    return jax.shard_map(
        shards, mesh=mesh, in_specs=placed, out_specs=P("groups", "row", "col"), check_vma=False
    )
```

```python
import math

import jax
import jax.numpy as jnp
from jax import lax
from jax.sharding import PartitionSpec as P

HEAD_SIZE = 128
BLOCK_TOKENS = 64
RANDOM_BLOCKS = 2
GLOBAL_BLOCKS = 2


rope_base = 1000000.0
norm_eps = 1e-06

SWAP = [(0, 1), (1, 0)]


def apply_rotation(values, token_positions):
    half = values.shape[-1] // 2
    freqs = 1.0 / rope_base ** (jnp.arange(half, dtype=jnp.float32) * 2.0 / values.shape[-1])
    angles = token_positions[:, None] * freqs[None, :]
    cosine = jnp.concatenate([jnp.cos(angles), jnp.cos(angles)], axis=-1)[None, :, None, :]
    sine = jnp.concatenate([jnp.sin(angles), jnp.sin(angles)], axis=-1)[None, :, None, :]
    turned = jnp.concatenate([-values[..., half:], values[..., :half]], axis=-1)
    return values * cosine + turned * sine


def snake_order(count):
    return [2 * z for z in range(count // 2)] + [2 * z + 1 for z in reversed(range(count // 2))]


def gather_rows(ahead, behind, count, here):
    if count != 8:
        shard = jnp.concatenate([ahead, behind], axis=0)
        return lax.all_gather(shard, "row", axis=0, tiled=True), ahead
    order = snake_order(count)
    position = [0] * count
    for i, d in enumerate(order):
        position[d] = i
    forward = [(order[i], order[(i + 1) % count]) for i in range(count)]
    backward = [(order[i], order[(i - 1) % count]) for i in range(count)]
    half = ahead.shape[0]
    ahead_parts, behind_parts = [ahead], [behind]
    for _ in range(count - 1):
        ahead = lax.ppermute(ahead, "row", forward)
        behind = lax.ppermute(behind, "row", backward)
        ahead_parts.append(ahead)
        behind_parts.append(behind)
    table = jnp.array(position, dtype=jnp.int32)
    mine = table[here]
    ahead_pick = (mine - table) % count
    behind_pick = (table - mine) % count
    joined = jnp.concatenate(
        [jnp.stack(ahead_parts)[ahead_pick], jnp.stack(behind_parts)[behind_pick]], axis=1
    )
    return joined.reshape(count * 2 * half, ahead.shape[1]), ahead_parts[1]


def shards(
    tokens,
    gain,
    w_query,
    b_query,
    key_weight,
    b_key,
    value_weight,
    value_bias,
    random_block_index,
    global_block_index,
):
    row_count = lax.axis_size("row")
    here = lax.axis_index("row")
    column = lax.axis_index("col")
    group = lax.axis_index("groups")
    passages, length, _ = tokens.shape
    heads_here = w_query.shape[1] // HEAD_SIZE
    pairs_here = key_weight.shape[1] // HEAD_SIZE
    passage_groups = heads_here // pairs_here
    per_device = length // BLOCK_TOKENS
    passage_blocks = row_count * per_device
    scale = 1.0 / math.sqrt(HEAD_SIZE)

    rotary_cols = (heads_here + pairs_here) * HEAD_SIZE
    split = rotary_cols // 2
    value_cols = pairs_here * HEAD_SIZE
    value_split = value_cols // 2
    rotary_w = jnp.concatenate([w_query, key_weight], axis=1)
    rotary_b = jnp.concatenate([b_query, b_key], axis=0)
    first = group == 0
    rows_here = w_query.shape[0]

    def panel_rows(start, stop):
        return jnp.concatenate(
            [
                lax.dynamic_slice_in_dim(rotary_w[start:stop], group * split, split, 1),
                lax.dynamic_slice_in_dim(
                    value_weight[start:stop], group * value_split, value_split, 1
                ),
            ],
            axis=1,
        )

    full_panel, first_arrival = gather_rows(
        panel_rows(0, rows_here // 2),
        panel_rows(rows_here // 2, rows_here),
        row_count,
        here,
    )
    panel_bias = jnp.where(
        first,
        jnp.concatenate([rotary_b[:split], value_bias[:value_split]]),
        jnp.concatenate([rotary_b[split:], value_bias[value_split:]]),
    )

    other_half = lax.ppermute(tokens, "col", SWAP)
    late_tokens, _ = lax.optimization_barrier((tokens, first_arrival))
    partner_half = lax.ppermute(late_tokens, "groups", SWAP)
    partner_other = lax.ppermute(partner_half, "col", SWAP)
    def in_feature_order(own, other):
        half = own.shape[2]
        placed = jnp.zeros(own.shape[:2] + (2 * half,), own.dtype)
        placed = lax.dynamic_update_slice(placed, own, (0, 0, column * half))
        return lax.dynamic_update_slice(placed, other, (0, 0, (1 - column) * half))

    whole = in_feature_order(tokens, other_half)
    partner = in_feature_order(partner_half, partner_other)
    both = jnp.concatenate([whole, partner], axis=0)
    widened = both.astype(jnp.float32)
    power = jnp.mean(widened * widened, axis=-1, keepdims=True)
    normed = (
        (widened * lax.rsqrt(power + norm_eps) * gain)
        .astype(jnp.bfloat16)
        .reshape(2 * passages * length, -1)
    )
    token_positions = (here * length + jnp.arange(length, dtype=jnp.int32)).astype(jnp.float32)

    summed = jnp.dot(normed, full_panel, preferred_element_type=jnp.float32) + panel_bias
    summed = summed.reshape(2 * passages, length, split + value_split)
    turned = apply_rotation(
        summed[..., :split].reshape(2 * passages, length, split // HEAD_SIZE, HEAD_SIZE),
        token_positions,
    ).astype(jnp.bfloat16)
    result = jnp.concatenate(
        [turned.reshape(2 * passages, length, split), summed[..., split:].astype(jnp.bfloat16)],
        axis=-1,
    )
    mine = result[:passages]
    returned = lax.ppermute(result[passages:], "groups", SWAP)
    low = jnp.where(first, mine, returned)
    high = jnp.where(first, returned, mine)
    rotary_rows = jnp.concatenate([low[..., :split], high[..., :split]], axis=-1)
    query_rows = rotary_rows[..., : heads_here * HEAD_SIZE]
    key = rotary_rows[..., heads_here * HEAD_SIZE :]
    value_rows = jnp.concatenate([low[..., split:], high[..., split:]], axis=-1)

    pairs = jnp.concatenate([key, value_rows], axis=-1)
    if row_count == 8:
        order = snake_order(row_count)
        position = [0] * row_count
        for i, d in enumerate(order):
            position[d] = i
        forward = [(order[i], order[(i + 1) % row_count]) for i in range(row_count)]
        backward = [(order[i], order[(i - 1) % row_count]) for i in range(row_count)]
        ahead, behind = pairs, pairs
        ahead_parts, behind_parts = [], []
        for step in range(1, row_count // 2 + 1):
            ahead = lax.ppermute(ahead, "row", forward)
            ahead_parts.append(ahead)
            if step < row_count // 2:
                behind = lax.ppermute(behind, "row", backward)
                behind_parts.append(behind)
        gathered = jnp.stack([pairs] + ahead_parts + behind_parts)
        table = jnp.array(position, dtype=jnp.int32)
        delta = (table[here] - table) % row_count
        owner_slot = jnp.where(delta <= row_count // 2, delta, row_count // 2 + row_count - delta)
    else:
        gathered = lax.all_gather(pairs, "row", axis=0, tiled=False)
        owner_slot = jnp.arange(row_count, dtype=jnp.int32)
    gathered = gathered.reshape(
        row_count, passages, per_device, BLOCK_TOKENS, pairs_here, 2 * HEAD_SIZE
    )[:, :, :, :, 0]
    gathered = gathered.transpose(1, 0, 2, 3, 4).reshape(
        passages, passage_blocks, BLOCK_TOKENS, 2 * HEAD_SIZE
    )
    block_ids = jnp.arange(passage_blocks, dtype=jnp.int32)
    slot_of_block = owner_slot[block_ids // per_device] * per_device + block_ids % per_device
    kv_blocks = gathered[:, slot_of_block]

    local_blocks = here * per_device + jnp.arange(per_device, dtype=jnp.int32)
    nearby_blocks = local_blocks[:, None] + jnp.arange(3, dtype=jnp.int32)[None, :] - 1
    inside = (nearby_blocks >= 0) & (nearby_blocks < passage_blocks)
    nearby_clamped = jnp.clip(nearby_blocks, 0, passage_blocks - 1)
    passage_ids = jnp.arange(passages, dtype=jnp.int32)
    window = kv_blocks[passage_ids[:, None, None], nearby_clamped[None]]
    window = window.reshape(passages, per_device, 3 * BLOCK_TOKENS, 2 * HEAD_SIZE)

    global_here = lax.dynamic_slice_in_dim(global_block_index, column * pairs_here, pairs_here, 1)
    global_pairs = kv_blocks[passage_ids[:, None], global_here[:, 0, :]]
    global_pairs = global_pairs.reshape(passages, GLOBAL_BLOCKS * BLOCK_TOKENS, 2 * HEAD_SIZE)

    selected = lax.dynamic_slice_in_dim(random_block_index, column * heads_here, heads_here, 2)
    selected = lax.dynamic_slice_in_dim(selected, here * per_device, per_device, 1)
    arrived = kv_blocks[passage_ids[:, None, None, None], selected]
    arrived = arrived.reshape(
        passages, per_device, heads_here, RANDOM_BLOCKS * BLOCK_TOKENS, 2 * HEAD_SIZE
    )

    query_block_rows = query_rows.reshape(
        passages, per_device, BLOCK_TOKENS, heads_here, HEAD_SIZE
    )
    first_scores = jnp.einsum(
        "sqbgh,sqwh->sqgbw",
        query_block_rows,
        window[..., :HEAD_SIZE],
        preferred_element_type=jnp.float32,
    )
    second_scores = jnp.einsum(
        "sqbgh,swh->sqgbw",
        query_block_rows,
        global_pairs[..., :HEAD_SIZE],
        preferred_element_type=jnp.float32,
    )
    third_scores = jnp.einsum(
        "sqbgh,sqgwh->sqgbw",
        query_block_rows,
        arrived[..., :HEAD_SIZE],
        preferred_element_type=jnp.float32,
    )
    first_scores = first_scores * scale
    second_scores = second_scores * scale
    third_scores = third_scores * scale
    near_mask = jnp.repeat(inside, BLOCK_TOKENS, axis=1)
    first_scores = jnp.where(near_mask[None, :, None, None, :], first_scores, -jnp.inf)
    top = jnp.maximum(
        jnp.max(first_scores, axis=-1, keepdims=True),
        jnp.maximum(
            jnp.max(second_scores, axis=-1, keepdims=True),
            jnp.max(third_scores, axis=-1, keepdims=True),
        ),
    )
    near_weights = jnp.exp(first_scores - top)
    global_weights = jnp.exp(second_scores - top)
    random_weights = jnp.exp(third_scores - top)
    total = (
        jnp.sum(near_weights, axis=-1, keepdims=True)
        + jnp.sum(global_weights, axis=-1, keepdims=True)
        + jnp.sum(random_weights, axis=-1, keepdims=True)
    )
    near_probs = (near_weights / total).astype(jnp.bfloat16)
    global_probs = (global_weights / total).astype(jnp.bfloat16)
    random_probs = (random_weights / total).astype(jnp.bfloat16)
    mixed = jnp.einsum(
        "sqgbw,sqwh->sqbgh",
        near_probs,
        window[..., HEAD_SIZE:],
        preferred_element_type=jnp.float32,
    )
    mixed = mixed + jnp.einsum(
        "sqgbw,swh->sqbgh",
        global_probs,
        global_pairs[..., HEAD_SIZE:],
        preferred_element_type=jnp.float32,
    )
    mixed = mixed + jnp.einsum(
        "sqgbw,sqgwh->sqbgh",
        random_probs,
        arrived[..., HEAD_SIZE:],
        preferred_element_type=jnp.float32,
    )
    return mixed.reshape(passages, length, heads_here * HEAD_SIZE).astype(jnp.bfloat16)


def solution(mesh):
    placed = (
        P("groups", "row", "col"),
        P(),
        P("row", "col"),
        P("col"),
        P("row", "col"),
        P("col"),
        P("row", "col"),
        P("col"),
        P("groups", None, None, None),
        P("groups", None, None),
    )
    return jax.shard_map(
        shards, mesh=mesh, in_specs=placed, out_specs=P("groups", "row", "col"), check_vma=False
    )
```

```python
import math

import jax
import jax.numpy as jnp
from jax import lax
from jax.sharding import PartitionSpec as P

HEAD_SIZE = 128
BLOCK_TOKENS = 64
RANDOM_BLOCKS = 2
GLOBAL_BLOCKS = 2


rope_base = 1000000.0
norm_eps = 1e-06

SWAP = [(0, 1), (1, 0)]


def apply_rotation(values, token_positions):
    half = values.shape[-1] // 2
    freqs = 1.0 / rope_base ** (jnp.arange(half, dtype=jnp.float32) * 2.0 / values.shape[-1])
    angles = token_positions[:, None] * freqs[None, :]
    cosine = jnp.concatenate([jnp.cos(angles), jnp.cos(angles)], axis=-1)[None, :, None, :]
    sine = jnp.concatenate([jnp.sin(angles), jnp.sin(angles)], axis=-1)[None, :, None, :]
    turned = jnp.concatenate([-values[..., half:], values[..., :half]], axis=-1)
    return values * cosine + turned * sine


def snake_order(count):
    return [2 * z for z in range(count // 2)] + [2 * z + 1 for z in reversed(range(count // 2))]


def gather_rows(ahead, behind, count, here):
    if count != 8:
        shard = jnp.concatenate([ahead, behind], axis=0)
        return lax.all_gather(shard, "row", axis=0, tiled=True), ahead
    order = snake_order(count)
    position = [0] * count
    for i, d in enumerate(order):
        position[d] = i
    forward = [(order[i], order[(i + 1) % count]) for i in range(count)]
    backward = [(order[i], order[(i - 1) % count]) for i in range(count)]
    half = ahead.shape[0]
    ahead_parts, behind_parts = [ahead], [behind]
    for _ in range(count - 1):
        ahead = lax.ppermute(ahead, "row", forward)
        behind = lax.ppermute(behind, "row", backward)
        ahead_parts.append(ahead)
        behind_parts.append(behind)
    table = jnp.array(position, dtype=jnp.int32)
    mine = table[here]
    ahead_pick = (mine - table) % count
    behind_pick = (table - mine) % count
    joined = jnp.concatenate(
        [jnp.stack(ahead_parts)[ahead_pick], jnp.stack(behind_parts)[behind_pick]], axis=1
    )
    return joined.reshape(count * 2 * half, ahead.shape[1]), ahead_parts[1]


def shards(
    tokens,
    gain,
    w_query,
    b_query,
    key_weight,
    b_key,
    value_weight,
    value_bias,
    random_block_index,
    global_block_index,
):
    row_count = lax.axis_size("row")
    here = lax.axis_index("row")
    column = lax.axis_index("col")
    group = lax.axis_index("groups")
    passages, length, _ = tokens.shape
    heads_here = w_query.shape[1] // HEAD_SIZE
    pairs_here = key_weight.shape[1] // HEAD_SIZE
    passage_groups = heads_here // pairs_here
    per_device = length // BLOCK_TOKENS
    passage_blocks = row_count * per_device
    scale = 1.0 / math.sqrt(HEAD_SIZE)

    rotary_cols = (heads_here + pairs_here) * HEAD_SIZE
    split = rotary_cols // 2
    value_cols = pairs_here * HEAD_SIZE
    value_split = value_cols // 2
    rotary_w = jnp.concatenate([w_query, key_weight], axis=1)
    rotary_b = jnp.concatenate([b_query, b_key], axis=0)
    first = group == 0
    rows_here = w_query.shape[0]

    def panel_rows(start, stop):
        return jnp.concatenate(
            [
                lax.dynamic_slice_in_dim(rotary_w[start:stop], group * split, split, 1),
                lax.dynamic_slice_in_dim(
                    value_weight[start:stop], group * value_split, value_split, 1
                ),
            ],
            axis=1,
        )

    full_panel, first_arrival = gather_rows(
        panel_rows(0, rows_here // 2),
        panel_rows(rows_here // 2, rows_here),
        row_count,
        here,
    )
    panel_bias = jnp.where(
        first,
        jnp.concatenate([rotary_b[:split], value_bias[:value_split]]),
        jnp.concatenate([rotary_b[split:], value_bias[value_split:]]),
    )

    late_tokens, _ = lax.optimization_barrier((tokens, first_arrival))
    partner_half = lax.ppermute(late_tokens, "groups", SWAP)
    halves = jnp.concatenate([tokens, partner_half], axis=0)
    other_halves = lax.ppermute(halves, "col", SWAP)
    both = jnp.where(
        column == 0,
        jnp.concatenate([halves, other_halves], axis=2),
        jnp.concatenate([other_halves, halves], axis=2),
    )
    widened = both.astype(jnp.float32)
    power = jnp.mean(widened * widened, axis=-1, keepdims=True)
    normed = (
        (widened * lax.rsqrt(power + norm_eps) * gain)
        .astype(jnp.bfloat16)
        .reshape(2 * passages * length, -1)
    )
    token_positions = (here * length + jnp.arange(length, dtype=jnp.int32)).astype(jnp.float32)

    summed = jnp.dot(normed, full_panel, preferred_element_type=jnp.float32) + panel_bias
    summed = summed.reshape(2 * passages, length, split + value_split)
    turned = apply_rotation(
        summed[..., :split].reshape(2 * passages, length, split // HEAD_SIZE, HEAD_SIZE),
        token_positions,
    ).astype(jnp.bfloat16)
    result = jnp.concatenate(
        [turned.reshape(2 * passages, length, split), summed[..., split:].astype(jnp.bfloat16)],
        axis=-1,
    )
    mine = result[:passages]
    returned = lax.ppermute(result[passages:], "groups", SWAP)
    low = jnp.where(first, mine, returned)
    high = jnp.where(first, returned, mine)
    rotary_rows = jnp.concatenate([low[..., :split], high[..., :split]], axis=-1)
    query_rows = rotary_rows[..., : heads_here * HEAD_SIZE]
    key = rotary_rows[..., heads_here * HEAD_SIZE :]
    value_rows = jnp.concatenate([low[..., split:], high[..., split:]], axis=-1)

    pairs = jnp.concatenate([key, value_rows], axis=-1)
    if row_count == 8:
        order = snake_order(row_count)
        position = [0] * row_count
        for i, d in enumerate(order):
            position[d] = i
        forward = [(order[i], order[(i + 1) % row_count]) for i in range(row_count)]
        backward = [(order[i], order[(i - 1) % row_count]) for i in range(row_count)]
        ahead, behind = pairs, pairs
        ahead_parts, behind_parts = [], []
        for step in range(1, row_count // 2 + 1):
            ahead = lax.ppermute(ahead, "row", forward)
            ahead_parts.append(ahead)
            if step < row_count // 2:
                behind = lax.ppermute(behind, "row", backward)
                behind_parts.append(behind)
        gathered = jnp.stack([pairs] + ahead_parts + behind_parts)
        table = jnp.array(position, dtype=jnp.int32)
        delta = (table[here] - table) % row_count
        owner_slot = jnp.where(delta <= row_count // 2, delta, row_count // 2 + row_count - delta)
    else:
        gathered = lax.all_gather(pairs, "row", axis=0, tiled=False)
        owner_slot = jnp.arange(row_count, dtype=jnp.int32)
    gathered = gathered.reshape(
        row_count, passages, per_device, BLOCK_TOKENS, pairs_here, 2 * HEAD_SIZE
    )[:, :, :, :, 0]
    gathered = gathered.transpose(1, 0, 2, 3, 4).reshape(
        passages, passage_blocks, BLOCK_TOKENS, 2 * HEAD_SIZE
    )
    block_ids = jnp.arange(passage_blocks, dtype=jnp.int32)
    slot_of_block = owner_slot[block_ids // per_device] * per_device + block_ids % per_device
    kv_blocks = gathered[:, slot_of_block]

    local_blocks = here * per_device + jnp.arange(per_device, dtype=jnp.int32)
    nearby_blocks = local_blocks[:, None] + jnp.arange(3, dtype=jnp.int32)[None, :] - 1
    inside = (nearby_blocks >= 0) & (nearby_blocks < passage_blocks)
    nearby_clamped = jnp.clip(nearby_blocks, 0, passage_blocks - 1)
    passage_ids = jnp.arange(passages, dtype=jnp.int32)
    window = kv_blocks[passage_ids[:, None, None], nearby_clamped[None]]
    window = window.reshape(passages, per_device, 3 * BLOCK_TOKENS, 2 * HEAD_SIZE)

    global_here = lax.dynamic_slice_in_dim(global_block_index, column * pairs_here, pairs_here, 1)
    global_pairs = kv_blocks[passage_ids[:, None], global_here[:, 0, :]]
    global_pairs = global_pairs.reshape(passages, GLOBAL_BLOCKS * BLOCK_TOKENS, 2 * HEAD_SIZE)

    selected = lax.dynamic_slice_in_dim(random_block_index, column * heads_here, heads_here, 2)
    selected = lax.dynamic_slice_in_dim(selected, here * per_device, per_device, 1)
    arrived = kv_blocks[passage_ids[:, None, None, None], selected]
    arrived = arrived.reshape(
        passages, per_device, heads_here, RANDOM_BLOCKS * BLOCK_TOKENS, 2 * HEAD_SIZE
    )

    query_block_rows = query_rows.reshape(
        passages, per_device, BLOCK_TOKENS, heads_here, HEAD_SIZE
    )
    first_scores = jnp.einsum(
        "sqbgh,sqwh->sqgbw",
        query_block_rows,
        window[..., :HEAD_SIZE],
        preferred_element_type=jnp.float32,
    )
    second_scores = jnp.einsum(
        "sqbgh,swh->sqgbw",
        query_block_rows,
        global_pairs[..., :HEAD_SIZE],
        preferred_element_type=jnp.float32,
    )
    third_scores = jnp.einsum(
        "sqbgh,sqgwh->sqgbw",
        query_block_rows,
        arrived[..., :HEAD_SIZE],
        preferred_element_type=jnp.float32,
    )
    first_scores = first_scores * scale
    second_scores = second_scores * scale
    third_scores = third_scores * scale
    near_mask = jnp.repeat(inside, BLOCK_TOKENS, axis=1)
    first_scores = jnp.where(near_mask[None, :, None, None, :], first_scores, -jnp.inf)
    top = jnp.maximum(
        jnp.max(first_scores, axis=-1, keepdims=True),
        jnp.maximum(
            jnp.max(second_scores, axis=-1, keepdims=True),
            jnp.max(third_scores, axis=-1, keepdims=True),
        ),
    )
    near_weights = jnp.exp(first_scores - top)
    global_weights = jnp.exp(second_scores - top)
    random_weights = jnp.exp(third_scores - top)
    total = (
        jnp.sum(near_weights, axis=-1, keepdims=True)
        + jnp.sum(global_weights, axis=-1, keepdims=True)
        + jnp.sum(random_weights, axis=-1, keepdims=True)
    )
    near_probs = (near_weights / total).astype(jnp.bfloat16)
    global_probs = (global_weights / total).astype(jnp.bfloat16)
    random_probs = (random_weights / total).astype(jnp.bfloat16)
    mixed = jnp.einsum(
        "sqgbw,sqwh->sqbgh",
        near_probs,
        window[..., HEAD_SIZE:],
        preferred_element_type=jnp.float32,
    )
    mixed = mixed + jnp.einsum(
        "sqgbw,swh->sqbgh",
        global_probs,
        global_pairs[..., HEAD_SIZE:],
        preferred_element_type=jnp.float32,
    )
    mixed = mixed + jnp.einsum(
        "sqgbw,sqgwh->sqbgh",
        random_probs,
        arrived[..., HEAD_SIZE:],
        preferred_element_type=jnp.float32,
    )
    return mixed.reshape(passages, length, heads_here * HEAD_SIZE).astype(jnp.bfloat16)


def solution(mesh):
    placed = (
        P("groups", "row", "col"),
        P(),
        P("row", "col"),
        P("col"),
        P("row", "col"),
        P("col"),
        P("row", "col"),
        P("col"),
        P("groups", None, None, None),
        P("groups", None, None),
    )
    return jax.shard_map(
        shards, mesh=mesh, in_specs=placed, out_specs=P("groups", "row", "col"), check_vma=False
    )
```

```python
import math

import jax
import jax.numpy as jnp
from jax import lax
from jax.sharding import PartitionSpec as P

HEAD_SIZE = 128
BLOCK_TOKENS = 64
RANDOM_BLOCKS = 2
GLOBAL_BLOCKS = 2


rope_base = 1000000.0
norm_eps = 1e-06

SWAP = [(0, 1), (1, 0)]


def apply_rotation(values, token_positions):
    half = values.shape[-1] // 2
    freqs = 1.0 / rope_base ** (jnp.arange(half, dtype=jnp.float32) * 2.0 / values.shape[-1])
    angles = token_positions[:, None] * freqs[None, :]
    cosine = jnp.concatenate([jnp.cos(angles), jnp.cos(angles)], axis=-1)[None, :, None, :]
    sine = jnp.concatenate([jnp.sin(angles), jnp.sin(angles)], axis=-1)[None, :, None, :]
    turned = jnp.concatenate([-values[..., half:], values[..., :half]], axis=-1)
    return values * cosine + turned * sine


def snake_order(count):
    return [2 * z for z in range(count // 2)] + [2 * z + 1 for z in reversed(range(count // 2))]


def gather_rows(ahead, behind, count, here):
    if count != 8:
        shard = jnp.concatenate([ahead, behind], axis=0)
        return lax.all_gather(shard, "row", axis=0, tiled=True), ahead
    order = snake_order(count)
    position = [0] * count
    for i, d in enumerate(order):
        position[d] = i
    forward = [(order[i], order[(i + 1) % count]) for i in range(count)]
    backward = [(order[i], order[(i - 1) % count]) for i in range(count)]
    half = ahead.shape[0]
    ahead_parts, behind_parts = [ahead], [behind]
    for _ in range(count - 1):
        ahead = lax.ppermute(ahead, "row", forward)
        behind = lax.ppermute(behind, "row", backward)
        ahead_parts.append(ahead)
        behind_parts.append(behind)
    table = jnp.array(position, dtype=jnp.int32)
    mine = table[here]
    ahead_pick = (mine - table) % count
    behind_pick = (table - mine) % count
    joined = jnp.concatenate(
        [jnp.stack(ahead_parts)[ahead_pick], jnp.stack(behind_parts)[behind_pick]], axis=1
    )
    return joined.reshape(count * 2 * half, ahead.shape[1]), ahead_parts[1]


def shards(
    tokens,
    gain,
    w_query,
    b_query,
    key_weight,
    b_key,
    value_weight,
    value_bias,
    random_block_index,
    global_block_index,
):
    row_count = lax.axis_size("row")
    here = lax.axis_index("row")
    column = lax.axis_index("col")
    group = lax.axis_index("groups")
    passages, length, _ = tokens.shape
    heads_here = w_query.shape[1] // HEAD_SIZE
    pairs_here = key_weight.shape[1] // HEAD_SIZE
    passage_groups = heads_here // pairs_here
    per_device = length // BLOCK_TOKENS
    passage_blocks = row_count * per_device
    scale = 1.0 / math.sqrt(HEAD_SIZE)

    rotary_cols = (heads_here + pairs_here) * HEAD_SIZE
    split = rotary_cols // 2
    value_cols = pairs_here * HEAD_SIZE
    value_split = value_cols // 2
    rotary_w = jnp.concatenate([w_query, key_weight], axis=1)
    rotary_b = jnp.concatenate([b_query, b_key], axis=0)
    first = group == 0
    rows_here = w_query.shape[0]

    def panel_rows(start, stop):
        return jnp.concatenate(
            [
                lax.dynamic_slice_in_dim(rotary_w[start:stop], group * split, split, 1),
                lax.dynamic_slice_in_dim(
                    value_weight[start:stop], group * value_split, value_split, 1
                ),
            ],
            axis=1,
        )

    full_panel, first_arrival = gather_rows(
        panel_rows(0, rows_here // 2),
        panel_rows(rows_here // 2, rows_here),
        row_count,
        here,
    )
    panel_bias = jnp.where(
        first,
        jnp.concatenate([rotary_b[:split], value_bias[:value_split]]),
        jnp.concatenate([rotary_b[split:], value_bias[value_split:]]),
    )

    other_half = lax.ppermute(tokens, "col", SWAP)
    late_tokens, _ = lax.optimization_barrier((tokens, first_arrival))
    partner_half = lax.ppermute(late_tokens, "groups", SWAP)
    partner_other = lax.ppermute(partner_half, "col", SWAP)
    whole = jnp.where(
        column == 0,
        jnp.concatenate([tokens, other_half], axis=2),
        jnp.concatenate([other_half, tokens], axis=2),
    )
    partner = jnp.where(
        column == 0,
        jnp.concatenate([partner_half, partner_other], axis=2),
        jnp.concatenate([partner_other, partner_half], axis=2),
    )
    both = jnp.concatenate([whole, partner], axis=0)
    widened = both.astype(jnp.float32)
    power = jnp.mean(widened * widened, axis=-1, keepdims=True)
    normed = (
        (widened * lax.rsqrt(power + norm_eps) * gain)
        .astype(jnp.bfloat16)
        .reshape(2 * passages * length, -1)
    )
    token_positions = (here * length + jnp.arange(length, dtype=jnp.int32)).astype(jnp.float32)

    lead = split - HEAD_SIZE

    def project(columns, bias, rotary_heads):
        summed = jnp.dot(normed, columns, preferred_element_type=jnp.float32) + bias
        summed = summed.reshape(2 * passages, length, -1)
        width = rotary_heads * HEAD_SIZE
        turned = apply_rotation(
            summed[..., :width].reshape(2 * passages, length, rotary_heads, HEAD_SIZE),
            token_positions,
        ).astype(jnp.bfloat16)
        return jnp.concatenate(
            [turned.reshape(2 * passages, length, width), summed[..., width:].astype(jnp.bfloat16)],
            axis=-1,
        )

    result_kv = project(full_panel[:, lead:], panel_bias[lead:], 1)
    returned_kv = lax.ppermute(result_kv[passages:], "groups", SWAP)
    result_q = project(full_panel[:, :lead], panel_bias[:lead], lead // HEAD_SIZE)
    returned_q = lax.ppermute(result_q[passages:], "groups", SWAP)
    mine_kv, mine_q = result_kv[:passages], result_q[:passages]
    low_kv = jnp.where(first, mine_kv, returned_kv)
    high_kv = jnp.where(first, returned_kv, mine_kv)
    key = high_kv[..., :HEAD_SIZE]
    value_rows = jnp.concatenate([low_kv[..., HEAD_SIZE:], high_kv[..., HEAD_SIZE:]], axis=-1)
    low_q = jnp.where(first, mine_q, returned_q)
    high_q = jnp.where(first, returned_q, mine_q)
    query_rows = jnp.concatenate([low_q, low_kv[..., :HEAD_SIZE], high_q], axis=-1)

    pairs = jnp.concatenate([key, value_rows], axis=-1)
    if row_count == 8:
        order = snake_order(row_count)
        position = [0] * row_count
        for i, d in enumerate(order):
            position[d] = i
        forward = [(order[i], order[(i + 1) % row_count]) for i in range(row_count)]
        backward = [(order[i], order[(i - 1) % row_count]) for i in range(row_count)]
        ahead, behind = pairs, pairs
        ahead_parts, behind_parts = [], []
        for step in range(1, row_count // 2 + 1):
            ahead = lax.ppermute(ahead, "row", forward)
            ahead_parts.append(ahead)
            if step < row_count // 2:
                behind = lax.ppermute(behind, "row", backward)
                behind_parts.append(behind)
        gathered = jnp.stack([pairs] + ahead_parts + behind_parts)
        table = jnp.array(position, dtype=jnp.int32)
        delta = (table[here] - table) % row_count
        owner_slot = jnp.where(delta <= row_count // 2, delta, row_count // 2 + row_count - delta)
    else:
        gathered = lax.all_gather(pairs, "row", axis=0, tiled=False)
        owner_slot = jnp.arange(row_count, dtype=jnp.int32)
    gathered = gathered.reshape(
        row_count, passages, per_device, BLOCK_TOKENS, pairs_here, 2 * HEAD_SIZE
    )[:, :, :, :, 0]
    gathered = gathered.transpose(1, 0, 2, 3, 4).reshape(
        passages, passage_blocks, BLOCK_TOKENS, 2 * HEAD_SIZE
    )
    block_ids = jnp.arange(passage_blocks, dtype=jnp.int32)
    slot_of_block = owner_slot[block_ids // per_device] * per_device + block_ids % per_device
    kv_blocks = gathered[:, slot_of_block]

    local_blocks = here * per_device + jnp.arange(per_device, dtype=jnp.int32)
    nearby_blocks = local_blocks[:, None] + jnp.arange(3, dtype=jnp.int32)[None, :] - 1
    inside = (nearby_blocks >= 0) & (nearby_blocks < passage_blocks)
    nearby_clamped = jnp.clip(nearby_blocks, 0, passage_blocks - 1)
    passage_ids = jnp.arange(passages, dtype=jnp.int32)
    window = kv_blocks[passage_ids[:, None, None], nearby_clamped[None]]
    window = window.reshape(passages, per_device, 3 * BLOCK_TOKENS, 2 * HEAD_SIZE)

    global_here = lax.dynamic_slice_in_dim(global_block_index, column * pairs_here, pairs_here, 1)
    global_pairs = kv_blocks[passage_ids[:, None], global_here[:, 0, :]]
    global_pairs = global_pairs.reshape(passages, GLOBAL_BLOCKS * BLOCK_TOKENS, 2 * HEAD_SIZE)

    selected = lax.dynamic_slice_in_dim(random_block_index, column * heads_here, heads_here, 2)
    selected = lax.dynamic_slice_in_dim(selected, here * per_device, per_device, 1)
    arrived = kv_blocks[passage_ids[:, None, None, None], selected]
    arrived = arrived.reshape(
        passages, per_device, heads_here, RANDOM_BLOCKS * BLOCK_TOKENS, 2 * HEAD_SIZE
    )

    query_block_rows = query_rows.reshape(
        passages, per_device, BLOCK_TOKENS, heads_here, HEAD_SIZE
    )
    first_scores = jnp.einsum(
        "sqbgh,sqwh->sqgbw",
        query_block_rows,
        window[..., :HEAD_SIZE],
        preferred_element_type=jnp.float32,
    )
    second_scores = jnp.einsum(
        "sqbgh,swh->sqgbw",
        query_block_rows,
        global_pairs[..., :HEAD_SIZE],
        preferred_element_type=jnp.float32,
    )
    third_scores = jnp.einsum(
        "sqbgh,sqgwh->sqgbw",
        query_block_rows,
        arrived[..., :HEAD_SIZE],
        preferred_element_type=jnp.float32,
    )
    first_scores = first_scores * scale
    second_scores = second_scores * scale
    third_scores = third_scores * scale
    near_mask = jnp.repeat(inside, BLOCK_TOKENS, axis=1)
    first_scores = jnp.where(near_mask[None, :, None, None, :], first_scores, -jnp.inf)
    top = jnp.maximum(
        jnp.max(first_scores, axis=-1, keepdims=True),
        jnp.maximum(
            jnp.max(second_scores, axis=-1, keepdims=True),
            jnp.max(third_scores, axis=-1, keepdims=True),
        ),
    )
    near_weights = jnp.exp(first_scores - top)
    global_weights = jnp.exp(second_scores - top)
    random_weights = jnp.exp(third_scores - top)
    total = (
        jnp.sum(near_weights, axis=-1, keepdims=True)
        + jnp.sum(global_weights, axis=-1, keepdims=True)
        + jnp.sum(random_weights, axis=-1, keepdims=True)
    )
    near_probs = (near_weights / total).astype(jnp.bfloat16)
    global_probs = (global_weights / total).astype(jnp.bfloat16)
    random_probs = (random_weights / total).astype(jnp.bfloat16)
    mixed = jnp.einsum(
        "sqgbw,sqwh->sqbgh",
        near_probs,
        window[..., HEAD_SIZE:],
        preferred_element_type=jnp.float32,
    )
    mixed = mixed + jnp.einsum(
        "sqgbw,swh->sqbgh",
        global_probs,
        global_pairs[..., HEAD_SIZE:],
        preferred_element_type=jnp.float32,
    )
    mixed = mixed + jnp.einsum(
        "sqgbw,sqgwh->sqbgh",
        random_probs,
        arrived[..., HEAD_SIZE:],
        preferred_element_type=jnp.float32,
    )
    return mixed.reshape(passages, length, heads_here * HEAD_SIZE).astype(jnp.bfloat16)


def solution(mesh):
    placed = (
        P("groups", "row", "col"),
        P(),
        P("row", "col"),
        P("col"),
        P("row", "col"),
        P("col"),
        P("row", "col"),
        P("col"),
        P("groups", None, None, None),
        P("groups", None, None),
    )
    return jax.shard_map(
        shards, mesh=mesh, in_specs=placed, out_specs=P("groups", "row", "col"), check_vma=False
    )
```

```python
import math

import jax
import jax.numpy as jnp
from jax import lax
from jax.sharding import PartitionSpec as P

HEAD_SIZE = 128
BLOCK_TOKENS = 64
RANDOM_BLOCKS = 2
GLOBAL_BLOCKS = 2


rope_base = 1000000.0
norm_eps = 1e-06

SWAP = [(0, 1), (1, 0)]


def apply_rotation(values, token_positions):
    half = values.shape[-1] // 2
    freqs = 1.0 / rope_base ** (jnp.arange(half, dtype=jnp.float32) * 2.0 / values.shape[-1])
    angles = token_positions[:, None] * freqs[None, :]
    cosine = jnp.concatenate([jnp.cos(angles), jnp.cos(angles)], axis=-1)[None, :, None, :]
    sine = jnp.concatenate([jnp.sin(angles), jnp.sin(angles)], axis=-1)[None, :, None, :]
    turned = jnp.concatenate([-values[..., half:], values[..., :half]], axis=-1)
    return values * cosine + turned * sine


def snake_order(count):
    return [2 * z for z in range(count // 2)] + [2 * z + 1 for z in reversed(range(count // 2))]


def gather_rows(ahead, behind, count, here):
    if count != 8:
        shard = jnp.concatenate([ahead, behind], axis=0)
        return lax.all_gather(shard, "row", axis=0, tiled=True), ahead
    order = snake_order(count)
    position = [0] * count
    for i, d in enumerate(order):
        position[d] = i
    forward = [(order[i], order[(i + 1) % count]) for i in range(count)]
    backward = [(order[i], order[(i - 1) % count]) for i in range(count)]
    half = ahead.shape[0]
    ahead_parts, behind_parts = [ahead], [behind]
    for _ in range(count - 1):
        ahead = lax.ppermute(ahead, "row", forward)
        behind = lax.ppermute(behind, "row", backward)
        ahead_parts.append(ahead)
        behind_parts.append(behind)
    table = jnp.array(position, dtype=jnp.int32)
    mine = table[here]
    ahead_pick = (mine - table) % count
    behind_pick = (table - mine) % count
    joined = jnp.concatenate(
        [jnp.stack(ahead_parts)[ahead_pick], jnp.stack(behind_parts)[behind_pick]], axis=1
    )
    return joined.reshape(count * 2 * half, ahead.shape[1]), ahead_parts[1]


def shards(
    tokens,
    gain,
    w_query,
    b_query,
    key_weight,
    b_key,
    value_weight,
    value_bias,
    random_block_index,
    global_block_index,
):
    row_count = lax.axis_size("row")
    here = lax.axis_index("row")
    column = lax.axis_index("col")
    group = lax.axis_index("groups")
    passages, length, _ = tokens.shape
    heads_here = w_query.shape[1] // HEAD_SIZE
    pairs_here = key_weight.shape[1] // HEAD_SIZE
    passage_groups = heads_here // pairs_here
    per_device = length // BLOCK_TOKENS
    passage_blocks = row_count * per_device
    scale = 1.0 / math.sqrt(HEAD_SIZE)

    rotary_cols = (heads_here + pairs_here) * HEAD_SIZE
    split = rotary_cols // 2
    value_cols = pairs_here * HEAD_SIZE
    value_split = value_cols // 2
    rotary_w = jnp.concatenate([w_query, key_weight], axis=1)
    rotary_b = jnp.concatenate([b_query, b_key], axis=0)
    first = group == 0
    rows_here = w_query.shape[0]

    def panel_rows(start, stop):
        rotary_rows, value_rows_w = rotary_w[start:stop], value_weight[start:stop]
        return jnp.where(
            first,
            jnp.concatenate([rotary_rows[:, :split], value_rows_w[:, :value_split]], axis=1),
            jnp.concatenate([rotary_rows[:, split:], value_rows_w[:, value_split:]], axis=1),
        )

    full_panel, first_arrival = gather_rows(
        panel_rows(0, rows_here // 2),
        panel_rows(rows_here // 2, rows_here),
        row_count,
        here,
    )
    panel_bias = jnp.where(
        first,
        jnp.concatenate([rotary_b[:split], value_bias[:value_split]]),
        jnp.concatenate([rotary_b[split:], value_bias[value_split:]]),
    )

    other_half = lax.ppermute(tokens, "col", SWAP)
    late_tokens, _ = lax.optimization_barrier((tokens, first_arrival))
    partner_half = lax.ppermute(late_tokens, "groups", SWAP)
    partner_other = lax.ppermute(partner_half, "col", SWAP)
    whole = jnp.where(
        column == 0,
        jnp.concatenate([tokens, other_half], axis=2),
        jnp.concatenate([other_half, tokens], axis=2),
    )
    partner = jnp.where(
        column == 0,
        jnp.concatenate([partner_half, partner_other], axis=2),
        jnp.concatenate([partner_other, partner_half], axis=2),
    )
    both = jnp.concatenate([whole, partner], axis=0)
    widened = both.astype(jnp.float32)
    power = jnp.mean(widened * widened, axis=-1, keepdims=True)
    normed = (
        (widened * lax.rsqrt(power + norm_eps) * gain)
        .astype(jnp.bfloat16)
        .reshape(2 * passages * length, -1)
    )
    token_positions = (here * length + jnp.arange(length, dtype=jnp.int32)).astype(jnp.float32)

    summed = jnp.dot(normed, full_panel, preferred_element_type=jnp.float32) + panel_bias
    summed = summed.reshape(2 * passages, length, split + value_split)
    turned = apply_rotation(
        summed[..., :split].reshape(2 * passages, length, split // HEAD_SIZE, HEAD_SIZE),
        token_positions,
    ).astype(jnp.bfloat16)
    result = jnp.concatenate(
        [turned.reshape(2 * passages, length, split), summed[..., split:].astype(jnp.bfloat16)],
        axis=-1,
    )
    mine = result[:passages]
    lead = split - HEAD_SIZE
    returned_kv = lax.ppermute(result[passages:, :, lead:], "groups", SWAP)
    returned_q = lax.ppermute(result[passages:, :, :lead], "groups", SWAP)
    low_kv = jnp.where(first, mine[..., lead:], returned_kv)
    high_kv = jnp.where(first, returned_kv, mine[..., lead:])
    key = high_kv[..., :HEAD_SIZE]
    value_rows = jnp.concatenate([low_kv[..., HEAD_SIZE:], high_kv[..., HEAD_SIZE:]], axis=-1)
    low_q = jnp.where(first, mine[..., :lead], returned_q)
    high_q = jnp.where(first, returned_q, mine[..., :lead])
    query_rows = jnp.concatenate([low_q, low_kv[..., :HEAD_SIZE], high_q], axis=-1)

    pairs = jnp.concatenate([key, value_rows], axis=-1)
    if row_count == 8:
        order = snake_order(row_count)
        position = [0] * row_count
        for i, d in enumerate(order):
            position[d] = i
        forward = [(order[i], order[(i + 1) % row_count]) for i in range(row_count)]
        backward = [(order[i], order[(i - 1) % row_count]) for i in range(row_count)]
        ahead, behind = pairs, pairs
        ahead_parts, behind_parts = [], []
        for step in range(1, row_count // 2 + 1):
            ahead = lax.ppermute(ahead, "row", forward)
            ahead_parts.append(ahead)
            if step < row_count // 2:
                behind = lax.ppermute(behind, "row", backward)
                behind_parts.append(behind)
        gathered = jnp.stack([pairs] + ahead_parts + behind_parts)
        table = jnp.array(position, dtype=jnp.int32)
        delta = (table[here] - table) % row_count
        owner_slot = jnp.where(delta <= row_count // 2, delta, row_count // 2 + row_count - delta)
    else:
        gathered = lax.all_gather(pairs, "row", axis=0, tiled=False)
        owner_slot = jnp.arange(row_count, dtype=jnp.int32)
    gathered = gathered.reshape(
        row_count, passages, per_device, BLOCK_TOKENS, pairs_here, 2 * HEAD_SIZE
    )[:, :, :, :, 0]
    gathered = gathered.transpose(1, 0, 2, 3, 4).reshape(
        passages, passage_blocks, BLOCK_TOKENS, 2 * HEAD_SIZE
    )
    block_ids = jnp.arange(passage_blocks, dtype=jnp.int32)
    slot_of_block = owner_slot[block_ids // per_device] * per_device + block_ids % per_device
    kv_blocks = gathered[:, slot_of_block]

    local_blocks = here * per_device + jnp.arange(per_device, dtype=jnp.int32)
    nearby_blocks = local_blocks[:, None] + jnp.arange(3, dtype=jnp.int32)[None, :] - 1
    inside = (nearby_blocks >= 0) & (nearby_blocks < passage_blocks)
    nearby_clamped = jnp.clip(nearby_blocks, 0, passage_blocks - 1)
    passage_ids = jnp.arange(passages, dtype=jnp.int32)
    window = kv_blocks[passage_ids[:, None, None], nearby_clamped[None]]
    window = window.reshape(passages, per_device, 3 * BLOCK_TOKENS, 2 * HEAD_SIZE)

    global_here = lax.dynamic_slice_in_dim(global_block_index, column * pairs_here, pairs_here, 1)
    global_pairs = kv_blocks[passage_ids[:, None], global_here[:, 0, :]]
    global_pairs = global_pairs.reshape(passages, GLOBAL_BLOCKS * BLOCK_TOKENS, 2 * HEAD_SIZE)

    selected = lax.dynamic_slice_in_dim(random_block_index, column * heads_here, heads_here, 2)
    selected = lax.dynamic_slice_in_dim(selected, here * per_device, per_device, 1)
    arrived = kv_blocks[passage_ids[:, None, None, None], selected]
    arrived = arrived.reshape(
        passages, per_device, heads_here, RANDOM_BLOCKS * BLOCK_TOKENS, 2 * HEAD_SIZE
    )

    query_block_rows = query_rows.reshape(
        passages, per_device, BLOCK_TOKENS, heads_here, HEAD_SIZE
    )
    first_scores = jnp.einsum(
        "sqbgh,sqwh->sqgbw",
        query_block_rows,
        window[..., :HEAD_SIZE],
        preferred_element_type=jnp.float32,
    )
    second_scores = jnp.einsum(
        "sqbgh,swh->sqgbw",
        query_block_rows,
        global_pairs[..., :HEAD_SIZE],
        preferred_element_type=jnp.float32,
    )
    third_scores = jnp.einsum(
        "sqbgh,sqgwh->sqgbw",
        query_block_rows,
        arrived[..., :HEAD_SIZE],
        preferred_element_type=jnp.float32,
    )
    first_scores = first_scores * scale
    second_scores = second_scores * scale
    third_scores = third_scores * scale
    near_mask = jnp.repeat(inside, BLOCK_TOKENS, axis=1)
    first_scores = jnp.where(near_mask[None, :, None, None, :], first_scores, -jnp.inf)
    top = jnp.maximum(
        jnp.max(first_scores, axis=-1, keepdims=True),
        jnp.maximum(
            jnp.max(second_scores, axis=-1, keepdims=True),
            jnp.max(third_scores, axis=-1, keepdims=True),
        ),
    )
    near_weights = jnp.exp(first_scores - top)
    global_weights = jnp.exp(second_scores - top)
    random_weights = jnp.exp(third_scores - top)
    total = (
        jnp.sum(near_weights, axis=-1, keepdims=True)
        + jnp.sum(global_weights, axis=-1, keepdims=True)
        + jnp.sum(random_weights, axis=-1, keepdims=True)
    )
    near_probs = (near_weights / total).astype(jnp.bfloat16)
    global_probs = (global_weights / total).astype(jnp.bfloat16)
    random_probs = (random_weights / total).astype(jnp.bfloat16)
    mixed = jnp.einsum(
        "sqgbw,sqwh->sqbgh",
        near_probs,
        window[..., HEAD_SIZE:],
        preferred_element_type=jnp.float32,
    )
    mixed = mixed + jnp.einsum(
        "sqgbw,swh->sqbgh",
        global_probs,
        global_pairs[..., HEAD_SIZE:],
        preferred_element_type=jnp.float32,
    )
    mixed = mixed + jnp.einsum(
        "sqgbw,sqgwh->sqbgh",
        random_probs,
        arrived[..., HEAD_SIZE:],
        preferred_element_type=jnp.float32,
    )
    return mixed.reshape(passages, length, heads_here * HEAD_SIZE).astype(jnp.bfloat16)


def solution(mesh):
    placed = (
        P("groups", "row", "col"),
        P(),
        P("row", "col"),
        P("col"),
        P("row", "col"),
        P("col"),
        P("row", "col"),
        P("col"),
        P("groups", None, None, None),
        P("groups", None, None),
    )
    return jax.shard_map(
        shards, mesh=mesh, in_specs=placed, out_specs=P("groups", "row", "col"), check_vma=False
    )
```

```python
import math

import jax
import jax.numpy as jnp
from jax import lax
from jax.sharding import PartitionSpec as P

HEAD_SIZE = 128
BLOCK_TOKENS = 64
RANDOM_BLOCKS = 2
GLOBAL_BLOCKS = 2


rope_base = 1000000.0
norm_eps = 1e-06

SWAP = [(0, 1), (1, 0)]


def apply_rotation(values, token_positions):
    half = values.shape[-1] // 2
    freqs = 1.0 / rope_base ** (jnp.arange(half, dtype=jnp.float32) * 2.0 / values.shape[-1])
    angles = token_positions[:, None] * freqs[None, :]
    cosine = jnp.concatenate([jnp.cos(angles), jnp.cos(angles)], axis=-1)[None, :, None, :]
    sine = jnp.concatenate([jnp.sin(angles), jnp.sin(angles)], axis=-1)[None, :, None, :]
    turned = jnp.concatenate([-values[..., half:], values[..., :half]], axis=-1)
    return values * cosine + turned * sine


def snake_order(count):
    return [2 * z for z in range(count // 2)] + [2 * z + 1 for z in reversed(range(count // 2))]


def gather_rows(ahead, behind, count, here):
    if count != 8:
        shard = jnp.concatenate([ahead, behind], axis=0)
        return lax.all_gather(shard, "row", axis=0, tiled=True), ahead
    order = snake_order(count)
    position = [0] * count
    for i, d in enumerate(order):
        position[d] = i
    forward = [(order[i], order[(i + 1) % count]) for i in range(count)]
    backward = [(order[i], order[(i - 1) % count]) for i in range(count)]
    half = ahead.shape[0]
    ahead_parts, behind_parts = [ahead], [behind]
    for _ in range(count - 1):
        ahead = lax.ppermute(ahead, "row", forward)
        behind = lax.ppermute(behind, "row", backward)
        ahead_parts.append(ahead)
        behind_parts.append(behind)
    table = jnp.array(position, dtype=jnp.int32)
    mine = table[here]
    ahead_pick = (mine - table) % count
    behind_pick = (table - mine) % count
    joined = jnp.concatenate(
        [jnp.stack(ahead_parts)[ahead_pick], jnp.stack(behind_parts)[behind_pick]], axis=1
    )
    return joined.reshape(count * 2 * half, ahead.shape[1]), ahead_parts[1]


def shards(
    tokens,
    gain,
    w_query,
    b_query,
    key_weight,
    b_key,
    value_weight,
    value_bias,
    random_block_index,
    global_block_index,
):
    row_count = lax.axis_size("row")
    here = lax.axis_index("row")
    column = lax.axis_index("col")
    group = lax.axis_index("groups")
    passages, length, _ = tokens.shape
    heads_here = w_query.shape[1] // HEAD_SIZE
    pairs_here = key_weight.shape[1] // HEAD_SIZE
    passage_groups = heads_here // pairs_here
    per_device = length // BLOCK_TOKENS
    passage_blocks = row_count * per_device
    scale = 1.0 / math.sqrt(HEAD_SIZE)

    rotary_cols = (heads_here + pairs_here) * HEAD_SIZE
    split = rotary_cols // 2
    value_cols = pairs_here * HEAD_SIZE
    value_split = value_cols // 2
    rotary_w = jnp.concatenate([w_query, key_weight], axis=1)
    rotary_b = jnp.concatenate([b_query, b_key], axis=0)
    first = group == 0
    rows_here = w_query.shape[0]

    def panel_rows(start, stop):
        return jnp.concatenate(
            [
                lax.dynamic_slice_in_dim(rotary_w[start:stop], group * split, split, 1),
                lax.dynamic_slice_in_dim(
                    value_weight[start:stop], group * value_split, value_split, 1
                ),
            ],
            axis=1,
        )

    full_panel, first_arrival = gather_rows(
        panel_rows(0, rows_here // 2),
        panel_rows(rows_here // 2, rows_here),
        row_count,
        here,
    )
    panel_bias = jnp.where(
        first,
        jnp.concatenate([rotary_b[:split], value_bias[:value_split]]),
        jnp.concatenate([rotary_b[split:], value_bias[value_split:]]),
    )

    other_half = lax.ppermute(tokens, "col", SWAP)
    late_tokens, _ = lax.optimization_barrier((tokens, first_arrival))
    partner_half = lax.ppermute(late_tokens, "groups", SWAP)
    partner_other = lax.ppermute(partner_half, "col", SWAP)
    whole = jnp.where(
        column == 0,
        jnp.concatenate([tokens, other_half], axis=2),
        jnp.concatenate([other_half, tokens], axis=2),
    )
    partner = jnp.where(
        column == 0,
        jnp.concatenate([partner_half, partner_other], axis=2),
        jnp.concatenate([partner_other, partner_half], axis=2),
    )
    both = jnp.concatenate([whole, partner], axis=0)
    widened = both.astype(jnp.float32)
    power = jnp.mean(widened * widened, axis=-1, keepdims=True)
    normed = (
        (widened * lax.rsqrt(power + norm_eps) * gain)
        .astype(jnp.bfloat16)
        .reshape(2 * passages * length, -1)
    )
    token_positions = (here * length + jnp.arange(length, dtype=jnp.int32)).astype(jnp.float32)

    summed = jnp.dot(normed, full_panel, preferred_element_type=jnp.float32) + panel_bias
    summed = summed.reshape(2 * passages, length, split + value_split)
    turned = apply_rotation(
        summed[..., :split].reshape(2 * passages, length, split // HEAD_SIZE, HEAD_SIZE),
        token_positions,
    ).astype(jnp.bfloat16)
    result = jnp.concatenate(
        [turned.reshape(2 * passages, length, split), summed[..., split:].astype(jnp.bfloat16)],
        axis=-1,
    )
    mine = result[:passages]
    lead = split - HEAD_SIZE
    returned_kv = lax.ppermute(result[passages:, :, lead:], "groups", SWAP)
    low_kv = jnp.where(first, mine[..., lead:], returned_kv)
    high_kv = jnp.where(first, returned_kv, mine[..., lead:])
    key = high_kv[..., :HEAD_SIZE]
    value_rows = jnp.concatenate([low_kv[..., HEAD_SIZE:], high_kv[..., HEAD_SIZE:]], axis=-1)
    late_q, _ = lax.optimization_barrier((result[passages:, :, :lead], value_rows))
    returned_q = lax.ppermute(late_q, "groups", SWAP)
    low_q = jnp.where(first, mine[..., :lead], returned_q)
    high_q = jnp.where(first, returned_q, mine[..., :lead])
    query_rows = jnp.concatenate([low_q, low_kv[..., :HEAD_SIZE], high_q], axis=-1)

    pairs = jnp.concatenate([key, value_rows], axis=-1)
    if row_count == 8:
        order = snake_order(row_count)
        position = [0] * row_count
        for i, d in enumerate(order):
            position[d] = i
        forward = [(order[i], order[(i + 1) % row_count]) for i in range(row_count)]
        backward = [(order[i], order[(i - 1) % row_count]) for i in range(row_count)]
        ahead, behind = pairs, pairs
        ahead_parts, behind_parts = [], []
        for step in range(1, row_count // 2 + 1):
            ahead = lax.ppermute(ahead, "row", forward)
            ahead_parts.append(ahead)
            if step < row_count // 2:
                behind = lax.ppermute(behind, "row", backward)
                behind_parts.append(behind)
        gathered = jnp.stack([pairs] + ahead_parts + behind_parts)
        table = jnp.array(position, dtype=jnp.int32)
        delta = (table[here] - table) % row_count
        owner_slot = jnp.where(delta <= row_count // 2, delta, row_count // 2 + row_count - delta)
    else:
        gathered = lax.all_gather(pairs, "row", axis=0, tiled=False)
        owner_slot = jnp.arange(row_count, dtype=jnp.int32)
    gathered = gathered.reshape(
        row_count, passages, per_device, BLOCK_TOKENS, pairs_here, 2 * HEAD_SIZE
    )[:, :, :, :, 0]
    gathered = gathered.transpose(1, 0, 2, 3, 4).reshape(
        passages, passage_blocks, BLOCK_TOKENS, 2 * HEAD_SIZE
    )
    block_ids = jnp.arange(passage_blocks, dtype=jnp.int32)
    slot_of_block = owner_slot[block_ids // per_device] * per_device + block_ids % per_device
    kv_blocks = gathered[:, slot_of_block]

    local_blocks = here * per_device + jnp.arange(per_device, dtype=jnp.int32)
    nearby_blocks = local_blocks[:, None] + jnp.arange(3, dtype=jnp.int32)[None, :] - 1
    inside = (nearby_blocks >= 0) & (nearby_blocks < passage_blocks)
    nearby_clamped = jnp.clip(nearby_blocks, 0, passage_blocks - 1)
    passage_ids = jnp.arange(passages, dtype=jnp.int32)
    window = kv_blocks[passage_ids[:, None, None], nearby_clamped[None]]
    window = window.reshape(passages, per_device, 3 * BLOCK_TOKENS, 2 * HEAD_SIZE)

    global_here = lax.dynamic_slice_in_dim(global_block_index, column * pairs_here, pairs_here, 1)
    global_pairs = kv_blocks[passage_ids[:, None], global_here[:, 0, :]]
    global_pairs = global_pairs.reshape(passages, GLOBAL_BLOCKS * BLOCK_TOKENS, 2 * HEAD_SIZE)

    selected = lax.dynamic_slice_in_dim(random_block_index, column * heads_here, heads_here, 2)
    selected = lax.dynamic_slice_in_dim(selected, here * per_device, per_device, 1)
    arrived = kv_blocks[passage_ids[:, None, None, None], selected]
    arrived = arrived.reshape(
        passages, per_device, heads_here, RANDOM_BLOCKS * BLOCK_TOKENS, 2 * HEAD_SIZE
    )

    query_block_rows = query_rows.reshape(
        passages, per_device, BLOCK_TOKENS, heads_here, HEAD_SIZE
    )
    first_scores = jnp.einsum(
        "sqbgh,sqwh->sqgbw",
        query_block_rows,
        window[..., :HEAD_SIZE],
        preferred_element_type=jnp.float32,
    )
    second_scores = jnp.einsum(
        "sqbgh,swh->sqgbw",
        query_block_rows,
        global_pairs[..., :HEAD_SIZE],
        preferred_element_type=jnp.float32,
    )
    third_scores = jnp.einsum(
        "sqbgh,sqgwh->sqgbw",
        query_block_rows,
        arrived[..., :HEAD_SIZE],
        preferred_element_type=jnp.float32,
    )
    first_scores = first_scores * scale
    second_scores = second_scores * scale
    third_scores = third_scores * scale
    near_mask = jnp.repeat(inside, BLOCK_TOKENS, axis=1)
    first_scores = jnp.where(near_mask[None, :, None, None, :], first_scores, -jnp.inf)
    top = jnp.maximum(
        jnp.max(first_scores, axis=-1, keepdims=True),
        jnp.maximum(
            jnp.max(second_scores, axis=-1, keepdims=True),
            jnp.max(third_scores, axis=-1, keepdims=True),
        ),
    )
    near_weights = jnp.exp(first_scores - top)
    global_weights = jnp.exp(second_scores - top)
    random_weights = jnp.exp(third_scores - top)
    total = (
        jnp.sum(near_weights, axis=-1, keepdims=True)
        + jnp.sum(global_weights, axis=-1, keepdims=True)
        + jnp.sum(random_weights, axis=-1, keepdims=True)
    )
    near_probs = (near_weights / total).astype(jnp.bfloat16)
    global_probs = (global_weights / total).astype(jnp.bfloat16)
    random_probs = (random_weights / total).astype(jnp.bfloat16)
    mixed = jnp.einsum(
        "sqgbw,sqwh->sqbgh",
        near_probs,
        window[..., HEAD_SIZE:],
        preferred_element_type=jnp.float32,
    )
    mixed = mixed + jnp.einsum(
        "sqgbw,swh->sqbgh",
        global_probs,
        global_pairs[..., HEAD_SIZE:],
        preferred_element_type=jnp.float32,
    )
    mixed = mixed + jnp.einsum(
        "sqgbw,sqgwh->sqbgh",
        random_probs,
        arrived[..., HEAD_SIZE:],
        preferred_element_type=jnp.float32,
    )
    return mixed.reshape(passages, length, heads_here * HEAD_SIZE).astype(jnp.bfloat16)


def solution(mesh):
    placed = (
        P("groups", "row", "col"),
        P(),
        P("row", "col"),
        P("col"),
        P("row", "col"),
        P("col"),
        P("row", "col"),
        P("col"),
        P("groups", None, None, None),
        P("groups", None, None),
    )
    return jax.shard_map(
        shards, mesh=mesh, in_specs=placed, out_specs=P("groups", "row", "col"), check_vma=False
    )
```
